128 devices in a mesh: seq: 16 (over z, y_hi, core), tp: 8 (over x, y_lo).
Axes of the slice: x: 4, y: 4 (y_hi: 2, y_lo: 2; y = y_hi * 2 + y_lo), z: 4, core: 2. Of those that a mesh axis runs over, the one named last changes fastest.
Arguments:
- trainer_rows: float32 [2, 1024, 12544], P(None, ('seq', 'tp')), as said below
- shard_order: int32 [128], replicated, may hold values from 0 to 127, each once
- residual_in: float32 [16384, 1024], P(('seq', 'tp')), may hold values from -6 to 6
- norm_gains: float32 [2, 2, 1024], replicated, may hold values from 0.25 to 1.75
- prompt_lengths: int32 [16, 4], P('seq'), may hold values from 1 to 512, 1024 in all within a row
- variate_ids: int32 [16384], P('seq'), may hold values from 0 to 7
- variate_bias: float32 [2, 16, 2], replicated, may hold values from -2 to 260
Outputs:
- hidden_states: float32 [16384, 1024], P(('seq', 'tp'))
The draws below stay inside these ranges and needn't reach their ends.
Inputs may be any that keep to these rules, and one draw needn't show every extreme that they name: shard_order is a permutation of the trainer shards' row blocks. `prompt_lengths`: each row sums to 1024, and one entry of each row is 512. `trainer_rows`: entries of columns up to 9728 are at most 6 / sqrt(1024) in size, later ones at most 6 / sqrt(2816).
All inputs are finite; a program needn't handle non-finite values.
Results may differ from the reference program's by a relative error of at most 0.017.
Values may be sent and summed in bfloat16 or wider, within the bound.
No kernel may reach another device: no remote copies, remote signals or barrier semaphores. Data moves between devices by JAX's collectives and lax.ppermute only.
A program may use at most 128 MiB of HBM per device.

```python
import math
import jax
import jax.numpy as jnp
import numpy as np
from jax import lax

D = 1024
H = 16
HD = 64
FF = 2816
LAYERS = 2
NVAR = 8
LEN = 512
TOK_DEV = 1024
PROMPTS_DEV = 4
TOKENS = 16384
N_SEQ = 16
N_TP = 8
DEVICES = 128


def draw_trainer_rows(key, part):
    values = jnp.clip(jax.random.normal(key, (LAYERS, D, 4 * D + 3 * FF), jnp.float32), -6.0, 6.0)
    column = jnp.arange(4 * D + 3 * FF)
    scales = jnp.where(column >= 4 * D + 2 * FF, FF ** (-0.5), D ** (-0.5)).astype(jnp.float32)
    return values * scales[None, None, :]


def draw_variate_bias(key, part):
    key_base = jax.random.fold_in(key, 11)
    offsets = jax.random.uniform(key_base, (LAYERS, H, 2), jnp.float32, -2.0, 2.0)
    return offsets


def set_ends(values, stream_key, low, largest):
    spot = [jax.random.randint(jax.random.fold_in(stream_key, axis), (), 0, length) for axis, length in enumerate(values.shape)]
    main_axis = values.shape.index(max(values.shape))
    neighbour = spot[:main_axis] + [(spot[main_axis] + 1) % values.shape[main_axis]] + spot[main_axis + 1:]
    return values.at[tuple(spot)].set(low).at[tuple(neighbour)].set(largest)


def steps_of(own_key, extent, split, least, high):
    def one(position, shards_of):
        heights = jax.random.uniform(jax.random.fold_in(jax.random.fold_in(own_key, 6), position), (shards_of,), jnp.float32, least / len(split), high / len(split))
        return jnp.repeat(jnp.exp(heights), extent[position] // shards_of).reshape((-1,) + (1,) * (len(extent) - position - 1))

    level = one(*split[0])
    for cut in split[1:]:
        level = level * one(*cut)
    return level


def split_up(amount, total, reach, lean):
    loads = [(1 << 20) // math.isqrt(grade ** lean) + 1 for grade in range(2, amount + 1)]
    rest, counts = total - reach - (amount - 1), [1] * (amount - 1)
    while rest > 0:
        candidates = [i for i in range(amount - 1) if counts[i] < reach]
        mass, remaining = sum([loads[i] for i in candidates]), rest
        for i in candidates:
            extra = min(reach - counts[i], max(1, remaining * loads[i] // mass), rest)
            counts[i] = counts[i] + extra
            rest = rest - extra
    return np.array([reach] + counts)


def uneven(stream_key, number_of, total, bound, lean):
    if number_of == 2:
        one = jax.random.randint(stream_key, (), max(1, total - bound), min(bound, total - 1) + 1)
        return jnp.stack([one, total - one])
    sizes = jnp.asarray(split_up(number_of, total, bound, lean), jnp.int32)
    pairs = (number_of - 1) // 2
    source_of, sink = sizes[1:1 + 2 * pairs:2], sizes[2:2 + 2 * pairs:2]
    slack = jnp.minimum(source_of - 1, bound - sink)
    passed = jax.random.randint(jax.random.fold_in(stream_key, 1), (pairs,), 0, 1 << 20) % (slack + 1)
    sizes = sizes.at[1:1 + 2 * pairs:2].set(source_of - passed).at[2:2 + 2 * pairs:2].set(sink + passed)
    return sizes[jax.random.permutation(jax.random.fold_in(stream_key, 2), number_of)]


def scatter_about(rng, shape, scale, bound, split=(), kind=jnp.bfloat16):
    array = scale * jax.random.normal(rng, shape, jnp.float32)
    if split:
        array = array * steps_of(rng, shape, split, -0.22, 0.18)
    return jnp.clip(array, -bound, bound).astype(kind)


def setup_inputs(seed: int = 0) -> dict:
    arg_keys = jax.random.split(jax.random.key(seed), 8)
    trainer_rows = draw_trainer_rows(jax.random.fold_in(arg_keys[7], 71), 0)
    shard_order = jax.random.permutation(arg_keys[1], DEVICES).astype(jnp.int32)
    residual_in = scatter_about(arg_keys[2], (TOKENS, D), 1.0, 6.0, ((0, 128),), jnp.float32)
    norm_gains = jnp.clip(1.0 + 0.15 * jax.random.normal(arg_keys[3], (LAYERS, 2, D), jnp.float32), 0.25, 1.75)
    prompt_lengths = jax.vmap(lambda own: uneven(own, PROMPTS_DEV, TOK_DEV, LEN, 2))(jax.random.split(arg_keys[4], N_SEQ)).reshape((N_SEQ, PROMPTS_DEV)).astype(jnp.int32)
    variate_ids = set_ends(jax.random.randint(arg_keys[5], (TOKENS,), 0, NVAR), jax.random.fold_in(arg_keys[5], 1), 0, NVAR - 1).astype(jnp.int32)
    variate_bias = draw_variate_bias(jax.random.fold_in(arg_keys[7], 71), 0)
    return {"trainer_rows": trainer_rows, "shard_order": shard_order, "residual_in": residual_in, "norm_gains": norm_gains, "prompt_lengths": prompt_lengths, "variate_ids": variate_ids, "variate_bias": variate_bias}


NEGATIVE = -1e+30
EPSILON = 1e-05

def rms_scaled(values, gain):
    mean_square = lax.optimization_barrier(jnp.mean(values * values, axis=-1, keepdims=True))
    return values * lax.rsqrt(mean_square + EPSILON) * gain

def rotate(values, offsets):
    half_width = values.shape[-1] // 2
    frequency = 10000.0 ** (-jnp.arange(half_width, dtype=jnp.float32) / half_width)
    angles = offsets.astype(jnp.float32)[:, None] * frequency[None, :]
    cosine = jnp.cos(angles)[:, None, :]
    sine_part = jnp.sin(angles)[:, None, :]
    front_half = values[..., :half_width]
    back_half = values[..., half_width:]
    return jnp.concatenate([front_half * cosine - back_half * sine_part, front_half * sine_part + back_half * cosine], axis=-1)

def prompt_layout(lengths, token_count):
    prompt_ends = jnp.cumsum(lengths).astype(jnp.int32)
    prompt_starts = (prompt_ends - lengths).astype(jnp.int32)
    positions = jnp.arange(token_count, dtype=jnp.int32)
    segment = lax.optimization_barrier(jnp.sum((positions[:, None] >= prompt_ends[None, :]).astype(jnp.int32), axis=1)).astype(jnp.int32)
    member = segment[:, None] == jnp.arange(lengths.shape[0], dtype=jnp.int32)[None, :]
    offsets = (positions - lax.optimization_barrier(jnp.sum(jnp.where(member, prompt_starts[None, :], 0), axis=1))).astype(jnp.int32)
    return (segment, offsets)

def group_sum(source, weight_t):
    group_width = source.shape[1] // N_TP
    terms = jnp.einsum('tgw,dgw->gtd', source.reshape(source.shape[0], N_TP, group_width).astype(jnp.float32), weight_t.reshape(weight_t.shape[0], N_TP, group_width).astype(jnp.float32))
    rounded = lax.optimization_barrier(terms.astype(jnp.bfloat16))
    return lax.optimization_barrier(jnp.sum(rounded.astype(jnp.float32), axis=0))

def reference(trainer_rows, shard_order, residual_in, norm_gains, prompt_lengths, variate_ids, variate_bias):
    blocks = trainer_rows.reshape(LAYERS, DEVICES, D // DEVICES, 4 * D + 3 * FF)
    placed = jnp.zeros_like(blocks).at[:, shard_order].set(blocks)
    weights = placed.reshape(LAYERS, D, 4 * D + 3 * FF).astype(jnp.bfloat16)

    def one_block(inputs):
        residual, lengths, variates = inputs
        segment, offsets = prompt_layout(lengths, TOK_DEV)
        same_prompt = segment[:, None] == segment[None, :]
        same_variate = variates[:, None] == variates[None, :]
        for layer_index in range(LAYERS):
            layer_bias = variate_bias[layer_index]
            pair_bias = jnp.where(same_variate[None], layer_bias[:, 1][:, None, None], layer_bias[:, 0][:, None, None])
            layer_weights = weights[layer_index]
            normed = rms_scaled(residual, norm_gains[layer_index, 0]).astype(jnp.bfloat16)
            projected = jnp.dot(normed, layer_weights[:, :3 * D], preferred_element_type=jnp.float32)
            queries = rotate(projected[:, :D].reshape(TOK_DEV, H, HD), offsets).astype(jnp.bfloat16)
            key_rows = rotate(projected[:, D:2 * D].reshape(TOK_DEV, H, HD), offsets).astype(jnp.bfloat16)
            values = projected[:, 2 * D:3 * D].reshape(TOK_DEV, H, HD).astype(jnp.bfloat16)
            scores = jnp.einsum('qhd,khd->hqk', queries.astype(jnp.float32), key_rows.astype(jnp.float32)) * HD ** (-0.5) + pair_bias
            scores = jnp.where(same_prompt[None], scores, NEGATIVE)
            row_peak = lax.optimization_barrier(jnp.max(scores, axis=2, keepdims=True))
            weights_exp = jnp.exp(scores - row_peak)
            attn_weights = (weights_exp / lax.optimization_barrier(jnp.sum(weights_exp, axis=2, keepdims=True))).astype(jnp.bfloat16)
            mixed_heads = jnp.einsum('hqk,khd->qhd', attn_weights.astype(jnp.float32), values.astype(jnp.float32)).astype(jnp.bfloat16).reshape(TOK_DEV, D)
            residual = residual + group_sum(mixed_heads, layer_weights[:, 3 * D:4 * D])
            normed_mlp = rms_scaled(residual, norm_gains[layer_index, 1]).astype(jnp.bfloat16)
            gate_up = jnp.dot(normed_mlp, layer_weights[:, 4 * D:4 * D + 2 * FF], preferred_element_type=jnp.float32)
            hidden = (jax.nn.silu(gate_up[:, :FF]) * gate_up[:, FF:]).astype(jnp.bfloat16)
            residual = residual + group_sum(hidden, layer_weights[:, 4 * D + 2 * FF:])
        return residual
    outputs = lax.map(one_block, (residual_in.reshape(N_SEQ, TOK_DEV, D), prompt_lengths, variate_ids.reshape(N_SEQ, TOK_DEV)))
    return outputs.reshape(TOK_DEV * N_SEQ, D)
```

```python
import jax
import jax.numpy as jnp
from jax import lax
from jax.sharding import PartitionSpec as P

NEGATIVE = -1e30
EPSILON = 1e-05


def rms_scaled(values, gain):
    mean_square = jnp.mean(values * values, axis=-1, keepdims=True)
    return values * lax.rsqrt(mean_square + EPSILON) * gain


def rotate(values, offsets):
    half_width = values.shape[-1] // 2
    frequency = 10000.0 ** (-jnp.arange(half_width, dtype=jnp.float32) / half_width)
    angles = offsets.astype(jnp.float32)[:, None] * frequency[None, :]
    cosine = jnp.cos(angles)[:, None, :]
    sine_part = jnp.sin(angles)[:, None, :]
    front_half = values[..., :half_width]
    back_half = values[..., half_width:]
    return jnp.concatenate(
        [front_half * cosine - back_half * sine_part, front_half * sine_part + back_half * cosine],
        axis=-1,
    )


def prompt_layout(lengths, token_count):
    prompt_ends = jnp.cumsum(lengths)
    prompt_starts = prompt_ends - lengths
    positions = jnp.arange(token_count, dtype=jnp.int32)
    segment = jnp.sum((positions[:, None] >= prompt_ends[None, :]).astype(jnp.int32), axis=1)
    member = segment[:, None] == jnp.arange(lengths.shape[0], dtype=jnp.int32)[None, :]
    offsets = positions - jnp.sum(jnp.where(member, prompt_starts[None, :], 0), axis=1)
    return (segment, offsets)


def project_rows(row_piece, weight):
    return jnp.dot(row_piece, weight, preferred_element_type=jnp.float32)


def gated_units(row_piece, weight):
    gate_up = jnp.dot(row_piece, weight, preferred_element_type=jnp.float32)
    half_width = weight.shape[1] // 2
    return (jax.nn.silu(gate_up[:, :half_width]) * gate_up[:, half_width:]).astype(jnp.bfloat16)


def project_out(source, weight):
    return lax.dot_general(
        source, weight, (((1,), (1,)), ((), ())), preferred_element_type=jnp.float32
    )


def gather_tp(values, tp_count):
    stacked = jnp.broadcast_to(values[None], (tp_count,) + values.shape)
    gathered = lax.all_to_all(stacked, "tp", 0, 0, tiled=True)
    return gathered.reshape((tp_count * values.shape[0],) + values.shape[1:])


def reduce_tp(products, tp_count):
    pieces = products.reshape((tp_count, products.shape[0] // tp_count) + products.shape[1:])
    received = lax.all_to_all(pieces, "tp", 0, 0, tiled=True)
    return jnp.sum(received.astype(jnp.float32), axis=0)


def on_device(
    trainer_rows, shard_order, residual_in, norm_gains, prompt_lengths, variate_ids, variate_bias
):
    tp_count = lax.axis_size("tp")
    seq_count = lax.axis_size("seq")
    layer_count, block_rows, total_cols = trainer_rows.shape
    model_width = residual_in.shape[1]
    ff_width = (total_cols - 4 * model_width) // 3
    head_cols = model_width // tp_count
    unit_cols = ff_width // tp_count
    block_count = seq_count * tp_count
    part_widths = [model_width] * 4 + [ff_width] * 3

    def layer_weights_of(layer_index):
        rounded = trainer_rows[layer_index].astype(jnp.bfloat16)
        grouped_parts = []
        column_start = 0
        for part_width in part_widths:
            grouped_parts.append(
                rounded[:, column_start : column_start + part_width].reshape(
                    block_rows, tp_count, part_width // tp_count
                )
            )
            column_start = column_start + part_width
        grouped = jnp.concatenate(grouped_parts, axis=2)
        regrouped = lax.all_to_all(grouped, "tp", split_axis=1, concat_axis=0, tiled=True)
        collected = lax.all_gather(regrouped, "seq", axis=0, tiled=True)
        return collected.reshape(block_count * block_rows, collected.shape[2])

    def to_stored(values):
        blocks = values.reshape(values.shape[:-1] + (block_count, block_rows))
        return jnp.take(blocks, shard_order, axis=-2).reshape(values.shape)

    inverse_order = jnp.zeros_like(shard_order).at[shard_order].set(
        jnp.arange(block_count, dtype=shard_order.dtype)
    )

    def from_stored(values):
        blocks = values.reshape(values.shape[:-1] + (block_count, block_rows))
        return jnp.take(blocks, inverse_order, axis=-2).reshape(values.shape)

    gains = to_stored(norm_gains)
    token_count = variate_ids.shape[0]
    segment, offsets = prompt_layout(prompt_lengths[0], token_count)
    same_prompt = segment[:, None] == segment[None, :]
    same_variate = variate_ids[:, None] == variate_ids[None, :]
    head_count = variate_bias.shape[1]
    local_heads = head_count // tp_count
    head_size = head_cols // local_heads
    bias_table = lax.dynamic_slice_in_dim(
        variate_bias, lax.axis_index("tp") * local_heads, local_heads, 1
    )
    residual = to_stored(residual_in)
    for layer_index in range(layer_count):
        layer_bias = bias_table[layer_index]
        pair_bias = jnp.where(
            same_variate[None], layer_bias[:, 1][:, None, None], layer_bias[:, 0][:, None, None]
        )
        layer_weights = layer_weights_of(layer_index)
        qkv_weight = layer_weights[:, : 3 * head_cols]
        out_weight = layer_weights[:, 3 * head_cols : 4 * head_cols]
        gate_up_weight = layer_weights[:, 4 * head_cols : 4 * head_cols + 2 * unit_cols]
        down_weight = layer_weights[:, 4 * head_cols + 2 * unit_cols :]
        normed = rms_scaled(residual, gains[layer_index, 0]).astype(jnp.bfloat16)
        projected = project_rows(gather_tp(normed, tp_count), weight=qkv_weight)
        queries = rotate(
            projected[:, :head_cols].reshape(token_count, local_heads, head_size), offsets
        ).astype(jnp.bfloat16)
        key_rows = rotate(
            projected[:, head_cols : 2 * head_cols].reshape(token_count, local_heads, head_size),
            offsets,
        ).astype(jnp.bfloat16)
        values = (
            projected[:, 2 * head_cols : 3 * head_cols]
            .reshape(token_count, local_heads, head_size)
            .astype(jnp.bfloat16)
        )
        scores = (
            jnp.einsum("qhd,khd->hqk", queries, key_rows, preferred_element_type=jnp.float32)
            * head_size ** (-0.5)
            + pair_bias
        )
        scores = jnp.where(same_prompt[None], scores, NEGATIVE)
        row_peak = jnp.max(scores, axis=2, keepdims=True)
        weights_exp = jnp.exp(scores - row_peak)
        attn_weights = (weights_exp / jnp.sum(weights_exp, axis=2, keepdims=True)).astype(
            jnp.bfloat16
        )
        mixed_heads = (
            jnp.einsum("hqk,khd->qhd", attn_weights, values, preferred_element_type=jnp.float32)
            .astype(jnp.bfloat16)
            .reshape(token_count, head_cols)
        )
        head_total = reduce_tp(
            project_out(source=mixed_heads, weight=out_weight).astype(jnp.bfloat16), tp_count
        )
        residual = residual + head_total
        normed_mlp = rms_scaled(residual, gains[layer_index, 1]).astype(jnp.bfloat16)
        hidden = gated_units(gather_tp(normed_mlp, tp_count), weight=gate_up_weight)
        unit_total = reduce_tp(
            project_out(source=hidden, weight=down_weight).astype(jnp.bfloat16), tp_count
        )
        residual = residual + unit_total
    return from_stored(residual)


def solution(mesh):
    return jax.shard_map(
        on_device,
        mesh=mesh,
        in_specs=(
            P(None, ("seq", "tp"), None),
            P(),
            P(("seq", "tp"), None),
            P(),
            P("seq", None),
            P("seq"),
            P(),
        ),
        out_specs=P(("seq", "tp"), None),
        check_vma=False,
    )
```

```python
import jax
import jax.numpy as jnp
from jax import lax
from jax.sharding import PartitionSpec as P

NEGATIVE = -1e30
EPSILON = 1e-05


def rms_scaled(values, gain):
    mean_square = jnp.mean(values * values, axis=-1, keepdims=True)
    return values * lax.rsqrt(mean_square + EPSILON) * gain


def rotate(values, offsets):
    half_width = values.shape[-1] // 2
    frequency = 10000.0 ** (-jnp.arange(half_width, dtype=jnp.float32) / half_width)
    angles = offsets.astype(jnp.float32)[:, None] * frequency[None, :]
    cosine = jnp.cos(angles)[:, None, :]
    sine_part = jnp.sin(angles)[:, None, :]
    front_half = values[..., :half_width]
    back_half = values[..., half_width:]
    return jnp.concatenate(
        [front_half * cosine - back_half * sine_part, front_half * sine_part + back_half * cosine],
        axis=-1,
    )


def prompt_layout(lengths, token_count):
    prompt_ends = jnp.cumsum(lengths)
    prompt_starts = prompt_ends - lengths
    positions = jnp.arange(token_count, dtype=jnp.int32)
    segment = jnp.sum((positions[:, None] >= prompt_ends[None, :]).astype(jnp.int32), axis=1)
    member = segment[:, None] == jnp.arange(lengths.shape[0], dtype=jnp.int32)[None, :]
    offsets = positions - jnp.sum(jnp.where(member, prompt_starts[None, :], 0), axis=1)
    return (segment, offsets)


def project_rows(row_piece, weight):
    return jnp.dot(row_piece, weight, preferred_element_type=jnp.float32)


def gated_units(row_piece, weight):
    gate_up = jnp.dot(row_piece, weight, preferred_element_type=jnp.float32)
    half_width = weight.shape[1] // 2
    return (jax.nn.silu(gate_up[:, :half_width]) * gate_up[:, half_width:]).astype(jnp.bfloat16)


def project_out(source, weight):
    return lax.dot_general(
        source, weight, (((1,), (1,)), ((), ())), preferred_element_type=jnp.float32
    )


def gather_tp(values, tp_count):
    stacked = jnp.broadcast_to(values[None], (tp_count,) + values.shape)
    gathered = lax.all_to_all(stacked, "tp", 0, 0, tiled=True)
    return gathered.reshape((tp_count * values.shape[0],) + values.shape[1:])


def reduce_tp(products, tp_count):
    pieces = products.reshape((tp_count, products.shape[0] // tp_count) + products.shape[1:])
    received = lax.all_to_all(pieces, "tp", 0, 0, tiled=True)
    return jnp.sum(received.astype(jnp.float32), axis=0)


def on_device(
    trainer_rows, shard_order, residual_in, norm_gains, prompt_lengths, variate_ids, variate_bias
):
    tp_count = lax.axis_size("tp")
    seq_count = lax.axis_size("seq")
    layer_count, block_rows, total_cols = trainer_rows.shape
    model_width = residual_in.shape[1]
    ff_width = (total_cols - 4 * model_width) // 3
    head_cols = model_width // tp_count
    unit_cols = ff_width // tp_count
    block_count = seq_count * tp_count
    part_widths = [model_width] * 4 + [ff_width] * 3

    rounded = trainer_rows.astype(jnp.bfloat16)
    grouped_parts = []
    column_start = 0
    for part_width in part_widths:
        grouped_parts.append(
            rounded[:, :, column_start : column_start + part_width].reshape(
                layer_count, block_rows, tp_count, part_width // tp_count
            )
        )
        column_start = column_start + part_width
    grouped = jnp.concatenate(grouped_parts, axis=3)
    regrouped = lax.all_to_all(grouped, "tp", split_axis=2, concat_axis=1, tiled=True)

    def collect(layer_index, first, last):
        piece = regrouped[layer_index, :, 0, first:last]
        return lax.all_gather(piece, "seq", axis=0, tiled=True)

    attention_cols = 4 * head_cols
    local_cols = regrouped.shape[3]

    def to_stored(values):
        blocks = values.reshape(values.shape[:-1] + (block_count, block_rows))
        return jnp.take(blocks, shard_order, axis=-2).reshape(values.shape)

    inverse_order = jnp.zeros_like(shard_order).at[shard_order].set(
        jnp.arange(block_count, dtype=shard_order.dtype)
    )

    def from_stored(values):
        blocks = values.reshape(values.shape[:-1] + (block_count, block_rows))
        return jnp.take(blocks, inverse_order, axis=-2).reshape(values.shape)

    gains = to_stored(norm_gains)
    token_count = variate_ids.shape[0]
    segment, offsets = prompt_layout(prompt_lengths[0], token_count)
    same_prompt = segment[:, None] == segment[None, :]
    same_variate = variate_ids[:, None] == variate_ids[None, :]
    head_count = variate_bias.shape[1]
    local_heads = head_count // tp_count
    head_size = head_cols // local_heads
    bias_table = lax.dynamic_slice_in_dim(
        variate_bias, lax.axis_index("tp") * local_heads, local_heads, 1
    )
    residual = to_stored(residual_in)
    for layer_index in range(layer_count):
        layer_bias = bias_table[layer_index]
        pair_bias = jnp.where(
            same_variate[None], layer_bias[:, 1][:, None, None], layer_bias[:, 0][:, None, None]
        )
        attention_weights = collect(layer_index, 0, attention_cols)
        mlp_weights = collect(layer_index, attention_cols, local_cols)
        qkv_weight = attention_weights[:, : 3 * head_cols]
        out_weight = attention_weights[:, 3 * head_cols :]
        gate_up_weight = mlp_weights[:, : 2 * unit_cols]
        down_weight = mlp_weights[:, 2 * unit_cols :]
        normed = rms_scaled(residual, gains[layer_index, 0]).astype(jnp.bfloat16)
        projected = project_rows(gather_tp(normed, tp_count), weight=qkv_weight)
        queries = rotate(
            projected[:, :head_cols].reshape(token_count, local_heads, head_size), offsets
        ).astype(jnp.bfloat16)
        key_rows = rotate(
            projected[:, head_cols : 2 * head_cols].reshape(token_count, local_heads, head_size),
            offsets,
        ).astype(jnp.bfloat16)
        values = (
            projected[:, 2 * head_cols : 3 * head_cols]
            .reshape(token_count, local_heads, head_size)
            .astype(jnp.bfloat16)
        )
        scores = (
            jnp.einsum("qhd,khd->hqk", queries, key_rows, preferred_element_type=jnp.float32)
            * head_size ** (-0.5)
            + pair_bias
        )
        scores = jnp.where(same_prompt[None], scores, NEGATIVE)
        row_peak = jnp.max(scores, axis=2, keepdims=True)
        weights_exp = jnp.exp(scores - row_peak)
        attn_weights = (weights_exp / jnp.sum(weights_exp, axis=2, keepdims=True)).astype(
            jnp.bfloat16
        )
        mixed_heads = (
            jnp.einsum("hqk,khd->qhd", attn_weights, values, preferred_element_type=jnp.float32)
            .astype(jnp.bfloat16)
            .reshape(token_count, head_cols)
        )
        head_total = reduce_tp(
            project_out(source=mixed_heads, weight=out_weight).astype(jnp.bfloat16), tp_count
        )
        residual = residual + head_total
        normed_mlp = rms_scaled(residual, gains[layer_index, 1]).astype(jnp.bfloat16)
        hidden = gated_units(gather_tp(normed_mlp, tp_count), weight=gate_up_weight)
        unit_total = reduce_tp(
            project_out(source=hidden, weight=down_weight).astype(jnp.bfloat16), tp_count
        )
        residual = residual + unit_total
    return from_stored(residual)


def solution(mesh):
    return jax.shard_map(
        on_device,
        mesh=mesh,
        in_specs=(
            P(None, ("seq", "tp"), None),
            P(),
            P(("seq", "tp"), None),
            P(),
            P("seq", None),
            P("seq"),
            P(),
        ),
        out_specs=P(("seq", "tp"), None),
        check_vma=False,
    )
```

```python
import jax
import jax.numpy as jnp
from jax import lax
from jax.sharding import Mesh
from jax.sharding import PartitionSpec as P

NEGATIVE = -1e30
EPSILON = 1e-05
CHIP_AXES = "chip"
SEQ_AXES = ("chip", "core")


def rms_scaled(values, gain):
    mean_square = jnp.mean(values * values, axis=-1, keepdims=True)
    return values * lax.rsqrt(mean_square + EPSILON) * gain


def rotate(values, offsets):
    half_width = values.shape[-1] // 2
    frequency = 10000.0 ** (-jnp.arange(half_width, dtype=jnp.float32) / half_width)
    angles = offsets.astype(jnp.float32)[:, None] * frequency[None, :]
    cosine = jnp.cos(angles)[:, None, :]
    sine_part = jnp.sin(angles)[:, None, :]
    front_half = values[..., :half_width]
    back_half = values[..., half_width:]
    return jnp.concatenate(
        [front_half * cosine - back_half * sine_part, front_half * sine_part + back_half * cosine],
        axis=-1,
    )


def prompt_layout(lengths, token_count):
    prompt_ends = jnp.cumsum(lengths)
    prompt_starts = prompt_ends - lengths
    positions = jnp.arange(token_count, dtype=jnp.int32)
    segment = jnp.sum((positions[:, None] >= prompt_ends[None, :]).astype(jnp.int32), axis=1)
    member = segment[:, None] == jnp.arange(lengths.shape[0], dtype=jnp.int32)[None, :]
    offsets = positions - jnp.sum(jnp.where(member, prompt_starts[None, :], 0), axis=1)
    return (segment, offsets)


def project_rows(row_piece, weight):
    return jnp.dot(row_piece, weight, preferred_element_type=jnp.float32)


def gated_units(row_piece, weight):
    gate_up = jnp.dot(row_piece, weight, preferred_element_type=jnp.float32)
    half_width = weight.shape[1] // 2
    return (jax.nn.silu(gate_up[:, :half_width]) * gate_up[:, half_width:]).astype(jnp.bfloat16)


def project_out(source, weight):
    return lax.dot_general(
        source, weight, (((1,), (1,)), ((), ())), preferred_element_type=jnp.float32
    )


def gather_tp(values, tp_count):
    stacked = jnp.broadcast_to(values[None], (tp_count,) + values.shape)
    gathered = lax.all_to_all(stacked, "tp", 0, 0, tiled=True)
    return gathered.reshape((tp_count * values.shape[0],) + values.shape[1:])


def reduce_tp(products, tp_count):
    pieces = products.reshape((tp_count, products.shape[0] // tp_count) + products.shape[1:])
    received = lax.all_to_all(pieces, "tp", 0, 0, tiled=True)
    return jnp.sum(received.astype(jnp.float32), axis=0)


def on_device(
    trainer_rows, shard_order, residual_in, norm_gains, prompt_lengths, variate_ids, variate_bias
):
    tp_count = lax.axis_size("tp")
    seq_count = lax.axis_size(SEQ_AXES)
    layer_count, block_rows, total_cols = trainer_rows.shape
    model_width = residual_in.shape[1]
    ff_width = (total_cols - 4 * model_width) // 3
    head_cols = model_width // tp_count
    unit_cols = ff_width // tp_count
    block_count = seq_count * tp_count
    part_widths = [model_width] * 4 + [ff_width] * 3

    rounded = trainer_rows.astype(jnp.bfloat16)
    grouped_parts = []
    column_start = 0
    for part_width in part_widths:
        grouped_parts.append(
            rounded[:, :, column_start : column_start + part_width].reshape(
                layer_count, block_rows, tp_count, part_width // tp_count
            )
        )
        column_start = column_start + part_width
    grouped = jnp.concatenate(grouped_parts, axis=3)
    regrouped = lax.all_to_all(grouped, "tp", split_axis=2, concat_axis=1, tiled=True)
    chip_count = lax.axis_size(CHIP_AXES)
    core = lax.axis_index("core")
    core_swap = [(0, 1), (1, 0)]

    def join_cores(half):
        other = lax.ppermute(half, "core", core_swap)
        return jnp.concatenate([half, other], axis=0)

    def collect(layer_index):
        piece = regrouped[layer_index, :, 0, :]
        if layer_index == 0:
            stacked = jnp.broadcast_to(piece[None], (chip_count,) + piece.shape)
            half = lax.all_to_all(stacked, CHIP_AXES, 0, 0, tiled=True).reshape(
                chip_count * piece.shape[0], piece.shape[1]
            )
        else:
            half = lax.all_gather(piece, CHIP_AXES, axis=0, tiled=True)
        return join_cores(half)

    block_index = jnp.arange(block_count, dtype=jnp.int32)
    half_blocks = block_count // 2
    core_of_block = jnp.where(block_index < half_blocks, core, 1 - core)
    within = block_index % half_blocks
    shard_of_block = ((within // tp_count) * 2 + core_of_block) * tp_count + within % tp_count
    stored_order = shard_order[shard_of_block]

    def to_stored(values):
        blocks = values.reshape(values.shape[:-1] + (block_count, block_rows))
        return jnp.take(blocks, stored_order, axis=-2).reshape(values.shape)

    inverse_order = jnp.zeros_like(stored_order).at[stored_order].set(block_index)

    def from_stored(values):
        blocks = values.reshape(values.shape[:-1] + (block_count, block_rows))
        return jnp.take(blocks, inverse_order, axis=-2).reshape(values.shape)

    gains = to_stored(norm_gains)
    token_count = variate_ids.shape[0]
    segment, offsets = prompt_layout(prompt_lengths[0], token_count)
    same_prompt = segment[:, None] == segment[None, :]
    same_variate = variate_ids[:, None] == variate_ids[None, :]
    head_count = variate_bias.shape[1]
    local_heads = head_count // tp_count
    head_size = head_cols // local_heads
    bias_table = lax.dynamic_slice_in_dim(
        variate_bias, lax.axis_index("tp") * local_heads, local_heads, 1
    )
    residual = to_stored(residual_in)
    for layer_index in range(layer_count):
        layer_bias = bias_table[layer_index]
        pair_bias = jnp.where(
            same_variate[None], layer_bias[:, 1][:, None, None], layer_bias[:, 0][:, None, None]
        )
        layer_weights = collect(layer_index)
        qkv_weight = layer_weights[:, : 3 * head_cols]
        out_weight = layer_weights[:, 3 * head_cols : 4 * head_cols]
        gate_up_weight = layer_weights[:, 4 * head_cols : 4 * head_cols + 2 * unit_cols]
        down_weight = layer_weights[:, 4 * head_cols + 2 * unit_cols :]
        normed = rms_scaled(residual, gains[layer_index, 0]).astype(jnp.bfloat16)
        projected = project_rows(gather_tp(normed, tp_count), weight=qkv_weight)
        queries = rotate(
            projected[:, :head_cols].reshape(token_count, local_heads, head_size), offsets
        ).astype(jnp.bfloat16)
        key_rows = rotate(
            projected[:, head_cols : 2 * head_cols].reshape(token_count, local_heads, head_size),
            offsets,
        ).astype(jnp.bfloat16)
        values = (
            projected[:, 2 * head_cols : 3 * head_cols]
            .reshape(token_count, local_heads, head_size)
            .astype(jnp.bfloat16)
        )
        scores = (
            jnp.einsum("qhd,khd->hqk", queries, key_rows, preferred_element_type=jnp.float32)
            * head_size ** (-0.5)
            + pair_bias
        )
        scores = jnp.where(same_prompt[None], scores, NEGATIVE)
        row_peak = jnp.max(scores, axis=2, keepdims=True)
        weights_exp = jnp.exp(scores - row_peak)
        attn_weights = (weights_exp / jnp.sum(weights_exp, axis=2, keepdims=True)).astype(
            jnp.bfloat16
        )
        mixed_heads = (
            jnp.einsum("hqk,khd->qhd", attn_weights, values, preferred_element_type=jnp.float32)
            .astype(jnp.bfloat16)
            .reshape(token_count, head_cols)
        )
        head_total = reduce_tp(
            project_out(source=mixed_heads, weight=out_weight).astype(jnp.bfloat16), tp_count
        )
        residual = residual + head_total
        normed_mlp = rms_scaled(residual, gains[layer_index, 1]).astype(jnp.bfloat16)
        hidden = gated_units(gather_tp(normed_mlp, tp_count), weight=gate_up_weight)
        unit_total = reduce_tp(
            project_out(source=hidden, weight=down_weight).astype(jnp.bfloat16), tp_count
        )
        residual = residual + unit_total
    return from_stored(residual)


def solution(mesh):
    seq_size = mesh.shape["seq"]
    chip_mesh = Mesh(
        mesh.devices.reshape((seq_size // 2, 2) + mesh.devices.shape[1:]),
        ("chip", "core", "tp"),
    )
    rows = SEQ_AXES + ("tp",)
    return jax.shard_map(
        on_device,
        mesh=chip_mesh,
        in_specs=(
            P(None, rows, None),
            P(),
            P(rows, None),
            P(),
            P(SEQ_AXES, None),
            P(SEQ_AXES),
            P(),
        ),
        out_specs=P(rows, None),
        check_vma=False,
    )
```

```python
import jax
import jax.numpy as jnp
from jax import lax
from jax.sharding import Mesh
from jax.sharding import PartitionSpec as P

NEGATIVE = -1e30
EPSILON = 1e-05
CHIP_AXES = "chip"
SEQ_AXES = ("chip", "core")


def rms_scaled(values, gain):
    mean_square = jnp.mean(values * values, axis=-1, keepdims=True)
    return values * lax.rsqrt(mean_square + EPSILON) * gain


def rotate(values, offsets):
    half_width = values.shape[-1] // 2
    frequency = 10000.0 ** (-jnp.arange(half_width, dtype=jnp.float32) / half_width)
    angles = offsets.astype(jnp.float32)[:, None] * frequency[None, :]
    cosine = jnp.cos(angles)[:, None, :]
    sine_part = jnp.sin(angles)[:, None, :]
    front_half = values[..., :half_width]
    back_half = values[..., half_width:]
    return jnp.concatenate(
        [front_half * cosine - back_half * sine_part, front_half * sine_part + back_half * cosine],
        axis=-1,
    )


def prompt_layout(lengths, token_count):
    prompt_ends = jnp.cumsum(lengths)
    prompt_starts = prompt_ends - lengths
    positions = jnp.arange(token_count, dtype=jnp.int32)
    segment = jnp.sum((positions[:, None] >= prompt_ends[None, :]).astype(jnp.int32), axis=1)
    member = segment[:, None] == jnp.arange(lengths.shape[0], dtype=jnp.int32)[None, :]
    offsets = positions - jnp.sum(jnp.where(member, prompt_starts[None, :], 0), axis=1)
    return (segment, offsets)


def project_rows(row_piece, weight):
    return jnp.dot(row_piece, weight, preferred_element_type=jnp.float32)


def gated_units(row_piece, weight):
    gate_up = jnp.dot(row_piece, weight, preferred_element_type=jnp.float32)
    half_width = weight.shape[1] // 2
    return (jax.nn.silu(gate_up[:, :half_width]) * gate_up[:, half_width:]).astype(jnp.bfloat16)


def project_out(source, weight):
    return lax.dot_general(
        source, weight, (((1,), (1,)), ((), ())), preferred_element_type=jnp.float32
    )


def gather_tp(values, tp_count):
    stacked = jnp.broadcast_to(values[None], (tp_count,) + values.shape)
    gathered = lax.all_to_all(stacked, "tp", 0, 0, tiled=True)
    return gathered.reshape((tp_count * values.shape[0],) + values.shape[1:])


def reduce_tp(products, tp_count):
    pieces = products.reshape((tp_count, products.shape[0] // tp_count) + products.shape[1:])
    received = lax.all_to_all(pieces, "tp", 0, 0, tiled=True)
    return jnp.sum(received.astype(jnp.float32), axis=0)


def on_device(
    trainer_rows, shard_order, residual_in, norm_gains, prompt_lengths, variate_ids, variate_bias
):
    tp_count = lax.axis_size("tp")
    seq_count = lax.axis_size(SEQ_AXES)
    layer_count, block_rows, total_cols = trainer_rows.shape
    model_width = residual_in.shape[1]
    ff_width = (total_cols - 4 * model_width) // 3
    head_cols = model_width // tp_count
    unit_cols = ff_width // tp_count
    block_count = seq_count * tp_count
    part_widths = [model_width] * 4 + [ff_width] * 3

    rounded = trainer_rows.astype(jnp.bfloat16)
    grouped_parts = []
    column_start = 0
    for part_width in part_widths:
        grouped_parts.append(
            rounded[:, :, column_start : column_start + part_width].reshape(
                layer_count, block_rows, tp_count, part_width // tp_count
            )
        )
        column_start = column_start + part_width
    grouped = jnp.concatenate(grouped_parts, axis=3)
    regrouped = lax.all_to_all(grouped, "tp", split_axis=2, concat_axis=1, tiled=True)
    chip_count = lax.axis_size(CHIP_AXES)
    core = lax.axis_index("core")
    core_swap = [(0, 1), (1, 0)]

    def join_cores(half):
        other = lax.ppermute(half, "core", core_swap)
        return jnp.concatenate([half, other], axis=0)

    def collect(layer_index):
        piece = regrouped[layer_index, :, 0, :]
        if layer_index == 0:
            stacked = jnp.broadcast_to(piece[None], (chip_count,) + piece.shape)
            half = lax.all_to_all(stacked, CHIP_AXES, 0, 0, tiled=True).reshape(
                chip_count * piece.shape[0], piece.shape[1]
            )
            return join_cores(half)
        return lax.all_gather(piece, SEQ_AXES, axis=0, tiled=True)

    block_index = jnp.arange(block_count, dtype=jnp.int32)
    half_blocks = block_count // 2
    core_of_block = jnp.where(block_index < half_blocks, core, 1 - core)
    within = block_index % half_blocks
    shard_of_block = ((within // tp_count) * 2 + core_of_block) * tp_count + within % tp_count
    block_of_shard = jnp.zeros_like(shard_of_block).at[shard_of_block].set(block_index)
    stored_orders = [shard_order[shard_of_block]] + [shard_order] * (layer_count - 1)

    def reorder(values, order):
        blocks = values.reshape(values.shape[:-1] + (block_count, block_rows))
        return jnp.take(blocks, order, axis=-2).reshape(values.shape)

    inverse_order = jnp.zeros_like(shard_order).at[shard_order].set(block_index)

    gains = [reorder(norm_gains[i], stored_orders[i]) for i in range(layer_count)]
    token_count = variate_ids.shape[0]
    segment, offsets = prompt_layout(prompt_lengths[0], token_count)
    same_prompt = segment[:, None] == segment[None, :]
    same_variate = variate_ids[:, None] == variate_ids[None, :]
    head_count = variate_bias.shape[1]
    local_heads = head_count // tp_count
    head_size = head_cols // local_heads
    bias_table = lax.dynamic_slice_in_dim(
        variate_bias, lax.axis_index("tp") * local_heads, local_heads, 1
    )
    residual = reorder(residual_in, stored_orders[0])
    for layer_index in range(layer_count):
        layer_bias = bias_table[layer_index]
        pair_bias = jnp.where(
            same_variate[None], layer_bias[:, 1][:, None, None], layer_bias[:, 0][:, None, None]
        )
        if layer_index == 1:
            residual = reorder(residual, block_of_shard)
        layer_weights = collect(layer_index)
        qkv_weight = layer_weights[:, : 3 * head_cols]
        out_weight = layer_weights[:, 3 * head_cols : 4 * head_cols]
        gate_up_weight = layer_weights[:, 4 * head_cols : 4 * head_cols + 2 * unit_cols]
        down_weight = layer_weights[:, 4 * head_cols + 2 * unit_cols :]
        normed = rms_scaled(residual, gains[layer_index][0]).astype(jnp.bfloat16)
        projected = project_rows(gather_tp(normed, tp_count), weight=qkv_weight)
        queries = rotate(
            projected[:, :head_cols].reshape(token_count, local_heads, head_size), offsets
        ).astype(jnp.bfloat16)
        key_rows = rotate(
            projected[:, head_cols : 2 * head_cols].reshape(token_count, local_heads, head_size),
            offsets,
        ).astype(jnp.bfloat16)
        values = (
            projected[:, 2 * head_cols : 3 * head_cols]
            .reshape(token_count, local_heads, head_size)
            .astype(jnp.bfloat16)
        )
        scores = (
            jnp.einsum("qhd,khd->hqk", queries, key_rows, preferred_element_type=jnp.float32)
            * head_size ** (-0.5)
            + pair_bias
        )
        scores = jnp.where(same_prompt[None], scores, NEGATIVE)
        row_peak = jnp.max(scores, axis=2, keepdims=True)
        weights_exp = jnp.exp(scores - row_peak)
        attn_weights = (weights_exp / jnp.sum(weights_exp, axis=2, keepdims=True)).astype(
            jnp.bfloat16
        )
        mixed_heads = (
            jnp.einsum("hqk,khd->qhd", attn_weights, values, preferred_element_type=jnp.float32)
            .astype(jnp.bfloat16)
            .reshape(token_count, head_cols)
        )
        head_total = reduce_tp(
            project_out(source=mixed_heads, weight=out_weight).astype(jnp.bfloat16), tp_count
        )
        residual = residual + head_total
        normed_mlp = rms_scaled(residual, gains[layer_index][1]).astype(jnp.bfloat16)
        hidden = gated_units(gather_tp(normed_mlp, tp_count), weight=gate_up_weight)
        unit_total = reduce_tp(
            project_out(source=hidden, weight=down_weight).astype(jnp.bfloat16), tp_count
        )
        residual = residual + unit_total
    return reorder(residual, inverse_order)


def solution(mesh):
    seq_size = mesh.shape["seq"]
    chip_mesh = Mesh(
        mesh.devices.reshape((seq_size // 2, 2) + mesh.devices.shape[1:]),
        ("chip", "core", "tp"),
    )
    rows = SEQ_AXES + ("tp",)
    return jax.shard_map(
        on_device,
        mesh=chip_mesh,
        in_specs=(
            P(None, rows, None),
            P(),
            P(rows, None),
            P(),
            P(SEQ_AXES, None),
            P(SEQ_AXES),
            P(),
        ),
        out_specs=P(rows, None),
        check_vma=False,
    )
```

```python
import jax
import jax.numpy as jnp
from jax import lax
from jax.sharding import Mesh
from jax.sharding import PartitionSpec as P

NEGATIVE = -1e30
EPSILON = 1e-05
CHIP_AXES = "chip"
SEQ_AXES = ("chip", "core")


def rms_scaled(values, gain):
    mean_square = jnp.mean(values * values, axis=-1, keepdims=True)
    return values * lax.rsqrt(mean_square + EPSILON) * gain


def rotate(values, offsets):
    half_width = values.shape[-1] // 2
    frequency = 10000.0 ** (-jnp.arange(half_width, dtype=jnp.float32) / half_width)
    angles = offsets.astype(jnp.float32)[:, None] * frequency[None, :]
    cosine = jnp.cos(angles)[:, None, :]
    sine_part = jnp.sin(angles)[:, None, :]
    front_half = values[..., :half_width]
    back_half = values[..., half_width:]
    return jnp.concatenate(
        [front_half * cosine - back_half * sine_part, front_half * sine_part + back_half * cosine],
        axis=-1,
    )


def prompt_layout(lengths, token_count):
    prompt_ends = jnp.cumsum(lengths)
    prompt_starts = prompt_ends - lengths
    positions = jnp.arange(token_count, dtype=jnp.int32)
    segment = jnp.sum((positions[:, None] >= prompt_ends[None, :]).astype(jnp.int32), axis=1)
    member = segment[:, None] == jnp.arange(lengths.shape[0], dtype=jnp.int32)[None, :]
    offsets = positions - jnp.sum(jnp.where(member, prompt_starts[None, :], 0), axis=1)
    return (segment, offsets)


def project_rows(row_piece, weight):
    return jnp.dot(row_piece, weight, preferred_element_type=jnp.float32)


def gated_units(row_piece, weight):
    gate_up = jnp.dot(row_piece, weight, preferred_element_type=jnp.float32)
    half_width = weight.shape[1] // 2
    return (jax.nn.silu(gate_up[:, :half_width]) * gate_up[:, half_width:]).astype(jnp.bfloat16)


def project_out(source, weight):
    return lax.dot_general(
        source, weight, (((1,), (1,)), ((), ())), preferred_element_type=jnp.float32
    )


def gather_tp(values, tp_count):
    stacked = jnp.broadcast_to(values[None], (tp_count,) + values.shape)
    gathered = lax.all_to_all(stacked, "tp", 0, 0, tiled=True)
    return gathered.reshape((tp_count * values.shape[0],) + values.shape[1:])


def reduce_tp(products, tp_count):
    pieces = products.reshape((tp_count, products.shape[0] // tp_count) + products.shape[1:])
    received = lax.all_to_all(pieces, "tp", 0, 0, tiled=True)
    return jnp.sum(received.astype(jnp.float32), axis=0)


def on_device(
    trainer_rows, shard_order, residual_in, norm_gains, prompt_lengths, variate_ids, variate_bias
):
    tp_count = lax.axis_size("tp")
    seq_count = lax.axis_size(SEQ_AXES)
    layer_count, block_rows, total_cols = trainer_rows.shape
    model_width = residual_in.shape[1]
    ff_width = (total_cols - 4 * model_width) // 3
    head_cols = model_width // tp_count
    unit_cols = ff_width // tp_count
    block_count = seq_count * tp_count
    part_widths = [model_width] * 4 + [ff_width] * 3

    rounded = trainer_rows.astype(jnp.bfloat16)
    grouped_parts = []
    column_start = 0
    for part_width in part_widths:
        grouped_parts.append(
            rounded[:, :, column_start : column_start + part_width].reshape(
                layer_count, block_rows, tp_count, part_width // tp_count
            )
        )
        column_start = column_start + part_width
    grouped = jnp.concatenate(grouped_parts, axis=3)
    weight_payload = jnp.moveaxis(grouped, 2, 0).reshape(tp_count, -1)
    chip_count = lax.axis_size(CHIP_AXES)
    core = lax.axis_index("core")
    core_swap = [(0, 1), (1, 0)]

    def join_cores(half):
        other = lax.ppermute(half, "core", core_swap)
        return jnp.concatenate([half, other], axis=0)

    def collect(layer_index, regrouped):
        piece = regrouped[layer_index]
        if layer_index == 0:
            stacked = jnp.broadcast_to(piece[None], (chip_count,) + piece.shape)
            half = lax.all_to_all(stacked, CHIP_AXES, 0, 0, tiled=True).reshape(
                chip_count * piece.shape[0], piece.shape[1]
            )
            return join_cores(half)
        return lax.all_gather(piece, SEQ_AXES, axis=0, tiled=True)

    block_index = jnp.arange(block_count, dtype=jnp.int32)
    half_blocks = block_count // 2
    core_of_block = jnp.where(block_index < half_blocks, core, 1 - core)
    within = block_index % half_blocks
    shard_of_block = ((within // tp_count) * 2 + core_of_block) * tp_count + within % tp_count
    block_of_shard = jnp.zeros_like(shard_of_block).at[shard_of_block].set(block_index)
    stored_orders = [shard_order[shard_of_block]] + [shard_order] * (layer_count - 1)

    def reorder(values, order):
        blocks = values.reshape(values.shape[:-1] + (block_count, block_rows))
        return jnp.take(blocks, order, axis=-2).reshape(values.shape)

    inverse_order = jnp.zeros_like(shard_order).at[shard_order].set(block_index)

    gains = [reorder(norm_gains[i], stored_orders[i]) for i in range(layer_count)]
    token_count = variate_ids.shape[0]
    segment, offsets = prompt_layout(prompt_lengths[0], token_count)
    same_prompt = segment[:, None] == segment[None, :]
    same_variate = variate_ids[:, None] == variate_ids[None, :]
    head_count = variate_bias.shape[1]
    local_heads = head_count // tp_count
    head_size = head_cols // local_heads
    bias_table = lax.dynamic_slice_in_dim(
        variate_bias, lax.axis_index("tp") * local_heads, local_heads, 1
    )
    residual = reorder(residual_in, stored_orders[0])
    for layer_index in range(layer_count):
        layer_bias = bias_table[layer_index]
        pair_bias = jnp.where(
            same_variate[None], layer_bias[:, 1][:, None, None], layer_bias[:, 0][:, None, None]
        )
        if layer_index == 1:
            residual = reorder(residual, block_of_shard)
        normed = rms_scaled(residual, gains[layer_index][0]).astype(jnp.bfloat16)
        if layer_index == 0:
            token_payload = jnp.broadcast_to(normed.reshape(1, -1), (tp_count, normed.size))
            received = lax.all_to_all(
                jnp.concatenate([token_payload, weight_payload], axis=1), "tp", 0, 0, tiled=True
            )
            gathered = received[:, : normed.size].reshape(tp_count * normed.shape[0], model_width)
            regrouped = jnp.moveaxis(
                received[:, normed.size :].reshape(tp_count, layer_count, block_rows, -1), 0, 1
            ).reshape(layer_count, tp_count * block_rows, -1)
        else:
            gathered = gather_tp(normed, tp_count)
        layer_weights = collect(layer_index, regrouped)
        qkv_weight = layer_weights[:, : 3 * head_cols]
        out_weight = layer_weights[:, 3 * head_cols : 4 * head_cols]
        gate_up_weight = layer_weights[:, 4 * head_cols : 4 * head_cols + 2 * unit_cols]
        down_weight = layer_weights[:, 4 * head_cols + 2 * unit_cols :]
        projected = project_rows(gathered, weight=qkv_weight)
        queries = rotate(
            projected[:, :head_cols].reshape(token_count, local_heads, head_size), offsets
        ).astype(jnp.bfloat16)
        key_rows = rotate(
            projected[:, head_cols : 2 * head_cols].reshape(token_count, local_heads, head_size),
            offsets,
        ).astype(jnp.bfloat16)
        values = (
            projected[:, 2 * head_cols : 3 * head_cols]
            .reshape(token_count, local_heads, head_size)
            .astype(jnp.bfloat16)
        )
        scores = (
            jnp.einsum("qhd,khd->hqk", queries, key_rows, preferred_element_type=jnp.float32)
            * head_size ** (-0.5)
            + pair_bias
        )
        scores = jnp.where(same_prompt[None], scores, NEGATIVE)
        row_peak = jnp.max(scores, axis=2, keepdims=True)
        weights_exp = jnp.exp(scores - row_peak)
        attn_weights = (weights_exp / jnp.sum(weights_exp, axis=2, keepdims=True)).astype(
            jnp.bfloat16
        )
        mixed_heads = (
            jnp.einsum("hqk,khd->qhd", attn_weights, values, preferred_element_type=jnp.float32)
            .astype(jnp.bfloat16)
            .reshape(token_count, head_cols)
        )
        head_total = reduce_tp(
            project_out(source=mixed_heads, weight=out_weight).astype(jnp.bfloat16), tp_count
        )
        residual = residual + head_total
        normed_mlp = rms_scaled(residual, gains[layer_index][1]).astype(jnp.bfloat16)
        hidden = gated_units(gather_tp(normed_mlp, tp_count), weight=gate_up_weight)
        unit_total = reduce_tp(
            project_out(source=hidden, weight=down_weight).astype(jnp.bfloat16), tp_count
        )
        residual = residual + unit_total
    return reorder(residual, inverse_order)


def solution(mesh):
    seq_size = mesh.shape["seq"]
    chip_mesh = Mesh(
        mesh.devices.reshape((seq_size // 2, 2) + mesh.devices.shape[1:]),
        ("chip", "core", "tp"),
    )
    rows = SEQ_AXES + ("tp",)
    return jax.shard_map(
        on_device,
        mesh=chip_mesh,
        in_specs=(
            P(None, rows, None),
            P(),
            P(rows, None),
            P(),
            P(SEQ_AXES, None),
            P(SEQ_AXES),
            P(),
        ),
        out_specs=P(rows, None),
        check_vma=False,
    )
```

```python
import jax
import jax.numpy as jnp
from jax import lax
from jax.sharding import Mesh
from jax.sharding import PartitionSpec as P

NEGATIVE = -1e30
EPSILON = 1e-05
CHIP_AXES = "chip"
SEQ_AXES = ("chip", "core")


def rms_scaled(values, gain):
    mean_square = jnp.mean(values * values, axis=-1, keepdims=True)
    return values * lax.rsqrt(mean_square + EPSILON) * gain


def rotate(values, offsets):
    half_width = values.shape[-1] // 2
    frequency = 10000.0 ** (-jnp.arange(half_width, dtype=jnp.float32) / half_width)
    angles = offsets.astype(jnp.float32)[:, None] * frequency[None, :]
    cosine = jnp.cos(angles)[:, None, :]
    sine_part = jnp.sin(angles)[:, None, :]
    front_half = values[..., :half_width]
    back_half = values[..., half_width:]
    return jnp.concatenate(
        [front_half * cosine - back_half * sine_part, front_half * sine_part + back_half * cosine],
        axis=-1,
    )


def prompt_layout(lengths, token_count):
    prompt_ends = jnp.cumsum(lengths)
    prompt_starts = prompt_ends - lengths
    positions = jnp.arange(token_count, dtype=jnp.int32)
    segment = jnp.sum((positions[:, None] >= prompt_ends[None, :]).astype(jnp.int32), axis=1)
    member = segment[:, None] == jnp.arange(lengths.shape[0], dtype=jnp.int32)[None, :]
    offsets = positions - jnp.sum(jnp.where(member, prompt_starts[None, :], 0), axis=1)
    return (segment, offsets)


def project_rows(row_piece, weight):
    return jnp.dot(row_piece, weight, preferred_element_type=jnp.float32)


def gated_units(row_piece, weight):
    gate_up = jnp.dot(row_piece, weight, preferred_element_type=jnp.float32)
    half_width = weight.shape[1] // 2
    return (jax.nn.silu(gate_up[:, :half_width]) * gate_up[:, half_width:]).astype(jnp.bfloat16)


def project_out(source, weight):
    return lax.dot_general(
        source, weight, (((1,), (1,)), ((), ())), preferred_element_type=jnp.float32
    )


def gather_tp(values, tp_count):
    stacked = jnp.broadcast_to(values[None], (tp_count,) + values.shape)
    gathered = lax.all_to_all(stacked, "tp", 0, 0, tiled=True)
    return gathered.reshape((tp_count * values.shape[0],) + values.shape[1:])


def reduce_tp(products, tp_count):
    pieces = products.reshape((tp_count, products.shape[0] // tp_count) + products.shape[1:])
    received = lax.all_to_all(pieces, "tp", 0, 0, tiled=True)
    return jnp.sum(received.astype(jnp.float32), axis=0)


def on_device(
    trainer_rows, shard_order, residual_in, norm_gains, prompt_lengths, variate_ids, variate_bias
):
    tp_count = lax.axis_size("tp")
    seq_count = lax.axis_size(SEQ_AXES)
    layer_count, block_rows, total_cols = trainer_rows.shape
    model_width = residual_in.shape[1]
    ff_width = (total_cols - 4 * model_width) // 3
    head_cols = model_width // tp_count
    unit_cols = ff_width // tp_count
    block_count = seq_count * tp_count
    part_widths = [model_width] * 4 + [ff_width] * 3

    rounded = trainer_rows.astype(jnp.bfloat16)
    grouped_parts = []
    column_start = 0
    for part_width in part_widths:
        grouped_parts.append(
            rounded[:, :, column_start : column_start + part_width].reshape(
                layer_count, block_rows, tp_count, part_width // tp_count
            )
        )
        column_start = column_start + part_width
    grouped = jnp.concatenate(grouped_parts, axis=3)
    regrouped = lax.all_to_all(grouped, "tp", split_axis=2, concat_axis=1, tiled=True)
    chip_count = lax.axis_size(CHIP_AXES)
    core = lax.axis_index("core")
    core_swap = [(0, 1), (1, 0)]

    def join_cores(half):
        other = lax.ppermute(half, "core", core_swap)
        return jnp.concatenate([half, other], axis=0)

    def collect(layer_index):
        piece = regrouped[layer_index, :, 0, :]
        if layer_index == 0:
            shifted = [piece] + [
                lax.ppermute(
                    piece, CHIP_AXES, [(i, (i + shift) % chip_count) for i in range(chip_count)]
                )
                for shift in range(1, chip_count)
            ]
            return join_cores(jnp.concatenate(shifted, axis=0))
        return lax.all_gather(piece, SEQ_AXES, axis=0, tiled=True)

    block_index = jnp.arange(block_count, dtype=jnp.int32)
    half_blocks = block_count // 2
    core_of_block = jnp.where(block_index < half_blocks, core, 1 - core)
    within = block_index % half_blocks
    source_chip = (lax.axis_index(CHIP_AXES) - within // tp_count) % chip_count
    shard_of_block = (source_chip * 2 + core_of_block) * tp_count + within % tp_count
    block_of_shard = jnp.zeros_like(shard_of_block).at[shard_of_block].set(block_index)
    stored_orders = [shard_order[shard_of_block]] + [shard_order] * (layer_count - 1)

    def reorder(values, order):
        blocks = values.reshape(values.shape[:-1] + (block_count, block_rows))
        return jnp.take(blocks, order, axis=-2).reshape(values.shape)

    inverse_order = jnp.zeros_like(shard_order).at[shard_order].set(block_index)

    gains = [reorder(norm_gains[i], stored_orders[i]) for i in range(layer_count)]
    token_count = variate_ids.shape[0]
    segment, offsets = prompt_layout(prompt_lengths[0], token_count)
    same_prompt = segment[:, None] == segment[None, :]
    same_variate = variate_ids[:, None] == variate_ids[None, :]
    head_count = variate_bias.shape[1]
    local_heads = head_count // tp_count
    head_size = head_cols // local_heads
    bias_table = lax.dynamic_slice_in_dim(
        variate_bias, lax.axis_index("tp") * local_heads, local_heads, 1
    )
    residual = reorder(residual_in, stored_orders[0])
    for layer_index in range(layer_count):
        layer_bias = bias_table[layer_index]
        pair_bias = jnp.where(
            same_variate[None], layer_bias[:, 1][:, None, None], layer_bias[:, 0][:, None, None]
        )
        if layer_index == 1:
            residual = reorder(residual, block_of_shard)
        layer_weights = collect(layer_index)
        qkv_weight = layer_weights[:, : 3 * head_cols]
        out_weight = layer_weights[:, 3 * head_cols : 4 * head_cols]
        gate_up_weight = layer_weights[:, 4 * head_cols : 4 * head_cols + 2 * unit_cols]
        down_weight = layer_weights[:, 4 * head_cols + 2 * unit_cols :]
        normed = rms_scaled(residual, gains[layer_index][0]).astype(jnp.bfloat16)
        projected = project_rows(gather_tp(normed, tp_count), weight=qkv_weight)
        queries = rotate(
            projected[:, :head_cols].reshape(token_count, local_heads, head_size), offsets
        ).astype(jnp.bfloat16)
        key_rows = rotate(
            projected[:, head_cols : 2 * head_cols].reshape(token_count, local_heads, head_size),
            offsets,
        ).astype(jnp.bfloat16)
        values = (
            projected[:, 2 * head_cols : 3 * head_cols]
            .reshape(token_count, local_heads, head_size)
            .astype(jnp.bfloat16)
        )
        scores = (
            jnp.einsum("qhd,khd->hqk", queries, key_rows, preferred_element_type=jnp.float32)
            * head_size ** (-0.5)
            + pair_bias
        )
        scores = jnp.where(same_prompt[None], scores, NEGATIVE)
        row_peak = jnp.max(scores, axis=2, keepdims=True)
        weights_exp = jnp.exp(scores - row_peak)
        attn_weights = (weights_exp / jnp.sum(weights_exp, axis=2, keepdims=True)).astype(
            jnp.bfloat16
        )
        mixed_heads = (
            jnp.einsum("hqk,khd->qhd", attn_weights, values, preferred_element_type=jnp.float32)
            .astype(jnp.bfloat16)
            .reshape(token_count, head_cols)
        )
        head_total = reduce_tp(
            project_out(source=mixed_heads, weight=out_weight).astype(jnp.bfloat16), tp_count
        )
        residual = residual + head_total
        normed_mlp = rms_scaled(residual, gains[layer_index][1]).astype(jnp.bfloat16)
        hidden = gated_units(gather_tp(normed_mlp, tp_count), weight=gate_up_weight)
        unit_total = reduce_tp(
            project_out(source=hidden, weight=down_weight).astype(jnp.bfloat16), tp_count
        )
        residual = residual + unit_total
    return reorder(residual, inverse_order)


def solution(mesh):
    seq_size = mesh.shape["seq"]
    chip_mesh = Mesh(
        mesh.devices.reshape((seq_size // 2, 2) + mesh.devices.shape[1:]),
        ("chip", "core", "tp"),
    )
    rows = SEQ_AXES + ("tp",)
    return jax.shard_map(
        on_device,
        mesh=chip_mesh,
        in_specs=(
            P(None, rows, None),
            P(),
            P(rows, None),
            P(),
            P(SEQ_AXES, None),
            P(SEQ_AXES),
            P(),
        ),
        out_specs=P(rows, None),
        check_vma=False,
    )
```

```python
import jax
import jax.numpy as jnp
from jax import lax
from jax.sharding import Mesh
from jax.sharding import PartitionSpec as P

NEGATIVE = -1e30
EPSILON = 1e-05
CHIP_AXES = "chip"
SEQ_AXES = ("chip", "core")


def rms_scaled(values, gain):
    mean_square = jnp.mean(values * values, axis=-1, keepdims=True)
    return values * lax.rsqrt(mean_square + EPSILON) * gain


def rotate(values, offsets):
    half_width = values.shape[-1] // 2
    frequency = 10000.0 ** (-jnp.arange(half_width, dtype=jnp.float32) / half_width)
    angles = offsets.astype(jnp.float32)[:, None] * frequency[None, :]
    cosine = jnp.cos(angles)[:, None, :]
    sine_part = jnp.sin(angles)[:, None, :]
    front_half = values[..., :half_width]
    back_half = values[..., half_width:]
    return jnp.concatenate(
        [front_half * cosine - back_half * sine_part, front_half * sine_part + back_half * cosine],
        axis=-1,
    )


def prompt_layout(lengths, token_count):
    prompt_ends = jnp.cumsum(lengths)
    prompt_starts = prompt_ends - lengths
    positions = jnp.arange(token_count, dtype=jnp.int32)
    segment = jnp.sum((positions[:, None] >= prompt_ends[None, :]).astype(jnp.int32), axis=1)
    member = segment[:, None] == jnp.arange(lengths.shape[0], dtype=jnp.int32)[None, :]
    offsets = positions - jnp.sum(jnp.where(member, prompt_starts[None, :], 0), axis=1)
    return (segment, offsets)


def project_rows(row_piece, weight):
    return jnp.dot(row_piece, weight, preferred_element_type=jnp.float32)


def gated_units(row_piece, weight):
    gate_up = jnp.dot(row_piece, weight, preferred_element_type=jnp.float32)
    half_width = weight.shape[1] // 2
    return (jax.nn.silu(gate_up[:, :half_width]) * gate_up[:, half_width:]).astype(jnp.bfloat16)


def project_out(source, weight):
    return lax.dot_general(
        source, weight, (((1,), (1,)), ((), ())), preferred_element_type=jnp.float32
    )


def gather_tp(values, tp_count):
    stacked = jnp.broadcast_to(values[None], (tp_count,) + values.shape)
    gathered = lax.all_to_all(stacked, "tp", 0, 0, tiled=True)
    return gathered.reshape((tp_count * values.shape[0],) + values.shape[1:])


def reduce_tp(products, tp_count):
    pieces = products.reshape((tp_count, products.shape[0] // tp_count) + products.shape[1:])
    received = lax.all_to_all(pieces, "tp", 0, 0, tiled=True)
    return jnp.sum(received.astype(jnp.float32), axis=0)


def project_owned(mixed_heads, out_weight, tp_count):
    own_rows = mixed_heads.shape[0] // tp_count
    pieces = mixed_heads.reshape(tp_count, own_rows, mixed_heads.shape[1])
    received = lax.all_to_all(pieces, "tp", 0, 0, tiled=True)
    group_weight = out_weight.reshape(out_weight.shape[0], tp_count, mixed_heads.shape[1])
    products = jnp.einsum(
        "gtc,rgc->gtr", received, group_weight, preferred_element_type=jnp.float32
    ).astype(jnp.bfloat16)
    return jnp.sum(products.astype(jnp.float32), axis=0)


def on_device(
    trainer_rows, shard_order, residual_in, norm_gains, prompt_lengths, variate_ids, variate_bias
):
    tp_count = lax.axis_size("tp")
    seq_count = lax.axis_size(SEQ_AXES)
    layer_count, block_rows, total_cols = trainer_rows.shape
    model_width = residual_in.shape[1]
    ff_width = (total_cols - 4 * model_width) // 3
    head_cols = model_width // tp_count
    unit_cols = ff_width // tp_count
    block_count = seq_count * tp_count
    part_widths = [model_width] * 4 + [ff_width] * 3

    rounded = trainer_rows.astype(jnp.bfloat16)
    grouped_parts = []
    column_start = 0
    for part_index, part_width in enumerate(part_widths):
        part = rounded[:, :, column_start : column_start + part_width]
        if part_index == 3:
            part = jnp.broadcast_to(part[:, :, None, :], (layer_count, block_rows, tp_count, part_width))
        else:
            part = part.reshape(layer_count, block_rows, tp_count, part_width // tp_count)
        grouped_parts.append(part)
        column_start = column_start + part_width
    grouped = jnp.concatenate(grouped_parts, axis=3)
    regrouped = lax.all_to_all(grouped, "tp", split_axis=2, concat_axis=1, tiled=True)
    chip_count = lax.axis_size(CHIP_AXES)
    core = lax.axis_index("core")
    core_swap = [(0, 1), (1, 0)]

    def join_cores(half):
        other = lax.ppermute(half, "core", core_swap)
        return jnp.concatenate([half, other], axis=0)

    def collect(layer_index):
        piece = regrouped[layer_index, :, 0, :]
        if layer_index == 0:
            stacked = jnp.broadcast_to(piece[None], (chip_count,) + piece.shape)
            half = lax.all_to_all(stacked, CHIP_AXES, 0, 0, tiled=True).reshape(
                chip_count * piece.shape[0], piece.shape[1]
            )
            return join_cores(half)
        return lax.all_gather(piece, SEQ_AXES, axis=0, tiled=True)

    block_index = jnp.arange(block_count, dtype=jnp.int32)
    half_blocks = block_count // 2
    core_of_block = jnp.where(block_index < half_blocks, core, 1 - core)
    within = block_index % half_blocks
    shard_of_block = ((within // tp_count) * 2 + core_of_block) * tp_count + within % tp_count
    block_of_shard = jnp.zeros_like(shard_of_block).at[shard_of_block].set(block_index)
    stored_orders = [shard_order[shard_of_block]] + [shard_order] * (layer_count - 1)

    def reorder(values, order):
        blocks = values.reshape(values.shape[:-1] + (block_count, block_rows))
        return jnp.take(blocks, order, axis=-2).reshape(values.shape)

    inverse_order = jnp.zeros_like(shard_order).at[shard_order].set(block_index)

    gains = [reorder(norm_gains[i], stored_orders[i]) for i in range(layer_count)]
    token_count = variate_ids.shape[0]
    segment, offsets = prompt_layout(prompt_lengths[0], token_count)
    same_prompt = segment[:, None] == segment[None, :]
    same_variate = variate_ids[:, None] == variate_ids[None, :]
    head_count = variate_bias.shape[1]
    local_heads = head_count // tp_count
    head_size = head_cols // local_heads
    bias_table = lax.dynamic_slice_in_dim(
        variate_bias, lax.axis_index("tp") * local_heads, local_heads, 1
    )
    residual = reorder(residual_in, stored_orders[0])
    for layer_index in range(layer_count):
        layer_bias = bias_table[layer_index]
        pair_bias = jnp.where(
            same_variate[None], layer_bias[:, 1][:, None, None], layer_bias[:, 0][:, None, None]
        )
        if layer_index == 1:
            residual = reorder(residual, block_of_shard)
        layer_weights = collect(layer_index)
        qkv_weight = layer_weights[:, : 3 * head_cols]
        mlp_start = 3 * head_cols + model_width
        out_weight = layer_weights[:, 3 * head_cols : mlp_start]
        gate_up_weight = layer_weights[:, mlp_start : mlp_start + 2 * unit_cols]
        down_weight = layer_weights[:, mlp_start + 2 * unit_cols :]
        normed = rms_scaled(residual, gains[layer_index][0]).astype(jnp.bfloat16)
        projected = project_rows(gather_tp(normed, tp_count), weight=qkv_weight)
        queries = rotate(
            projected[:, :head_cols].reshape(token_count, local_heads, head_size), offsets
        ).astype(jnp.bfloat16)
        key_rows = rotate(
            projected[:, head_cols : 2 * head_cols].reshape(token_count, local_heads, head_size),
            offsets,
        ).astype(jnp.bfloat16)
        values = (
            projected[:, 2 * head_cols : 3 * head_cols]
            .reshape(token_count, local_heads, head_size)
            .astype(jnp.bfloat16)
        )
        scores = (
            jnp.einsum("qhd,khd->hqk", queries, key_rows, preferred_element_type=jnp.float32)
            * head_size ** (-0.5)
            + pair_bias
        )
        scores = jnp.where(same_prompt[None], scores, NEGATIVE)
        row_peak = jnp.max(scores, axis=2, keepdims=True)
        weights_exp = jnp.exp(scores - row_peak)
        attn_weights = (weights_exp / jnp.sum(weights_exp, axis=2, keepdims=True)).astype(
            jnp.bfloat16
        )
        mixed_heads = (
            jnp.einsum("hqk,khd->qhd", attn_weights, values, preferred_element_type=jnp.float32)
            .astype(jnp.bfloat16)
            .reshape(token_count, head_cols)
        )
        head_total = project_owned(mixed_heads, out_weight, tp_count)
        residual = residual + head_total
        normed_mlp = rms_scaled(residual, gains[layer_index][1]).astype(jnp.bfloat16)
        hidden = gated_units(gather_tp(normed_mlp, tp_count), weight=gate_up_weight)
        unit_total = reduce_tp(
            project_out(source=hidden, weight=down_weight).astype(jnp.bfloat16), tp_count
        )
        residual = residual + unit_total
    return reorder(residual, inverse_order)


def solution(mesh):
    seq_size = mesh.shape["seq"]
    chip_mesh = Mesh(
        mesh.devices.reshape((seq_size // 2, 2) + mesh.devices.shape[1:]),
        ("chip", "core", "tp"),
    )
    rows = SEQ_AXES + ("tp",)
    return jax.shard_map(
        on_device,
        mesh=chip_mesh,
        in_specs=(
            P(None, rows, None),
            P(),
            P(rows, None),
            P(),
            P(SEQ_AXES, None),
            P(SEQ_AXES),
            P(),
        ),
        out_specs=P(rows, None),
        check_vma=False,
    )
```

```python
import jax
import jax.numpy as jnp
from jax import lax
from jax.sharding import Mesh
from jax.sharding import PartitionSpec as P

NEGATIVE = -1e30
EPSILON = 1e-05
CHIP_AXES = "chip"
SEQ_AXES = ("chip", "core")


def rms_scaled(values, gain):
    mean_square = jnp.mean(values * values, axis=-1, keepdims=True)
    return values * lax.rsqrt(mean_square + EPSILON) * gain


def rotate(values, offsets):
    half_width = values.shape[-1] // 2
    frequency = 10000.0 ** (-jnp.arange(half_width, dtype=jnp.float32) / half_width)
    angles = offsets.astype(jnp.float32)[:, None] * frequency[None, :]
    cosine = jnp.cos(angles)[:, None, :]
    sine_part = jnp.sin(angles)[:, None, :]
    front_half = values[..., :half_width]
    back_half = values[..., half_width:]
    return jnp.concatenate(
        [front_half * cosine - back_half * sine_part, front_half * sine_part + back_half * cosine],
        axis=-1,
    )


def prompt_layout(lengths, token_count):
    prompt_ends = jnp.cumsum(lengths)
    prompt_starts = prompt_ends - lengths
    positions = jnp.arange(token_count, dtype=jnp.int32)
    segment = jnp.sum((positions[:, None] >= prompt_ends[None, :]).astype(jnp.int32), axis=1)
    member = segment[:, None] == jnp.arange(lengths.shape[0], dtype=jnp.int32)[None, :]
    offsets = positions - jnp.sum(jnp.where(member, prompt_starts[None, :], 0), axis=1)
    return (segment, offsets)


def project_rows(row_piece, weight):
    return jnp.dot(row_piece, weight, preferred_element_type=jnp.float32)


def gated_units(row_piece, weight):
    gate_up = jnp.dot(row_piece, weight, preferred_element_type=jnp.float32)
    half_width = weight.shape[1] // 2
    return (jax.nn.silu(gate_up[:, :half_width]) * gate_up[:, half_width:]).astype(jnp.bfloat16)


def project_out(source, weight):
    return lax.dot_general(
        source, weight, (((1,), (1,)), ((), ())), preferred_element_type=jnp.float32
    )


def gather_tp(values, tp_count):
    stacked = jnp.broadcast_to(values[None], (tp_count,) + values.shape)
    gathered = lax.all_to_all(stacked, "tp", 0, 0, tiled=True)
    return gathered.reshape((tp_count * values.shape[0],) + values.shape[1:])


def reduce_tp(products, tp_count):
    pieces = products.reshape((tp_count, products.shape[0] // tp_count) + products.shape[1:])
    received = lax.all_to_all(pieces, "tp", 0, 0, tiled=True)
    return jnp.sum(received.astype(jnp.float32), axis=0)


def project_owned(mixed_heads, out_weight, tp_count):
    own_rows = mixed_heads.shape[0] // tp_count
    pieces = mixed_heads.reshape(tp_count, own_rows, mixed_heads.shape[1])
    received = lax.all_to_all(pieces, "tp", 0, 0, tiled=True)
    group_weight = out_weight.reshape(out_weight.shape[0], tp_count, mixed_heads.shape[1])
    products = jnp.einsum(
        "gtc,rgc->gtr", received, group_weight, preferred_element_type=jnp.float32
    ).astype(jnp.bfloat16)
    return jnp.sum(products.astype(jnp.float32), axis=0)


def on_device(
    trainer_rows, shard_order, residual_in, norm_gains, prompt_lengths, variate_ids, variate_bias
):
    tp_count = lax.axis_size("tp")
    seq_count = lax.axis_size(SEQ_AXES)
    layer_count, block_rows, total_cols = trainer_rows.shape
    model_width = residual_in.shape[1]
    ff_width = (total_cols - 4 * model_width) // 3
    head_cols = model_width // tp_count
    unit_cols = ff_width // tp_count
    block_count = seq_count * tp_count
    part_widths = [model_width] * 4 + [ff_width] * 3

    rounded = trainer_rows.astype(jnp.bfloat16)
    grouped_parts = []
    column_start = 0
    for part_index, part_width in enumerate(part_widths):
        part = rounded[:, :, column_start : column_start + part_width]
        if part_index == 3:
            part = jnp.broadcast_to(part[:, :, None, :], (layer_count, block_rows, tp_count, part_width))
        else:
            part = part.reshape(layer_count, block_rows, tp_count, part_width // tp_count)
        grouped_parts.append(part)
        column_start = column_start + part_width
    grouped = jnp.concatenate(grouped_parts, axis=3)
    regrouped = lax.all_to_all(grouped, "tp", split_axis=2, concat_axis=1, tiled=True)
    chip_count = lax.axis_size(CHIP_AXES)
    core = lax.axis_index("core")
    core_swap = [(0, 1), (1, 0)]

    def join_cores(half):
        other = lax.ppermute(half, "core", core_swap)
        return jnp.concatenate([half, other], axis=0)

    def gather_seq(piece):
        return lax.all_gather(piece, SEQ_AXES, axis=0, tiled=True)

    def gather_chips(piece):
        stacked = jnp.broadcast_to(piece[None], (chip_count,) + piece.shape)
        half = lax.all_to_all(stacked, CHIP_AXES, 0, 0, tiled=True).reshape(
            chip_count * piece.shape[0], piece.shape[1]
        )
        return join_cores(half)

    block_index = jnp.arange(block_count, dtype=jnp.int32)
    half_blocks = block_count // 2
    core_of_block = jnp.where(block_index < half_blocks, core, 1 - core)
    within = block_index % half_blocks
    shard_of_block = ((within // tp_count) * 2 + core_of_block) * tp_count + within % tp_count

    def reorder(values, order):
        blocks = values.reshape(values.shape[:-1] + (block_count, block_rows))
        return jnp.take(blocks, order, axis=-2).reshape(values.shape)

    inverse_order = jnp.zeros_like(shard_order).at[shard_order].set(block_index)

    gains = [reorder(norm_gains[i], shard_order) for i in range(layer_count)]
    token_count = variate_ids.shape[0]
    segment, offsets = prompt_layout(prompt_lengths[0], token_count)
    same_prompt = segment[:, None] == segment[None, :]
    same_variate = variate_ids[:, None] == variate_ids[None, :]
    head_count = variate_bias.shape[1]
    local_heads = head_count // tp_count
    head_size = head_cols // local_heads
    bias_table = lax.dynamic_slice_in_dim(
        variate_bias, lax.axis_index("tp") * local_heads, local_heads, 1
    )
    residual = reorder(residual_in, shard_order)
    for layer_index in range(layer_count):
        layer_bias = bias_table[layer_index]
        pair_bias = jnp.where(
            same_variate[None], layer_bias[:, 1][:, None, None], layer_bias[:, 0][:, None, None]
        )
        normed = rms_scaled(residual, gains[layer_index][0]).astype(jnp.bfloat16)
        piece = regrouped[layer_index, :, 0, :]
        if layer_index == 0:
            qkv_weight = gather_chips(piece[:, : 3 * head_cols])
            normed = reorder(normed, shard_of_block)
            layer_weights = gather_seq(piece[:, 3 * head_cols :])
        else:
            layer_weights = gather_seq(piece)
            qkv_weight = layer_weights[:, : 3 * head_cols]
            layer_weights = layer_weights[:, 3 * head_cols :]
        out_weight = layer_weights[:, :model_width]
        gate_up_weight = layer_weights[:, model_width : model_width + 2 * unit_cols]
        down_weight = layer_weights[:, model_width + 2 * unit_cols :]
        projected = project_rows(gather_tp(normed, tp_count), weight=qkv_weight)
        queries = rotate(
            projected[:, :head_cols].reshape(token_count, local_heads, head_size), offsets
        ).astype(jnp.bfloat16)
        key_rows = rotate(
            projected[:, head_cols : 2 * head_cols].reshape(token_count, local_heads, head_size),
            offsets,
        ).astype(jnp.bfloat16)
        values = (
            projected[:, 2 * head_cols : 3 * head_cols]
            .reshape(token_count, local_heads, head_size)
            .astype(jnp.bfloat16)
        )
        scores = (
            jnp.einsum("qhd,khd->hqk", queries, key_rows, preferred_element_type=jnp.float32)
            * head_size ** (-0.5)
            + pair_bias
        )
        scores = jnp.where(same_prompt[None], scores, NEGATIVE)
        row_peak = jnp.max(scores, axis=2, keepdims=True)
        weights_exp = jnp.exp(scores - row_peak)
        attn_weights = (weights_exp / jnp.sum(weights_exp, axis=2, keepdims=True)).astype(
            jnp.bfloat16
        )
        mixed_heads = (
            jnp.einsum("hqk,khd->qhd", attn_weights, values, preferred_element_type=jnp.float32)
            .astype(jnp.bfloat16)
            .reshape(token_count, head_cols)
        )
        head_total = project_owned(mixed_heads, out_weight, tp_count)
        residual = residual + head_total
        normed_mlp = rms_scaled(residual, gains[layer_index][1]).astype(jnp.bfloat16)
        hidden = gated_units(gather_tp(normed_mlp, tp_count), weight=gate_up_weight)
        unit_total = reduce_tp(
            project_out(source=hidden, weight=down_weight).astype(jnp.bfloat16), tp_count
        )
        residual = residual + unit_total
    return reorder(residual, inverse_order)


def solution(mesh):
    seq_size = mesh.shape["seq"]
    chip_mesh = Mesh(
        mesh.devices.reshape((seq_size // 2, 2) + mesh.devices.shape[1:]),
        ("chip", "core", "tp"),
    )
    rows = SEQ_AXES + ("tp",)
    return jax.shard_map(
        on_device,
        mesh=chip_mesh,
        in_specs=(
            P(None, rows, None),
            P(),
            P(rows, None),
            P(),
            P(SEQ_AXES, None),
            P(SEQ_AXES),
            P(),
        ),
        out_specs=P(rows, None),
        check_vma=False,
    )
```

```python
import jax
import jax.numpy as jnp
from jax import lax
from jax.sharding import Mesh
from jax.sharding import PartitionSpec as P

NEGATIVE = -1e30
EPSILON = 1e-05
CHIP_AXES = "chip"
SEQ_AXES = ("chip", "core")


def rms_scaled(values, gain):
    mean_square = jnp.mean(values * values, axis=-1, keepdims=True)
    return values * lax.rsqrt(mean_square + EPSILON) * gain


def rotate(values, offsets):
    half_width = values.shape[-1] // 2
    frequency = 10000.0 ** (-jnp.arange(half_width, dtype=jnp.float32) / half_width)
    angles = offsets.astype(jnp.float32)[:, None] * frequency[None, :]
    cosine = jnp.cos(angles)[:, None, :]
    sine_part = jnp.sin(angles)[:, None, :]
    front_half = values[..., :half_width]
    back_half = values[..., half_width:]
    return jnp.concatenate(
        [front_half * cosine - back_half * sine_part, front_half * sine_part + back_half * cosine],
        axis=-1,
    )


def prompt_layout(lengths, token_count):
    prompt_ends = jnp.cumsum(lengths)
    prompt_starts = prompt_ends - lengths
    positions = jnp.arange(token_count, dtype=jnp.int32)
    segment = jnp.sum((positions[:, None] >= prompt_ends[None, :]).astype(jnp.int32), axis=1)
    member = segment[:, None] == jnp.arange(lengths.shape[0], dtype=jnp.int32)[None, :]
    offsets = positions - jnp.sum(jnp.where(member, prompt_starts[None, :], 0), axis=1)
    return (segment, offsets)


def project_rows(row_piece, weight):
    return jnp.dot(row_piece, weight, preferred_element_type=jnp.float32)


def gated_units(row_piece, weight):
    gate_up = jnp.dot(row_piece, weight, preferred_element_type=jnp.float32)
    half_width = weight.shape[1] // 2
    return (jax.nn.silu(gate_up[:, :half_width]) * gate_up[:, half_width:]).astype(jnp.bfloat16)


def project_out(source, weight):
    return lax.dot_general(
        source, weight, (((1,), (1,)), ((), ())), preferred_element_type=jnp.float32
    )


def gather_tp(values, tp_count):
    stacked = jnp.broadcast_to(values[None], (tp_count,) + values.shape)
    gathered = lax.all_to_all(stacked, "tp", 0, 0, tiled=True)
    return gathered.reshape((tp_count * values.shape[0],) + values.shape[1:])


def reduce_tp(products, tp_count):
    pieces = products.reshape((tp_count, products.shape[0] // tp_count) + products.shape[1:])
    received = lax.all_to_all(pieces, "tp", 0, 0, tiled=True)
    return jnp.sum(received.astype(jnp.float32), axis=0)


def project_owned(mixed_heads, out_weight, tp_count):
    own_rows = mixed_heads.shape[0] // tp_count
    pieces = mixed_heads.reshape(tp_count, own_rows, mixed_heads.shape[1])
    received = lax.all_to_all(pieces, "tp", 0, 0, tiled=True)
    group_weight = out_weight.reshape(out_weight.shape[0], tp_count, mixed_heads.shape[1])
    products = jnp.einsum(
        "gtc,rgc->gtr", received, group_weight, preferred_element_type=jnp.float32
    ).astype(jnp.bfloat16)
    return jnp.sum(products.astype(jnp.float32), axis=0)


def on_device(
    trainer_rows, shard_order, residual_in, norm_gains, prompt_lengths, variate_ids, variate_bias
):
    tp_count = lax.axis_size("tp")
    seq_count = lax.axis_size(SEQ_AXES)
    layer_count, block_rows, total_cols = trainer_rows.shape
    model_width = residual_in.shape[1]
    ff_width = (total_cols - 4 * model_width) // 3
    head_cols = model_width // tp_count
    unit_cols = ff_width // tp_count
    block_count = seq_count * tp_count
    part_widths = [model_width] * 4 + [ff_width] * 3

    rounded = trainer_rows.astype(jnp.bfloat16)
    grouped_parts = []
    column_start = 0
    for part_index, part_width in enumerate(part_widths):
        part = rounded[:, :, column_start : column_start + part_width]
        if part_index == 3:
            part = jnp.broadcast_to(part[:, :, None, :], (layer_count, block_rows, tp_count, part_width))
        else:
            part = part.reshape(layer_count, block_rows, tp_count, part_width // tp_count)
        grouped_parts.append(part)
        column_start = column_start + part_width
    grouped = jnp.concatenate(grouped_parts, axis=3)
    attention_cols = 3 * head_cols + model_width
    grouped = jnp.concatenate([grouped[0], grouped[1, :, :, :attention_cols]], axis=2)
    regrouped = lax.all_to_all(grouped, "tp", split_axis=1, concat_axis=0, tiled=True)
    chip_count = lax.axis_size(CHIP_AXES)
    core = lax.axis_index("core")
    core_swap = [(0, 1), (1, 0)]

    def join_cores(half):
        other = lax.ppermute(half, "core", core_swap)
        return jnp.concatenate([half, other], axis=0)

    def gather_seq(piece):
        return lax.all_gather(piece, SEQ_AXES, axis=0, tiled=True)

    def gather_chips(piece):
        stacked = jnp.broadcast_to(piece[None], (chip_count,) + piece.shape)
        half = lax.all_to_all(stacked, CHIP_AXES, 0, 0, tiled=True).reshape(
            chip_count * piece.shape[0], piece.shape[1]
        )
        return join_cores(half)

    block_index = jnp.arange(block_count, dtype=jnp.int32)
    half_blocks = block_count // 2
    core_of_block = jnp.where(block_index < half_blocks, core, 1 - core)
    within = block_index % half_blocks
    shard_of_block = ((within // tp_count) * 2 + core_of_block) * tp_count + within % tp_count

    def reorder(values, order):
        blocks = values.reshape(values.shape[:-1] + (block_count, block_rows))
        return jnp.take(blocks, order, axis=-2).reshape(values.shape)

    inverse_order = jnp.zeros_like(shard_order).at[shard_order].set(block_index)

    gains = [reorder(norm_gains[i], shard_order) for i in range(layer_count)]
    token_count = variate_ids.shape[0]
    segment, offsets = prompt_layout(prompt_lengths[0], token_count)
    same_prompt = segment[:, None] == segment[None, :]
    same_variate = variate_ids[:, None] == variate_ids[None, :]
    head_count = variate_bias.shape[1]
    local_heads = head_count // tp_count
    head_size = head_cols // local_heads
    bias_table = lax.dynamic_slice_in_dim(
        variate_bias, lax.axis_index("tp") * local_heads, local_heads, 1
    )
    residual = reorder(residual_in, shard_order)
    for layer_index in range(layer_count):
        layer_bias = bias_table[layer_index]
        pair_bias = jnp.where(
            same_variate[None], layer_bias[:, 1][:, None, None], layer_bias[:, 0][:, None, None]
        )
        normed = rms_scaled(residual, gains[layer_index][0]).astype(jnp.bfloat16)
        first_cols = regrouped.shape[2] - attention_cols
        piece = regrouped[:, 0, :first_cols] if layer_index == 0 else regrouped[:, 0, first_cols:]
        if layer_index == 0:
            qkv_weight = gather_chips(piece[:, : 3 * head_cols])
            normed = reorder(normed, shard_of_block)
            layer_weights = gather_seq(piece[:, 3 * head_cols :])
        else:
            layer_weights = gather_seq(piece)
            qkv_weight = layer_weights[:, : 3 * head_cols]
            layer_weights = layer_weights[:, 3 * head_cols :]
            full_mlp = lax.all_gather(
                rounded[layer_index, :, 4 * model_width :], SEQ_AXES + ("tp",), axis=0, tiled=True
            )
        out_weight = layer_weights[:, :model_width]
        gate_up_weight = layer_weights[:, model_width : model_width + 2 * unit_cols]
        down_weight = layer_weights[:, model_width + 2 * unit_cols :]
        projected = project_rows(gather_tp(normed, tp_count), weight=qkv_weight)
        queries = rotate(
            projected[:, :head_cols].reshape(token_count, local_heads, head_size), offsets
        ).astype(jnp.bfloat16)
        key_rows = rotate(
            projected[:, head_cols : 2 * head_cols].reshape(token_count, local_heads, head_size),
            offsets,
        ).astype(jnp.bfloat16)
        values = (
            projected[:, 2 * head_cols : 3 * head_cols]
            .reshape(token_count, local_heads, head_size)
            .astype(jnp.bfloat16)
        )
        scores = (
            jnp.einsum("qhd,khd->hqk", queries, key_rows, preferred_element_type=jnp.float32)
            * head_size ** (-0.5)
            + pair_bias
        )
        scores = jnp.where(same_prompt[None], scores, NEGATIVE)
        row_peak = jnp.max(scores, axis=2, keepdims=True)
        weights_exp = jnp.exp(scores - row_peak)
        attn_weights = (weights_exp / jnp.sum(weights_exp, axis=2, keepdims=True)).astype(
            jnp.bfloat16
        )
        mixed_heads = (
            jnp.einsum("hqk,khd->qhd", attn_weights, values, preferred_element_type=jnp.float32)
            .astype(jnp.bfloat16)
            .reshape(token_count, head_cols)
        )
        head_total = project_owned(mixed_heads, out_weight, tp_count)
        residual = residual + head_total
        normed_mlp = rms_scaled(residual, gains[layer_index][1]).astype(jnp.bfloat16)
        if layer_index == 0:
            hidden = gated_units(gather_tp(normed_mlp, tp_count), weight=gate_up_weight)
            unit_total = reduce_tp(
                project_out(source=hidden, weight=down_weight).astype(jnp.bfloat16), tp_count
            )
        else:
            hidden = gated_units(normed_mlp, weight=full_mlp[:, : 2 * ff_width])
            group_weight = full_mlp[:, 2 * ff_width :].reshape(model_width, tp_count, unit_cols)
            products = jnp.einsum(
                "tgu,rgu->gtr",
                hidden.reshape(hidden.shape[0], tp_count, unit_cols),
                group_weight,
                preferred_element_type=jnp.float32,
            ).astype(jnp.bfloat16)
            unit_total = jnp.sum(products.astype(jnp.float32), axis=0)
        residual = residual + unit_total
    return reorder(residual, inverse_order)


def solution(mesh):
    seq_size = mesh.shape["seq"]
    chip_mesh = Mesh(
        mesh.devices.reshape((seq_size // 2, 2) + mesh.devices.shape[1:]),
        ("chip", "core", "tp"),
    )
    rows = SEQ_AXES + ("tp",)
    return jax.shard_map(
        on_device,
        mesh=chip_mesh,
        in_specs=(
            P(None, rows, None),
            P(),
            P(rows, None),
            P(),
            P(SEQ_AXES, None),
            P(SEQ_AXES),
            P(),
        ),
        out_specs=P(rows, None),
        check_vma=False,
    )
```

```python
import jax
import jax.numpy as jnp
from jax import lax
from jax.sharding import Mesh
from jax.sharding import PartitionSpec as P

NEGATIVE = -1e30
EPSILON = 1e-05
CHIP_AXES = "chip"
SEQ_AXES = ("chip", "core")


def rms_scaled(values, gain):
    mean_square = jnp.mean(values * values, axis=-1, keepdims=True)
    return values * lax.rsqrt(mean_square + EPSILON) * gain


def rotate(values, offsets):
    half_width = values.shape[-1] // 2
    frequency = 10000.0 ** (-jnp.arange(half_width, dtype=jnp.float32) / half_width)
    angles = offsets.astype(jnp.float32)[:, None] * frequency[None, :]
    cosine = jnp.cos(angles)[:, None, :]
    sine_part = jnp.sin(angles)[:, None, :]
    front_half = values[..., :half_width]
    back_half = values[..., half_width:]
    return jnp.concatenate(
        [front_half * cosine - back_half * sine_part, front_half * sine_part + back_half * cosine],
        axis=-1,
    )


def prompt_layout(lengths, token_count):
    prompt_ends = jnp.cumsum(lengths)
    prompt_starts = prompt_ends - lengths
    positions = jnp.arange(token_count, dtype=jnp.int32)
    segment = jnp.sum((positions[:, None] >= prompt_ends[None, :]).astype(jnp.int32), axis=1)
    member = segment[:, None] == jnp.arange(lengths.shape[0], dtype=jnp.int32)[None, :]
    offsets = positions - jnp.sum(jnp.where(member, prompt_starts[None, :], 0), axis=1)
    return (segment, offsets)


def project_rows(row_piece, weight):
    return jnp.dot(row_piece, weight, preferred_element_type=jnp.float32)


def gated_units(row_piece, weight):
    gate_up = jnp.dot(row_piece, weight, preferred_element_type=jnp.float32)
    half_width = weight.shape[1] // 2
    return (jax.nn.silu(gate_up[:, :half_width]) * gate_up[:, half_width:]).astype(jnp.bfloat16)


def project_out(source, weight):
    return lax.dot_general(
        source, weight, (((1,), (1,)), ((), ())), preferred_element_type=jnp.float32
    )


def gather_tp(values, tp_count):
    stacked = jnp.broadcast_to(values[None], (tp_count,) + values.shape)
    gathered = lax.all_to_all(stacked, "tp", 0, 0, tiled=True)
    return gathered.reshape((tp_count * values.shape[0],) + values.shape[1:])


def reduce_tp(products, tp_count):
    pieces = products.reshape((tp_count, products.shape[0] // tp_count) + products.shape[1:])
    received = lax.all_to_all(pieces, "tp", 0, 0, tiled=True)
    return jnp.sum(received.astype(jnp.float32), axis=0)


def project_owned(mixed_heads, out_weight, tp_count):
    own_rows = mixed_heads.shape[0] // tp_count
    pieces = mixed_heads.reshape(tp_count, own_rows, mixed_heads.shape[1])
    received = lax.all_to_all(pieces, "tp", 0, 0, tiled=True)
    group_weight = out_weight.reshape(out_weight.shape[0], tp_count, mixed_heads.shape[1])
    products = jnp.einsum(
        "gtc,rgc->gtr", received, group_weight, preferred_element_type=jnp.float32
    ).astype(jnp.bfloat16)
    return jnp.sum(products.astype(jnp.float32), axis=0)


def owned_qkv(normed, qkv_weight, own_offsets, tp_count, head_count, head_size):
    own_rows, model_width = normed.shape
    projected = project_rows(normed, weight=qkv_weight)
    queries = rotate(projected[:, :model_width].reshape(own_rows, head_count, head_size), own_offsets)
    key_rows = rotate(
        projected[:, model_width : 2 * model_width].reshape(own_rows, head_count, head_size),
        own_offsets,
    )
    values = projected[:, 2 * model_width :].reshape(own_rows, head_count, head_size)
    local_heads = head_count // tp_count
    stacked = jnp.stack([queries, key_rows, values], axis=0).astype(jnp.bfloat16)
    pieces = jnp.moveaxis(
        stacked.reshape(3, own_rows, tp_count, local_heads, head_size), 2, 0
    )
    received = lax.all_to_all(pieces, "tp", 0, 0, tiled=True)
    gathered = jnp.moveaxis(received, 1, 0).reshape(3, tp_count * own_rows, local_heads, head_size)
    return gathered[0], gathered[1], gathered[2]


def on_device(
    trainer_rows, shard_order, residual_in, norm_gains, prompt_lengths, variate_ids, variate_bias
):
    tp_count = lax.axis_size("tp")
    seq_count = lax.axis_size(SEQ_AXES)
    layer_count, block_rows, total_cols = trainer_rows.shape
    model_width = residual_in.shape[1]
    ff_width = (total_cols - 4 * model_width) // 3
    head_cols = model_width // tp_count
    unit_cols = ff_width // tp_count
    block_count = seq_count * tp_count
    part_widths = [model_width] * 4 + [ff_width] * 3

    rounded = trainer_rows.astype(jnp.bfloat16)
    grouped_parts = []
    for layer_index in range(layer_count):
        column_start = 0
        for part_index, part_width in enumerate(part_widths):
            part = rounded[layer_index, :, column_start : column_start + part_width]
            if part_index == 3 or (part_index < 3 and layer_index > 0):
                part = jnp.broadcast_to(part[:, None, :], (block_rows, tp_count, part_width))
            else:
                part = part.reshape(block_rows, tp_count, part_width // tp_count)
            grouped_parts.append(part)
            column_start = column_start + part_width
    grouped = jnp.concatenate(grouped_parts, axis=2)
    first_cols = 3 * head_cols + model_width + 3 * unit_cols
    regrouped = lax.all_to_all(grouped, "tp", split_axis=1, concat_axis=0, tiled=True)
    chip_count = lax.axis_size(CHIP_AXES)
    core = lax.axis_index("core")
    core_swap = [(0, 1), (1, 0)]

    def join_cores(half):
        other = lax.ppermute(half, "core", core_swap)
        return jnp.concatenate([half, other], axis=0)

    def gather_seq(piece):
        return lax.all_gather(piece, SEQ_AXES, axis=0, tiled=True)

    def gather_chips(piece):
        stacked = jnp.broadcast_to(piece[None], (chip_count,) + piece.shape)
        half = lax.all_to_all(stacked, CHIP_AXES, 0, 0, tiled=True).reshape(
            chip_count * piece.shape[0], piece.shape[1]
        )
        return join_cores(half)

    block_index = jnp.arange(block_count, dtype=jnp.int32)
    half_blocks = block_count // 2
    core_of_block = jnp.where(block_index < half_blocks, core, 1 - core)
    within = block_index % half_blocks
    shard_of_block = ((within // tp_count) * 2 + core_of_block) * tp_count + within % tp_count

    def reorder(values, order):
        blocks = values.reshape(values.shape[:-1] + (block_count, block_rows))
        return jnp.take(blocks, order, axis=-2).reshape(values.shape)

    inverse_order = jnp.zeros_like(shard_order).at[shard_order].set(block_index)

    gains = [reorder(norm_gains[i], shard_order) for i in range(layer_count)]
    token_count = variate_ids.shape[0]
    segment, offsets = prompt_layout(prompt_lengths[0], token_count)
    same_prompt = segment[:, None] == segment[None, :]
    same_variate = variate_ids[:, None] == variate_ids[None, :]
    head_count = variate_bias.shape[1]
    local_heads = head_count // tp_count
    head_size = head_cols // local_heads
    bias_table = lax.dynamic_slice_in_dim(
        variate_bias, lax.axis_index("tp") * local_heads, local_heads, 1
    )
    residual = reorder(residual_in, shard_order)
    own_offsets = lax.dynamic_slice_in_dim(
        offsets, lax.axis_index("tp") * residual.shape[0], residual.shape[0]
    )
    for layer_index in range(layer_count):
        layer_bias = bias_table[layer_index]
        pair_bias = jnp.where(
            same_variate[None], layer_bias[:, 1][:, None, None], layer_bias[:, 0][:, None, None]
        )
        normed = rms_scaled(residual, gains[layer_index][0]).astype(jnp.bfloat16)
        if layer_index == 0:
            piece = regrouped[:, 0, :first_cols]
            qkv_weight = gather_chips(piece[:, : 3 * head_cols])
            normed = reorder(normed, shard_of_block)
            layer_weights = gather_seq(piece[:, 3 * head_cols :])
            projected = project_rows(gather_tp(normed, tp_count), weight=qkv_weight)
            queries = rotate(
                projected[:, :head_cols].reshape(token_count, local_heads, head_size), offsets
            ).astype(jnp.bfloat16)
            key_rows = rotate(
                projected[:, head_cols : 2 * head_cols].reshape(token_count, local_heads, head_size),
                offsets,
            ).astype(jnp.bfloat16)
            values = (
                projected[:, 2 * head_cols : 3 * head_cols]
                .reshape(token_count, local_heads, head_size)
                .astype(jnp.bfloat16)
            )
        else:
            layer_weights = gather_seq(regrouped[:, 0, first_cols:])
            qkv_weight = layer_weights[:, : 3 * model_width]
            layer_weights = layer_weights[:, 3 * model_width :]
            queries, key_rows, values = owned_qkv(
                normed, qkv_weight, own_offsets, tp_count, head_count, head_size
            )
        out_weight = layer_weights[:, :model_width]
        gate_up_weight = layer_weights[:, model_width : model_width + 2 * unit_cols]
        down_weight = layer_weights[:, model_width + 2 * unit_cols :]
        scores = (
            jnp.einsum("qhd,khd->hqk", queries, key_rows, preferred_element_type=jnp.float32)
            * head_size ** (-0.5)
            + pair_bias
        )
        scores = jnp.where(same_prompt[None], scores, NEGATIVE)
        row_peak = jnp.max(scores, axis=2, keepdims=True)
        weights_exp = jnp.exp(scores - row_peak)
        attn_weights = (weights_exp / jnp.sum(weights_exp, axis=2, keepdims=True)).astype(
            jnp.bfloat16
        )
        mixed_heads = (
            jnp.einsum("hqk,khd->qhd", attn_weights, values, preferred_element_type=jnp.float32)
            .astype(jnp.bfloat16)
            .reshape(token_count, head_cols)
        )
        head_total = project_owned(mixed_heads, out_weight, tp_count)
        residual = residual + head_total
        normed_mlp = rms_scaled(residual, gains[layer_index][1]).astype(jnp.bfloat16)
        hidden = gated_units(gather_tp(normed_mlp, tp_count), weight=gate_up_weight)
        unit_total = reduce_tp(
            project_out(source=hidden, weight=down_weight).astype(jnp.bfloat16), tp_count
        )
        residual = residual + unit_total
    return reorder(residual, inverse_order)


def solution(mesh):
    seq_size = mesh.shape["seq"]
    chip_mesh = Mesh(
        mesh.devices.reshape((seq_size // 2, 2) + mesh.devices.shape[1:]),
        ("chip", "core", "tp"),
    )
    rows = SEQ_AXES + ("tp",)
    return jax.shard_map(
        on_device,
        mesh=chip_mesh,
        in_specs=(
            P(None, rows, None),
            P(),
            P(rows, None),
            P(),
            P(SEQ_AXES, None),
            P(SEQ_AXES),
            P(),
        ),
        out_specs=P(rows, None),
        check_vma=False,
    )
```

```python
import jax
import jax.numpy as jnp
from jax import lax
from jax.sharding import Mesh
from jax.sharding import PartitionSpec as P

NEGATIVE = -1e30
EPSILON = 1e-05
CHIP_AXES = "chip"
SEQ_AXES = ("chip", "core")


def rms_scaled(values, gain):
    mean_square = jnp.mean(values * values, axis=-1, keepdims=True)
    return values * lax.rsqrt(mean_square + EPSILON) * gain


def rotate(values, offsets):
    half_width = values.shape[-1] // 2
    frequency = 10000.0 ** (-jnp.arange(half_width, dtype=jnp.float32) / half_width)
    angles = offsets.astype(jnp.float32)[:, None] * frequency[None, :]
    cosine = jnp.cos(angles)[:, None, :]
    sine_part = jnp.sin(angles)[:, None, :]
    front_half = values[..., :half_width]
    back_half = values[..., half_width:]
    return jnp.concatenate(
        [front_half * cosine - back_half * sine_part, front_half * sine_part + back_half * cosine],
        axis=-1,
    )


def prompt_layout(lengths, token_count):
    prompt_ends = jnp.cumsum(lengths)
    prompt_starts = prompt_ends - lengths
    positions = jnp.arange(token_count, dtype=jnp.int32)
    segment = jnp.sum((positions[:, None] >= prompt_ends[None, :]).astype(jnp.int32), axis=1)
    member = segment[:, None] == jnp.arange(lengths.shape[0], dtype=jnp.int32)[None, :]
    offsets = positions - jnp.sum(jnp.where(member, prompt_starts[None, :], 0), axis=1)
    return (segment, offsets)


def project_rows(row_piece, weight):
    return jnp.dot(row_piece, weight, preferred_element_type=jnp.float32)


def gated_units(row_piece, weight):
    gate_up = jnp.dot(row_piece, weight, preferred_element_type=jnp.float32)
    half_width = weight.shape[1] // 2
    return (jax.nn.silu(gate_up[:, :half_width]) * gate_up[:, half_width:]).astype(jnp.bfloat16)


def project_out(source, weight):
    return lax.dot_general(
        source, weight, (((1,), (1,)), ((), ())), preferred_element_type=jnp.float32
    )


def gather_tp(values, tp_count):
    stacked = jnp.broadcast_to(values[None], (tp_count,) + values.shape)
    gathered = lax.all_to_all(stacked, "tp", 0, 0, tiled=True)
    return gathered.reshape((tp_count * values.shape[0],) + values.shape[1:])


def reduce_tp(products, tp_count):
    pieces = products.reshape((tp_count, products.shape[0] // tp_count) + products.shape[1:])
    received = lax.all_to_all(pieces, "tp", 0, 0, tiled=True)
    return jnp.sum(received.astype(jnp.float32), axis=0)


def project_owned(mixed_heads, out_weight, tp_count):
    own_rows = mixed_heads.shape[0] // tp_count
    pieces = mixed_heads.reshape(tp_count, own_rows, mixed_heads.shape[1])
    received = lax.all_to_all(pieces, "tp", 0, 0, tiled=True)
    group_weight = out_weight.reshape(out_weight.shape[0], tp_count, mixed_heads.shape[1])
    products = jnp.einsum(
        "gtc,rgc->gtr", received, group_weight, preferred_element_type=jnp.float32
    ).astype(jnp.bfloat16)
    return jnp.sum(products.astype(jnp.float32), axis=0)


def core_pair_mlp(normed_mlp, pair_mlp, shard_of_block, block_of_shard, core_swap, tp_count):
    own_rows, model_width = normed_mlp.shape
    block_count = shard_of_block.shape[0]

    def reorder(values, order):
        blocks = values.reshape(values.shape[:-1] + (block_count, model_width // block_count))
        return jnp.take(blocks, order, axis=-2).reshape(values.shape)

    partner = lax.ppermute(normed_mlp, "core", core_swap)
    tokens = reorder(jnp.concatenate([normed_mlp, partner], axis=0), shard_of_block)
    half_units = pair_mlp.shape[2]
    gate_up = jnp.dot(
        tokens, pair_mlp[:, :2].reshape(model_width, 2 * half_units), preferred_element_type=jnp.float32
    )
    hidden = (jax.nn.silu(gate_up[:, :half_units]) * gate_up[:, half_units:]).astype(jnp.bfloat16)
    group_count = tp_count // 2
    group_width = half_units // group_count
    products = jnp.einsum(
        "tgu,rgu->gtr",
        hidden.reshape(hidden.shape[0], group_count, group_width),
        pair_mlp[:, 2].reshape(model_width, group_count, group_width),
        preferred_element_type=jnp.float32,
    ).astype(jnp.bfloat16)
    partial = reorder(jnp.sum(products.astype(jnp.float32), axis=0), block_of_shard)
    return partial[:own_rows] + lax.ppermute(partial[own_rows:], "core", core_swap)


def on_device(
    trainer_rows, shard_order, residual_in, norm_gains, prompt_lengths, variate_ids, variate_bias
):
    tp_count = lax.axis_size("tp")
    seq_count = lax.axis_size(SEQ_AXES)
    layer_count, block_rows, total_cols = trainer_rows.shape
    model_width = residual_in.shape[1]
    ff_width = (total_cols - 4 * model_width) // 3
    head_cols = model_width // tp_count
    unit_cols = ff_width // tp_count
    block_count = seq_count * tp_count
    part_widths = [model_width] * 4 + [ff_width] * 3

    rounded = trainer_rows.astype(jnp.bfloat16)
    grouped_parts = []
    for layer_index in range(layer_count):
        column_start = 0
        for part_index, part_width in enumerate(part_widths):
            part = rounded[layer_index, :, column_start : column_start + part_width]
            column_start = column_start + part_width
            if part_index > 3 and layer_index > 0:
                continue
            if part_index == 3:
                part = jnp.broadcast_to(part[:, None, :], (block_rows, tp_count, part_width))
            else:
                part = part.reshape(block_rows, tp_count, part_width // tp_count)
            grouped_parts.append(part)
    grouped = jnp.concatenate(grouped_parts, axis=2)
    regrouped = lax.all_to_all(grouped, "tp", split_axis=1, concat_axis=0, tiled=True)
    first_cols = 3 * head_cols + model_width + 3 * unit_cols
    core = lax.axis_index("core")
    core_swap = [(0, 1), (1, 0)]
    mlp_rows = jnp.broadcast_to(
        rounded[1, :, 4 * model_width :][:, None, :], (block_rows, tp_count, 3 * ff_width)
    )
    mlp_chip_rows = lax.all_gather(
        lax.all_to_all(mlp_rows, "tp", split_axis=1, concat_axis=0, tiled=True)[:, 0, :],
        CHIP_AXES,
        axis=0,
        tiled=True,
    ).reshape(block_count // 2 * block_rows, 3, 2, ff_width // 2)
    own_units = lax.dynamic_index_in_dim(mlp_chip_rows, core, axis=2, keepdims=False)
    other_units = lax.dynamic_index_in_dim(mlp_chip_rows, 1 - core, axis=2, keepdims=False)
    pair_mlp = jnp.concatenate([own_units, lax.ppermute(other_units, "core", core_swap)], axis=0)
    chip_count = lax.axis_size(CHIP_AXES)

    def join_cores(half):
        other = lax.ppermute(half, "core", core_swap)
        return jnp.concatenate([half, other], axis=0)

    def gather_seq(piece):
        return lax.all_gather(piece, SEQ_AXES, axis=0, tiled=True)

    def gather_chips(piece):
        stacked = jnp.broadcast_to(piece[None], (chip_count,) + piece.shape)
        half = lax.all_to_all(stacked, CHIP_AXES, 0, 0, tiled=True).reshape(
            chip_count * piece.shape[0], piece.shape[1]
        )
        return join_cores(half)

    block_index = jnp.arange(block_count, dtype=jnp.int32)
    half_blocks = block_count // 2
    core_of_block = jnp.where(block_index < half_blocks, core, 1 - core)
    within = block_index % half_blocks
    shard_of_block = ((within // tp_count) * 2 + core_of_block) * tp_count + within % tp_count

    def reorder(values, order):
        blocks = values.reshape(values.shape[:-1] + (block_count, block_rows))
        return jnp.take(blocks, order, axis=-2).reshape(values.shape)

    inverse_order = jnp.zeros_like(shard_order).at[shard_order].set(block_index)
    block_of_shard = jnp.zeros_like(shard_of_block).at[shard_of_block].set(block_index)

    gains = [reorder(norm_gains[i], shard_order) for i in range(layer_count)]
    token_count = variate_ids.shape[0]
    segment, offsets = prompt_layout(prompt_lengths[0], token_count)
    same_prompt = segment[:, None] == segment[None, :]
    same_variate = variate_ids[:, None] == variate_ids[None, :]
    head_count = variate_bias.shape[1]
    local_heads = head_count // tp_count
    head_size = head_cols // local_heads
    bias_table = lax.dynamic_slice_in_dim(
        variate_bias, lax.axis_index("tp") * local_heads, local_heads, 1
    )
    residual = reorder(residual_in, shard_order)
    for layer_index in range(layer_count):
        layer_bias = bias_table[layer_index]
        pair_bias = jnp.where(
            same_variate[None], layer_bias[:, 1][:, None, None], layer_bias[:, 0][:, None, None]
        )
        normed = rms_scaled(residual, gains[layer_index][0]).astype(jnp.bfloat16)
        if layer_index == 0:
            piece = regrouped[:, 0, :first_cols]
            qkv_weight = gather_chips(piece[:, : 3 * head_cols])
            normed = reorder(normed, shard_of_block)
            layer_weights = gather_seq(piece[:, 3 * head_cols :])
        else:
            layer_weights = gather_seq(regrouped[:, 0, first_cols:])
            qkv_weight = layer_weights[:, : 3 * head_cols]
            layer_weights = layer_weights[:, 3 * head_cols :]
        out_weight = layer_weights[:, :model_width]
        gate_up_weight = layer_weights[:, model_width : model_width + 2 * unit_cols]
        down_weight = layer_weights[:, model_width + 2 * unit_cols :]
        projected = project_rows(gather_tp(normed, tp_count), weight=qkv_weight)
        queries = rotate(
            projected[:, :head_cols].reshape(token_count, local_heads, head_size), offsets
        ).astype(jnp.bfloat16)
        key_rows = rotate(
            projected[:, head_cols : 2 * head_cols].reshape(token_count, local_heads, head_size),
            offsets,
        ).astype(jnp.bfloat16)
        values = (
            projected[:, 2 * head_cols : 3 * head_cols]
            .reshape(token_count, local_heads, head_size)
            .astype(jnp.bfloat16)
        )
        scores = (
            jnp.einsum("qhd,khd->hqk", queries, key_rows, preferred_element_type=jnp.float32)
            * head_size ** (-0.5)
            + pair_bias
        )
        scores = jnp.where(same_prompt[None], scores, NEGATIVE)
        row_peak = jnp.max(scores, axis=2, keepdims=True)
        weights_exp = jnp.exp(scores - row_peak)
        attn_weights = (weights_exp / jnp.sum(weights_exp, axis=2, keepdims=True)).astype(
            jnp.bfloat16
        )
        mixed_heads = (
            jnp.einsum("hqk,khd->qhd", attn_weights, values, preferred_element_type=jnp.float32)
            .astype(jnp.bfloat16)
            .reshape(token_count, head_cols)
        )
        head_total = project_owned(mixed_heads, out_weight, tp_count)
        residual = residual + head_total
        normed_mlp = rms_scaled(residual, gains[layer_index][1]).astype(jnp.bfloat16)
        if layer_index == 0:
            hidden = gated_units(gather_tp(normed_mlp, tp_count), weight=gate_up_weight)
            unit_total = reduce_tp(
                project_out(source=hidden, weight=down_weight).astype(jnp.bfloat16), tp_count
            )
        else:
            unit_total = core_pair_mlp(
                normed_mlp, pair_mlp, shard_of_block, block_of_shard, core_swap, tp_count
            )
        residual = residual + unit_total
    return reorder(residual, inverse_order)


def solution(mesh):
    seq_size = mesh.shape["seq"]
    chip_mesh = Mesh(
        mesh.devices.reshape((seq_size // 2, 2) + mesh.devices.shape[1:]),
        ("chip", "core", "tp"),
    )
    rows = SEQ_AXES + ("tp",)
    return jax.shard_map(
        on_device,
        mesh=chip_mesh,
        in_specs=(
            P(None, rows, None),
            P(),
            P(rows, None),
            P(),
            P(SEQ_AXES, None),
            P(SEQ_AXES),
            P(),
        ),
        out_specs=P(rows, None),
        check_vma=False,
    )
```

```python
import jax
import jax.numpy as jnp
from jax import lax
from jax.sharding import Mesh
from jax.sharding import PartitionSpec as P

NEGATIVE = -1e30
EPSILON = 1e-05
CHIP_AXES = "chip"
SEQ_AXES = ("chip", "core")


def rms_scaled(values, gain):
    mean_square = jnp.mean(values * values, axis=-1, keepdims=True)
    return values * lax.rsqrt(mean_square + EPSILON) * gain


def rotate(values, offsets):
    half_width = values.shape[-1] // 2
    frequency = 10000.0 ** (-jnp.arange(half_width, dtype=jnp.float32) / half_width)
    angles = offsets.astype(jnp.float32)[:, None] * frequency[None, :]
    cosine = jnp.cos(angles)[:, None, :]
    sine_part = jnp.sin(angles)[:, None, :]
    front_half = values[..., :half_width]
    back_half = values[..., half_width:]
    return jnp.concatenate(
        [front_half * cosine - back_half * sine_part, front_half * sine_part + back_half * cosine],
        axis=-1,
    )


def prompt_layout(lengths, token_count):
    prompt_ends = jnp.cumsum(lengths)
    prompt_starts = prompt_ends - lengths
    positions = jnp.arange(token_count, dtype=jnp.int32)
    segment = jnp.sum((positions[:, None] >= prompt_ends[None, :]).astype(jnp.int32), axis=1)
    member = segment[:, None] == jnp.arange(lengths.shape[0], dtype=jnp.int32)[None, :]
    offsets = positions - jnp.sum(jnp.where(member, prompt_starts[None, :], 0), axis=1)
    return (segment, offsets)


def project_rows(row_piece, weight):
    return jnp.dot(row_piece, weight, preferred_element_type=jnp.float32)


def gated_units(row_piece, weight):
    gate_up = jnp.dot(row_piece, weight, preferred_element_type=jnp.float32)
    half_width = weight.shape[1] // 2
    return (jax.nn.silu(gate_up[:, :half_width]) * gate_up[:, half_width:]).astype(jnp.bfloat16)


def project_out(source, weight):
    return lax.dot_general(
        source, weight, (((1,), (1,)), ((), ())), preferred_element_type=jnp.float32
    )


def gather_tp(values, tp_count):
    stacked = jnp.broadcast_to(values[None], (tp_count,) + values.shape)
    gathered = lax.all_to_all(stacked, "tp", 0, 0, tiled=True)
    return gathered.reshape((tp_count * values.shape[0],) + values.shape[1:])


def reduce_tp(products, tp_count):
    pieces = products.reshape((tp_count, products.shape[0] // tp_count) + products.shape[1:])
    received = lax.all_to_all(pieces, "tp", 0, 0, tiled=True)
    return jnp.sum(received.astype(jnp.float32), axis=0)


def project_owned(mixed_heads, out_weight, tp_count):
    own_rows = mixed_heads.shape[0] // tp_count
    pieces = mixed_heads.reshape(tp_count, own_rows, mixed_heads.shape[1])
    received = lax.all_to_all(pieces, "tp", 0, 0, tiled=True)
    group_weight = out_weight.reshape(out_weight.shape[0], tp_count, mixed_heads.shape[1])
    products = jnp.einsum(
        "gtc,rgc->gtr", received, group_weight, preferred_element_type=jnp.float32
    ).astype(jnp.bfloat16)
    return jnp.sum(products.astype(jnp.float32), axis=0)


def on_device(
    trainer_rows, shard_order, residual_in, norm_gains, prompt_lengths, variate_ids, variate_bias
):
    tp_count = lax.axis_size("tp")
    seq_count = lax.axis_size(SEQ_AXES)
    layer_count, block_rows, total_cols = trainer_rows.shape
    model_width = residual_in.shape[1]
    ff_width = (total_cols - 4 * model_width) // 3
    head_cols = model_width // tp_count
    unit_cols = ff_width // tp_count
    block_count = seq_count * tp_count
    part_widths = [model_width] * 4 + [ff_width] * 3

    rounded = trainer_rows.astype(jnp.bfloat16)
    grouped_parts = []
    column_start = 0
    for part_index, part_width in enumerate(part_widths):
        part = rounded[:, :, column_start : column_start + part_width]
        if part_index == 3:
            part = jnp.broadcast_to(part[:, :, None, :], (layer_count, block_rows, tp_count, part_width))
        else:
            part = part.reshape(layer_count, block_rows, tp_count, part_width // tp_count)
        grouped_parts.append(part)
        column_start = column_start + part_width
    grouped = jnp.concatenate(grouped_parts, axis=3)
    regrouped = lax.all_to_all(grouped, "tp", split_axis=2, concat_axis=1, tiled=True)
    chip_count = lax.axis_size(CHIP_AXES)
    core = lax.axis_index("core")
    core_swap = [(0, 1), (1, 0)]

    def join_cores(half):
        other = lax.ppermute(half, "core", core_swap)
        return jnp.concatenate([half, other], axis=0)

    def gather_seq(piece):
        return lax.all_gather(piece, SEQ_AXES, axis=0, tiled=True)

    def gather_chips(piece):
        stacked = jnp.broadcast_to(piece[None], (chip_count,) + piece.shape)
        half = lax.all_to_all(stacked, CHIP_AXES, 0, 0, tiled=True).reshape(
            chip_count * piece.shape[0], piece.shape[1]
        )
        return join_cores(half)

    block_index = jnp.arange(block_count, dtype=jnp.int32)
    half_blocks = block_count // 2
    core_of_block = jnp.where(block_index < half_blocks, core, 1 - core)
    within = block_index % half_blocks
    shard_of_block = ((within // tp_count) * 2 + core_of_block) * tp_count + within % tp_count

    def reorder(values, order):
        blocks = values.reshape(values.shape[:-1] + (block_count, block_rows))
        return jnp.take(blocks, order, axis=-2).reshape(values.shape)

    inverse_order = jnp.zeros_like(shard_order).at[shard_order].set(block_index)

    gains = [reorder(norm_gains[i], shard_order) for i in range(layer_count)]
    token_count = variate_ids.shape[0]
    segment, offsets = prompt_layout(prompt_lengths[0], token_count)
    half_count = token_count // 2
    lengths = prompt_lengths[0]
    long_start = (jnp.cumsum(lengths) - lengths)[jnp.argmax(lengths)]
    position = jnp.arange(token_count, dtype=jnp.int32)
    half_order = jnp.where(
        position < half_count,
        long_start + position,
        jnp.where(position - half_count < long_start, position - half_count, position),
    )
    token_place = jnp.where(
        (position >= long_start) & (position < long_start + half_count),
        position - long_start,
        jnp.where(position < long_start, position + half_count, position),
    )
    half_segment = jnp.take(segment, half_order).reshape(2, half_count)
    half_variate = jnp.take(variate_ids, half_order).reshape(2, half_count)
    same_prompt = half_segment[:, :, None] == half_segment[:, None, :]
    same_variate = half_variate[:, :, None] == half_variate[:, None, :]
    head_count = variate_bias.shape[1]
    local_heads = head_count // tp_count
    head_size = head_cols // local_heads
    bias_table = lax.dynamic_slice_in_dim(
        variate_bias, lax.axis_index("tp") * local_heads, local_heads, 1
    )
    residual = reorder(residual_in, shard_order)
    for layer_index in range(layer_count):
        layer_bias = bias_table[layer_index]
        pair_bias = jnp.where(
            same_variate[:, None],
            layer_bias[:, 1][None, :, None, None],
            layer_bias[:, 0][None, :, None, None],
        )
        normed = rms_scaled(residual, gains[layer_index][0]).astype(jnp.bfloat16)
        piece = regrouped[layer_index, :, 0, :]
        if layer_index == 0:
            qkv_weight = gather_chips(piece[:, : 3 * head_cols])
            normed = reorder(normed, shard_of_block)
            layer_weights = gather_seq(piece[:, 3 * head_cols :])
        else:
            layer_weights = gather_seq(piece)
            qkv_weight = layer_weights[:, : 3 * head_cols]
            layer_weights = layer_weights[:, 3 * head_cols :]
        out_weight = layer_weights[:, :model_width]
        gate_up_weight = layer_weights[:, model_width : model_width + 2 * unit_cols]
        down_weight = layer_weights[:, model_width + 2 * unit_cols :]
        projected = project_rows(gather_tp(normed, tp_count), weight=qkv_weight)
        queries = rotate(
            projected[:, :head_cols].reshape(token_count, local_heads, head_size), offsets
        ).astype(jnp.bfloat16)
        key_rows = rotate(
            projected[:, head_cols : 2 * head_cols].reshape(token_count, local_heads, head_size),
            offsets,
        ).astype(jnp.bfloat16)
        values = (
            projected[:, 2 * head_cols : 3 * head_cols]
            .reshape(token_count, local_heads, head_size)
            .astype(jnp.bfloat16)
        )
        def halves(rows):
            return jnp.take(rows, half_order, axis=0).reshape(
                (2, half_count) + rows.shape[1:]
            )

        scores = (
            jnp.einsum(
                "bqhd,bkhd->bhqk",
                halves(queries),
                halves(key_rows),
                preferred_element_type=jnp.float32,
            )
            * head_size ** (-0.5)
            + pair_bias
        )
        scores = jnp.where(same_prompt[:, None], scores, NEGATIVE)
        row_peak = jnp.max(scores, axis=3, keepdims=True)
        weights_exp = jnp.exp(scores - row_peak)
        attn_weights = (weights_exp / jnp.sum(weights_exp, axis=3, keepdims=True)).astype(
            jnp.bfloat16
        )
        mixed_halves = jnp.einsum(
            "bhqk,bkhd->bqhd", attn_weights, halves(values), preferred_element_type=jnp.float32
        ).astype(jnp.bfloat16)
        mixed_heads = jnp.take(
            mixed_halves.reshape(token_count, local_heads, head_size), token_place, axis=0
        ).reshape(token_count, head_cols)
        head_total = project_owned(mixed_heads, out_weight, tp_count)
        residual = residual + head_total
        normed_mlp = rms_scaled(residual, gains[layer_index][1]).astype(jnp.bfloat16)
        hidden = gated_units(gather_tp(normed_mlp, tp_count), weight=gate_up_weight)
        unit_total = reduce_tp(
            project_out(source=hidden, weight=down_weight).astype(jnp.bfloat16), tp_count
        )
        residual = residual + unit_total
    return reorder(residual, inverse_order)


def solution(mesh):
    seq_size = mesh.shape["seq"]
    chip_mesh = Mesh(
        mesh.devices.reshape((seq_size // 2, 2) + mesh.devices.shape[1:]),
        ("chip", "core", "tp"),
    )
    rows = SEQ_AXES + ("tp",)
    return jax.shard_map(
        on_device,
        mesh=chip_mesh,
        in_specs=(
            P(None, rows, None),
            P(),
            P(rows, None),
            P(),
            P(SEQ_AXES, None),
            P(SEQ_AXES),
            P(),
        ),
        out_specs=P(rows, None),
        check_vma=False,
    )
```

```python
import jax
import jax.numpy as jnp
from jax import lax
from jax.sharding import Mesh
from jax.sharding import PartitionSpec as P

NEGATIVE = -1e30
EPSILON = 1e-05
CHIP_AXES = "chip"
SEQ_AXES = ("chip", "core")


def rms_scaled(values, gain):
    mean_square = jnp.mean(values * values, axis=-1, keepdims=True)
    return values * lax.rsqrt(mean_square + EPSILON) * gain


def rotate(values, offsets):
    half_width = values.shape[-1] // 2
    frequency = 10000.0 ** (-jnp.arange(half_width, dtype=jnp.float32) / half_width)
    angles = offsets.astype(jnp.float32)[:, None] * frequency[None, :]
    cosine = jnp.cos(angles)[:, None, :]
    sine_part = jnp.sin(angles)[:, None, :]
    front_half = values[..., :half_width]
    back_half = values[..., half_width:]
    return jnp.concatenate(
        [front_half * cosine - back_half * sine_part, front_half * sine_part + back_half * cosine],
        axis=-1,
    )


def prompt_layout(lengths, token_count):
    prompt_ends = jnp.cumsum(lengths)
    prompt_starts = prompt_ends - lengths
    positions = jnp.arange(token_count, dtype=jnp.int32)
    segment = jnp.sum((positions[:, None] >= prompt_ends[None, :]).astype(jnp.int32), axis=1)
    member = segment[:, None] == jnp.arange(lengths.shape[0], dtype=jnp.int32)[None, :]
    offsets = positions - jnp.sum(jnp.where(member, prompt_starts[None, :], 0), axis=1)
    return (segment, offsets)


def project_rows(row_piece, weight):
    return jnp.dot(row_piece, weight, preferred_element_type=jnp.float32)


def gated_units(row_piece, weight):
    gate_up = jnp.dot(row_piece, weight, preferred_element_type=jnp.float32)
    half_width = weight.shape[1] // 2
    return (jax.nn.silu(gate_up[:, :half_width]) * gate_up[:, half_width:]).astype(jnp.bfloat16)


def project_out(source, weight):
    return lax.dot_general(
        source, weight, (((1,), (1,)), ((), ())), preferred_element_type=jnp.float32
    )


def gather_tp(values, tp_count):
    stacked = jnp.broadcast_to(values[None], (tp_count,) + values.shape)
    gathered = lax.all_to_all(stacked, "tp", 0, 0, tiled=True)
    return gathered.reshape((tp_count * values.shape[0],) + values.shape[1:])


def reduce_tp(products, tp_count):
    pieces = products.reshape((tp_count, products.shape[0] // tp_count) + products.shape[1:])
    received = lax.all_to_all(pieces, "tp", 0, 0, tiled=True)
    return jnp.sum(received.astype(jnp.float32), axis=0)


def project_owned(mixed_heads, out_weight, tp_count):
    own_rows = mixed_heads.shape[0] // tp_count
    pieces = mixed_heads.reshape(tp_count, own_rows, mixed_heads.shape[1])
    received = lax.all_to_all(pieces, "tp", 0, 0, tiled=True)
    group_weight = out_weight.reshape(out_weight.shape[0], tp_count, mixed_heads.shape[1])
    products = jnp.einsum(
        "gtc,rgc->gtr", received, group_weight, preferred_element_type=jnp.float32
    ).astype(jnp.bfloat16)
    return jnp.sum(products.astype(jnp.float32), axis=0)


def rotate_rows(rows, shift):
    doubled = jnp.concatenate([rows, rows], axis=0)
    return lax.dynamic_slice_in_dim(doubled, shift, rows.shape[0], axis=0)


def on_device(
    trainer_rows, shard_order, residual_in, norm_gains, prompt_lengths, variate_ids, variate_bias
):
    tp_count = lax.axis_size("tp")
    seq_count = lax.axis_size(SEQ_AXES)
    layer_count, block_rows, total_cols = trainer_rows.shape
    model_width = residual_in.shape[1]
    ff_width = (total_cols - 4 * model_width) // 3
    head_cols = model_width // tp_count
    unit_cols = ff_width // tp_count
    block_count = seq_count * tp_count
    part_widths = [model_width] * 4 + [ff_width] * 3

    rounded = trainer_rows.astype(jnp.bfloat16)
    grouped_parts = []
    column_start = 0
    for part_index, part_width in enumerate(part_widths):
        part = rounded[:, :, column_start : column_start + part_width]
        if part_index == 3:
            part = jnp.broadcast_to(part[:, :, None, :], (layer_count, block_rows, tp_count, part_width))
        else:
            part = part.reshape(layer_count, block_rows, tp_count, part_width // tp_count)
        grouped_parts.append(part)
        column_start = column_start + part_width
    grouped = jnp.concatenate(grouped_parts, axis=3)
    regrouped = lax.all_to_all(grouped, "tp", split_axis=2, concat_axis=1, tiled=True)
    chip_count = lax.axis_size(CHIP_AXES)
    core = lax.axis_index("core")
    core_swap = [(0, 1), (1, 0)]

    def join_cores(half):
        other = lax.ppermute(half, "core", core_swap)
        return jnp.concatenate([half, other], axis=0)

    def gather_seq(piece):
        return lax.all_gather(piece, SEQ_AXES, axis=0, tiled=True)

    def gather_chips(piece):
        stacked = jnp.broadcast_to(piece[None], (chip_count,) + piece.shape)
        half = lax.all_to_all(stacked, CHIP_AXES, 0, 0, tiled=True).reshape(
            chip_count * piece.shape[0], piece.shape[1]
        )
        return join_cores(half)

    block_index = jnp.arange(block_count, dtype=jnp.int32)
    half_blocks = block_count // 2
    core_of_block = jnp.where(block_index < half_blocks, core, 1 - core)
    within = block_index % half_blocks
    shard_of_block = ((within // tp_count) * 2 + core_of_block) * tp_count + within % tp_count

    def reorder(values, order):
        blocks = values.reshape(values.shape[:-1] + (block_count, block_rows))
        return jnp.take(blocks, order, axis=-2).reshape(values.shape)

    inverse_order = jnp.zeros_like(shard_order).at[shard_order].set(block_index)

    gains = [reorder(norm_gains[i], shard_order) for i in range(layer_count)]
    token_count = variate_ids.shape[0]
    segment, offsets = prompt_layout(prompt_lengths[0], token_count)
    half_count = token_count // 2
    lengths = prompt_lengths[0]
    long_start = (jnp.cumsum(lengths) - lengths)[jnp.argmax(lengths)]
    half_segment = rotate_rows(segment, long_start).reshape(2, half_count)
    half_variate = rotate_rows(variate_ids, long_start).reshape(2, half_count)
    same_prompt = half_segment[:, :, None] == half_segment[:, None, :]
    same_variate = half_variate[:, :, None] == half_variate[:, None, :]
    head_count = variate_bias.shape[1]
    local_heads = head_count // tp_count
    head_size = head_cols // local_heads
    bias_table = lax.dynamic_slice_in_dim(
        variate_bias, lax.axis_index("tp") * local_heads, local_heads, 1
    )
    residual = reorder(residual_in, shard_order)
    for layer_index in range(layer_count):
        layer_bias = bias_table[layer_index]
        pair_bias = jnp.where(
            same_variate[:, None],
            layer_bias[:, 1][None, :, None, None],
            layer_bias[:, 0][None, :, None, None],
        )
        normed = rms_scaled(residual, gains[layer_index][0]).astype(jnp.bfloat16)
        piece = regrouped[layer_index, :, 0, :]
        if layer_index == 0:
            qkv_weight = gather_chips(piece[:, : 3 * head_cols])
            normed = reorder(normed, shard_of_block)
            layer_weights = gather_seq(piece[:, 3 * head_cols :])
        else:
            layer_weights = gather_seq(piece)
            qkv_weight = layer_weights[:, : 3 * head_cols]
            layer_weights = layer_weights[:, 3 * head_cols :]
        out_weight = layer_weights[:, :model_width]
        gate_up_weight = layer_weights[:, model_width : model_width + 2 * unit_cols]
        down_weight = layer_weights[:, model_width + 2 * unit_cols :]
        projected = project_rows(gather_tp(normed, tp_count), weight=qkv_weight)
        queries = rotate(
            projected[:, :head_cols].reshape(token_count, local_heads, head_size), offsets
        ).astype(jnp.bfloat16)
        key_rows = rotate(
            projected[:, head_cols : 2 * head_cols].reshape(token_count, local_heads, head_size),
            offsets,
        ).astype(jnp.bfloat16)
        values = (
            projected[:, 2 * head_cols : 3 * head_cols]
            .reshape(token_count, local_heads, head_size)
            .astype(jnp.bfloat16)
        )
        def halves(rows):
            return rotate_rows(rows, long_start).reshape((2, half_count) + rows.shape[1:])

        scores = (
            jnp.einsum(
                "bqhd,bkhd->bhqk",
                halves(queries),
                halves(key_rows),
                preferred_element_type=jnp.float32,
            )
            * head_size ** (-0.5)
            + pair_bias
        )
        scores = jnp.where(same_prompt[:, None], scores, NEGATIVE)
        row_peak = jnp.max(scores, axis=3, keepdims=True)
        weights_exp = jnp.exp(scores - row_peak)
        attn_weights = (weights_exp / jnp.sum(weights_exp, axis=3, keepdims=True)).astype(
            jnp.bfloat16
        )
        mixed_halves = jnp.einsum(
            "bhqk,bkhd->bqhd", attn_weights, halves(values), preferred_element_type=jnp.float32
        ).astype(jnp.bfloat16)
        mixed_heads = rotate_rows(
            mixed_halves.reshape(token_count, local_heads, head_size),
            (token_count - long_start) % token_count,
        ).reshape(token_count, head_cols)
        head_total = project_owned(mixed_heads, out_weight, tp_count)
        residual = residual + head_total
        normed_mlp = rms_scaled(residual, gains[layer_index][1]).astype(jnp.bfloat16)
        hidden = gated_units(gather_tp(normed_mlp, tp_count), weight=gate_up_weight)
        unit_total = reduce_tp(
            project_out(source=hidden, weight=down_weight).astype(jnp.bfloat16), tp_count
        )
        residual = residual + unit_total
    return reorder(residual, inverse_order)


def solution(mesh):
    seq_size = mesh.shape["seq"]
    chip_mesh = Mesh(
        mesh.devices.reshape((seq_size // 2, 2) + mesh.devices.shape[1:]),
        ("chip", "core", "tp"),
    )
    rows = SEQ_AXES + ("tp",)
    return jax.shard_map(
        on_device,
        mesh=chip_mesh,
        in_specs=(
            P(None, rows, None),
            P(),
            P(rows, None),
            P(),
            P(SEQ_AXES, None),
            P(SEQ_AXES),
            P(),
        ),
        out_specs=P(rows, None),
        check_vma=False,
    )
```

```python
import jax
import jax.numpy as jnp
from jax import lax
from jax.sharding import Mesh
from jax.sharding import PartitionSpec as P

NEGATIVE = -1e30
EPSILON = 1e-05
CHIP_AXES = "chip"
SEQ_AXES = ("chip", "core")


def rms_scaled(values, gain):
    mean_square = jnp.mean(values * values, axis=-1, keepdims=True)
    return values * lax.rsqrt(mean_square + EPSILON) * gain


def rotate(values, offsets):
    half_width = values.shape[-1] // 2
    frequency = 10000.0 ** (-jnp.arange(half_width, dtype=jnp.float32) / half_width)
    angles = offsets.astype(jnp.float32)[:, None] * frequency[None, :]
    cosine = jnp.cos(angles)[:, None, :]
    sine_part = jnp.sin(angles)[:, None, :]
    front_half = values[..., :half_width]
    back_half = values[..., half_width:]
    return jnp.concatenate(
        [front_half * cosine - back_half * sine_part, front_half * sine_part + back_half * cosine],
        axis=-1,
    )


def prompt_layout(lengths, token_count):
    prompt_ends = jnp.cumsum(lengths)
    prompt_starts = prompt_ends - lengths
    positions = jnp.arange(token_count, dtype=jnp.int32)
    segment = jnp.sum((positions[:, None] >= prompt_ends[None, :]).astype(jnp.int32), axis=1)
    member = segment[:, None] == jnp.arange(lengths.shape[0], dtype=jnp.int32)[None, :]
    offsets = positions - jnp.sum(jnp.where(member, prompt_starts[None, :], 0), axis=1)
    return (segment, offsets)


def project_rows(row_piece, weight):
    return jnp.dot(row_piece, weight, preferred_element_type=jnp.float32)


def gated_units(row_piece, weight):
    gate_up = jnp.dot(row_piece, weight, preferred_element_type=jnp.float32)
    half_width = weight.shape[1] // 2
    return (jax.nn.silu(gate_up[:, :half_width]) * gate_up[:, half_width:]).astype(jnp.bfloat16)


def project_out(source, weight):
    return lax.dot_general(
        source, weight, (((1,), (1,)), ((), ())), preferred_element_type=jnp.float32
    )


def gather_tp(values, tp_count):
    stacked = jnp.broadcast_to(values[None], (tp_count,) + values.shape)
    gathered = lax.all_to_all(stacked, "tp", 0, 0, tiled=True)
    return gathered.reshape((tp_count * values.shape[0],) + values.shape[1:])


def reduce_tp(products, tp_count):
    pieces = products.reshape((tp_count, products.shape[0] // tp_count) + products.shape[1:])
    received = lax.all_to_all(pieces, "tp", 0, 0, tiled=True)
    return jnp.sum(received.astype(jnp.float32), axis=0)


def project_owned(mixed_heads, out_weight, tp_count):
    own_rows = mixed_heads.shape[0] // tp_count
    pieces = mixed_heads.reshape(tp_count, own_rows, mixed_heads.shape[1])
    received = lax.all_to_all(pieces, "tp", 0, 0, tiled=True)
    group_weight = out_weight.reshape(out_weight.shape[0], tp_count, mixed_heads.shape[1])
    products = jnp.einsum(
        "gtc,rgc->gtr", received, group_weight, preferred_element_type=jnp.float32
    ).astype(jnp.bfloat16)
    return jnp.sum(products.astype(jnp.float32), axis=0)


def rotate_rows(rows, shift):
    doubled = jnp.concatenate([rows, rows], axis=0)
    return lax.dynamic_slice_in_dim(doubled, shift, rows.shape[0], axis=0)


def on_device(
    trainer_rows, shard_order, residual_in, norm_gains, prompt_lengths, variate_ids, variate_bias
):
    tp_count = lax.axis_size("tp")
    seq_count = lax.axis_size(SEQ_AXES)
    layer_count, block_rows, total_cols = trainer_rows.shape
    model_width = residual_in.shape[1]
    ff_width = (total_cols - 4 * model_width) // 3
    head_cols = model_width // tp_count
    unit_cols = ff_width // tp_count
    block_count = seq_count * tp_count
    part_widths = [model_width] * 4 + [ff_width] * 3

    rounded = trainer_rows.astype(jnp.bfloat16)
    grouped_parts = []
    column_start = 0
    for part_index, part_width in enumerate(part_widths):
        part = rounded[:, :, column_start : column_start + part_width]
        if part_index == 3:
            part = jnp.broadcast_to(part[:, :, None, :], (layer_count, block_rows, tp_count, part_width))
        else:
            part = part.reshape(layer_count, block_rows, tp_count, part_width // tp_count)
        grouped_parts.append(part)
        column_start = column_start + part_width
    grouped = jnp.concatenate(grouped_parts, axis=3)
    regrouped = lax.all_to_all(grouped, "tp", split_axis=2, concat_axis=1, tiled=True)
    chip_count = lax.axis_size(CHIP_AXES)
    core = lax.axis_index("core")
    core_swap = [(0, 1), (1, 0)]

    def join_cores(half):
        other = lax.ppermute(half, "core", core_swap)
        return jnp.concatenate([half, other], axis=0)

    def gather_seq(piece):
        return lax.all_gather(piece, SEQ_AXES, axis=0, tiled=True)

    def gather_chips(piece):
        stacked = jnp.broadcast_to(piece[None], (chip_count,) + piece.shape)
        half = lax.all_to_all(stacked, CHIP_AXES, 0, 0, tiled=True).reshape(
            chip_count * piece.shape[0], piece.shape[1]
        )
        return join_cores(half)

    block_index = jnp.arange(block_count, dtype=jnp.int32)
    half_blocks = block_count // 2
    core_of_block = jnp.where(block_index < half_blocks, core, 1 - core)
    within = block_index % half_blocks
    shard_of_block = ((within // tp_count) * 2 + core_of_block) * tp_count + within % tp_count

    def reorder(values, order):
        blocks = values.reshape(values.shape[:-1] + (block_count, block_rows))
        return jnp.take(blocks, order, axis=-2).reshape(values.shape)

    inverse_order = jnp.zeros_like(shard_order).at[shard_order[shard_of_block]].set(block_index)

    gains = [reorder(norm_gains[i], shard_order) for i in range(layer_count)]
    chip_order = shard_order[shard_of_block]
    chip_gains = [reorder(norm_gains[i], chip_order) for i in range(layer_count)]
    token_count = variate_ids.shape[0]
    segment, offsets = prompt_layout(prompt_lengths[0], token_count)
    half_count = token_count // 2
    lengths = prompt_lengths[0]
    long_start = (jnp.cumsum(lengths) - lengths)[jnp.argmax(lengths)]
    half_segment = rotate_rows(segment, long_start).reshape(2, half_count)
    half_variate = rotate_rows(variate_ids, long_start).reshape(2, half_count)
    same_prompt = half_segment[:, :, None] == half_segment[:, None, :]
    same_variate = half_variate[:, :, None] == half_variate[:, None, :]
    head_count = variate_bias.shape[1]
    local_heads = head_count // tp_count
    head_size = head_cols // local_heads
    bias_table = lax.dynamic_slice_in_dim(
        variate_bias, lax.axis_index("tp") * local_heads, local_heads, 1
    )
    residual = reorder(residual_in, shard_order)
    for layer_index in range(layer_count):
        layer_bias = bias_table[layer_index]
        pair_bias = jnp.where(
            same_variate[:, None],
            layer_bias[:, 1][None, :, None, None],
            layer_bias[:, 0][None, :, None, None],
        )
        normed = rms_scaled(residual, gains[layer_index][0]).astype(jnp.bfloat16)
        piece = regrouped[layer_index, :, 0, :]
        if layer_index == 0:
            qkv_weight = gather_chips(piece[:, : 3 * head_cols])
            normed = reorder(normed, shard_of_block)
            layer_weights = gather_seq(piece[:, 3 * head_cols :])
        else:
            residual = reorder(residual, shard_of_block)
            normed = rms_scaled(residual, chip_gains[layer_index][0]).astype(jnp.bfloat16)
            layer_weights = join_cores(lax.all_gather(piece, CHIP_AXES, axis=0, tiled=True))
            qkv_weight = layer_weights[:, : 3 * head_cols]
            layer_weights = layer_weights[:, 3 * head_cols :]
        out_weight = layer_weights[:, :model_width]
        gate_up_weight = layer_weights[:, model_width : model_width + 2 * unit_cols]
        down_weight = layer_weights[:, model_width + 2 * unit_cols :]
        projected = project_rows(gather_tp(normed, tp_count), weight=qkv_weight)
        queries = rotate(
            projected[:, :head_cols].reshape(token_count, local_heads, head_size), offsets
        ).astype(jnp.bfloat16)
        key_rows = rotate(
            projected[:, head_cols : 2 * head_cols].reshape(token_count, local_heads, head_size),
            offsets,
        ).astype(jnp.bfloat16)
        values = (
            projected[:, 2 * head_cols : 3 * head_cols]
            .reshape(token_count, local_heads, head_size)
            .astype(jnp.bfloat16)
        )
        def halves(rows):
            return rotate_rows(rows, long_start).reshape((2, half_count) + rows.shape[1:])

        scores = (
            jnp.einsum(
                "bqhd,bkhd->bhqk",
                halves(queries),
                halves(key_rows),
                preferred_element_type=jnp.float32,
            )
            * head_size ** (-0.5)
            + pair_bias
        )
        scores = jnp.where(same_prompt[:, None], scores, NEGATIVE)
        row_peak = jnp.max(scores, axis=3, keepdims=True)
        weights_exp = jnp.exp(scores - row_peak)
        attn_weights = (weights_exp / jnp.sum(weights_exp, axis=3, keepdims=True)).astype(
            jnp.bfloat16
        )
        mixed_halves = jnp.einsum(
            "bhqk,bkhd->bqhd", attn_weights, halves(values), preferred_element_type=jnp.float32
        ).astype(jnp.bfloat16)
        mixed_heads = rotate_rows(
            mixed_halves.reshape(token_count, local_heads, head_size),
            (token_count - long_start) % token_count,
        ).reshape(token_count, head_cols)
        head_total = project_owned(mixed_heads, out_weight, tp_count)
        residual = residual + head_total
        mlp_gain = gains[layer_index][1] if layer_index == 0 else chip_gains[layer_index][1]
        normed_mlp = rms_scaled(residual, mlp_gain).astype(jnp.bfloat16)
        hidden = gated_units(gather_tp(normed_mlp, tp_count), weight=gate_up_weight)
        unit_total = reduce_tp(
            project_out(source=hidden, weight=down_weight).astype(jnp.bfloat16), tp_count
        )
        residual = residual + unit_total
    return reorder(residual, inverse_order)


def solution(mesh):
    seq_size = mesh.shape["seq"]
    chip_mesh = Mesh(
        mesh.devices.reshape((seq_size // 2, 2) + mesh.devices.shape[1:]),
        ("chip", "core", "tp"),
    )
    rows = SEQ_AXES + ("tp",)
    return jax.shard_map(
        on_device,
        mesh=chip_mesh,
        in_specs=(
            P(None, rows, None),
            P(),
            P(rows, None),
            P(),
            P(SEQ_AXES, None),
            P(SEQ_AXES),
            P(),
        ),
        out_specs=P(rows, None),
        check_vma=False,
    )
```

```python
import jax
import jax.numpy as jnp
from jax import lax
from jax.sharding import Mesh
from jax.sharding import PartitionSpec as P

NEGATIVE = -1e30
EPSILON = 1e-05
CHIP_AXES = "chip"
SEQ_AXES = ("chip", "core")


def rms_scaled(values, gain):
    mean_square = jnp.mean(values * values, axis=-1, keepdims=True)
    return values * lax.rsqrt(mean_square + EPSILON) * gain


def rotate(values, offsets):
    half_width = values.shape[-1] // 2
    frequency = 10000.0 ** (-jnp.arange(half_width, dtype=jnp.float32) / half_width)
    angles = offsets.astype(jnp.float32)[:, None] * frequency[None, :]
    cosine = jnp.cos(angles)[:, None, :]
    sine_part = jnp.sin(angles)[:, None, :]
    front_half = values[..., :half_width]
    back_half = values[..., half_width:]
    return jnp.concatenate(
        [front_half * cosine - back_half * sine_part, front_half * sine_part + back_half * cosine],
        axis=-1,
    )


def prompt_layout(lengths, token_count):
    prompt_ends = jnp.cumsum(lengths)
    prompt_starts = prompt_ends - lengths
    positions = jnp.arange(token_count, dtype=jnp.int32)
    segment = jnp.sum((positions[:, None] >= prompt_ends[None, :]).astype(jnp.int32), axis=1)
    member = segment[:, None] == jnp.arange(lengths.shape[0], dtype=jnp.int32)[None, :]
    offsets = positions - jnp.sum(jnp.where(member, prompt_starts[None, :], 0), axis=1)
    return (segment, offsets)


def project_rows(row_piece, weight):
    return jnp.dot(row_piece, weight, preferred_element_type=jnp.float32)


def gated_units(row_piece, weight):
    gate_up = jnp.dot(row_piece, weight, preferred_element_type=jnp.float32)
    half_width = weight.shape[1] // 2
    return (jax.nn.silu(gate_up[:, :half_width]) * gate_up[:, half_width:]).astype(jnp.bfloat16)


def project_out(source, weight):
    return lax.dot_general(
        source, weight, (((1,), (1,)), ((), ())), preferred_element_type=jnp.float32
    )


def gather_tp(values, tp_count):
    stacked = jnp.broadcast_to(values[None], (tp_count,) + values.shape)
    gathered = lax.all_to_all(stacked, "tp", 0, 0, tiled=True)
    return gathered.reshape((tp_count * values.shape[0],) + values.shape[1:])


def reduce_tp(products, tp_count):
    pieces = products.reshape((tp_count, products.shape[0] // tp_count) + products.shape[1:])
    received = lax.all_to_all(pieces, "tp", 0, 0, tiled=True)
    return jnp.sum(received.astype(jnp.float32), axis=0)


def project_owned(mixed_heads, out_weight, tp_count):
    own_rows = mixed_heads.shape[0] // tp_count
    pieces = mixed_heads.reshape(tp_count, own_rows, mixed_heads.shape[1])
    received = lax.all_to_all(pieces, "tp", 0, 0, tiled=True)
    group_weight = out_weight.reshape(out_weight.shape[0], tp_count, mixed_heads.shape[1])
    products = jnp.einsum(
        "gtc,rgc->gtr", received, group_weight, preferred_element_type=jnp.float32
    ).astype(jnp.bfloat16)
    return jnp.sum(products.astype(jnp.float32), axis=0)


def rotate_rows(rows, shift):
    doubled = jnp.concatenate([rows, rows], axis=0)
    return lax.dynamic_slice_in_dim(doubled, shift, rows.shape[0], axis=0)


def on_device(
    trainer_rows, shard_order, residual_in, norm_gains, prompt_lengths, variate_ids, variate_bias
):
    tp_count = lax.axis_size("tp")
    seq_count = lax.axis_size(SEQ_AXES)
    layer_count, block_rows, total_cols = trainer_rows.shape
    model_width = residual_in.shape[1]
    ff_width = (total_cols - 4 * model_width) // 3
    head_cols = model_width // tp_count
    unit_cols = ff_width // tp_count
    block_count = seq_count * tp_count
    part_widths = [model_width] * 4 + [ff_width] * 3

    rounded = trainer_rows.astype(jnp.bfloat16)
    grouped_parts = []
    column_start = 0
    for part_index, part_width in enumerate(part_widths):
        part = rounded[:, :, column_start : column_start + part_width]
        if part_index == 3:
            part = jnp.broadcast_to(part[:, :, None, :], (layer_count, block_rows, tp_count, part_width))
        else:
            part = part.reshape(layer_count, block_rows, tp_count, part_width // tp_count)
        grouped_parts.append(part)
        column_start = column_start + part_width
    grouped = jnp.concatenate(grouped_parts, axis=3)
    regrouped = lax.all_to_all(grouped, "tp", split_axis=2, concat_axis=1, tiled=True)
    chip_count = lax.axis_size(CHIP_AXES)
    core = lax.axis_index("core")
    core_swap = [(0, 1), (1, 0)]

    def join_cores(half):
        other = lax.ppermute(half, "core", core_swap)
        return jnp.concatenate([half, other], axis=0)

    def gather_seq(piece):
        return lax.all_gather(piece, SEQ_AXES, axis=0, tiled=True)

    def gather_chips(piece):
        stacked = jnp.broadcast_to(piece[None], (chip_count,) + piece.shape)
        half = lax.all_to_all(stacked, CHIP_AXES, 0, 0, tiled=True).reshape(
            chip_count * piece.shape[0], piece.shape[1]
        )
        return join_cores(half)

    block_index = jnp.arange(block_count, dtype=jnp.int32)
    half_blocks = block_count // 2
    core_of_block = jnp.where(block_index < half_blocks, core, 1 - core)
    within = block_index % half_blocks
    shard_of_block = ((within // tp_count) * 2 + core_of_block) * tp_count + within % tp_count

    def reorder(values, order):
        blocks = values.reshape(values.shape[:-1] + (block_count, block_rows))
        return jnp.take(blocks, order, axis=-2).reshape(values.shape)

    inverse_order = jnp.zeros_like(shard_order).at[shard_order].set(block_index)

    gains = [reorder(norm_gains[i], shard_order) for i in range(layer_count)]
    token_count = variate_ids.shape[0]
    segment, offsets = prompt_layout(prompt_lengths[0], token_count)
    half_count = token_count // 2
    lengths = prompt_lengths[0]
    long_start = (jnp.cumsum(lengths) - lengths)[jnp.argmax(lengths)]
    half_segment = rotate_rows(segment, long_start).reshape(2, half_count)
    half_variate = rotate_rows(variate_ids, long_start).reshape(2, half_count)
    same_prompt = half_segment[:, :, None] == half_segment[:, None, :]
    same_variate = half_variate[:, :, None] == half_variate[:, None, :]
    head_count = variate_bias.shape[1]
    local_heads = head_count // tp_count
    head_size = head_cols // local_heads
    bias_table = lax.dynamic_slice_in_dim(
        variate_bias, lax.axis_index("tp") * local_heads, local_heads, 1
    )
    residual = reorder(residual_in, shard_order)
    for layer_index in range(layer_count):
        layer_bias = bias_table[layer_index]
        pair_bias = jnp.where(
            same_variate[:, None],
            layer_bias[:, 1][None, :, None, None],
            layer_bias[:, 0][None, :, None, None],
        )
        normed = rms_scaled(residual, gains[layer_index][0]).astype(jnp.bfloat16)
        piece = regrouped[layer_index, :, 0, :]
        if layer_index == 0:
            qkv_weight = gather_chips(piece[:, : 3 * head_cols])
            normed = reorder(normed, shard_of_block)
            layer_weights = gather_seq(piece[:, 3 * head_cols :])
        else:
            layer_weights = next_weights
            qkv_weight = layer_weights[:, : 3 * head_cols]
            layer_weights = layer_weights[:, 3 * head_cols :]
        out_weight = layer_weights[:, :model_width]
        gate_up_weight = layer_weights[:, model_width : model_width + 2 * unit_cols]
        down_weight = layer_weights[:, model_width + 2 * unit_cols :]
        projected = project_rows(gather_tp(normed, tp_count), weight=qkv_weight)
        queries = rotate(
            projected[:, :head_cols].reshape(token_count, local_heads, head_size), offsets
        ).astype(jnp.bfloat16)
        key_rows = rotate(
            projected[:, head_cols : 2 * head_cols].reshape(token_count, local_heads, head_size),
            offsets,
        ).astype(jnp.bfloat16)
        values = (
            projected[:, 2 * head_cols : 3 * head_cols]
            .reshape(token_count, local_heads, head_size)
            .astype(jnp.bfloat16)
        )
        def halves(rows):
            return rotate_rows(rows, long_start).reshape((2, half_count) + rows.shape[1:])

        scores = (
            jnp.einsum(
                "bqhd,bkhd->bhqk",
                halves(queries),
                halves(key_rows),
                preferred_element_type=jnp.float32,
            )
            * head_size ** (-0.5)
            + pair_bias
        )
        scores = jnp.where(same_prompt[:, None], scores, NEGATIVE)
        row_peak = jnp.max(scores, axis=3, keepdims=True)
        weights_exp = jnp.exp(scores - row_peak)
        attn_weights = (weights_exp / jnp.sum(weights_exp, axis=3, keepdims=True)).astype(
            jnp.bfloat16
        )
        mixed_halves = jnp.einsum(
            "bhqk,bkhd->bqhd", attn_weights, halves(values), preferred_element_type=jnp.float32
        ).astype(jnp.bfloat16)
        mixed_heads = rotate_rows(
            mixed_halves.reshape(token_count, local_heads, head_size),
            (token_count - long_start) % token_count,
        ).reshape(token_count, head_cols)
        head_total = project_owned(mixed_heads, out_weight, tp_count)
        residual = residual + head_total
        normed_mlp = rms_scaled(residual, gains[layer_index][1]).astype(jnp.bfloat16)
        mlp_tokens = gather_tp(normed_mlp, tp_count)
        if layer_index + 1 < layer_count:
            next_piece, mlp_tokens = lax.optimization_barrier(
                (regrouped[layer_index + 1, :, 0, :], mlp_tokens)
            )
            next_weights = gather_seq(next_piece)
        hidden = gated_units(mlp_tokens, weight=gate_up_weight)
        unit_total = reduce_tp(
            project_out(source=hidden, weight=down_weight).astype(jnp.bfloat16), tp_count
        )
        residual = residual + unit_total
    return reorder(residual, inverse_order)


def solution(mesh):
    seq_size = mesh.shape["seq"]
    chip_mesh = Mesh(
        mesh.devices.reshape((seq_size // 2, 2) + mesh.devices.shape[1:]),
        ("chip", "core", "tp"),
    )
    rows = SEQ_AXES + ("tp",)
    return jax.shard_map(
        on_device,
        mesh=chip_mesh,
        in_specs=(
            P(None, rows, None),
            P(),
            P(rows, None),
            P(),
            P(SEQ_AXES, None),
            P(SEQ_AXES),
            P(),
        ),
        out_specs=P(rows, None),
        check_vma=False,
    )
```

```python
import jax
import jax.numpy as jnp
from jax import lax
from jax.sharding import Mesh
from jax.sharding import PartitionSpec as P

NEGATIVE = -1e30
EPSILON = 1e-05
CHIP_AXES = "chip"
SEQ_AXES = ("chip", "core")


def rms_scaled(values, gain):
    mean_square = jnp.mean(values * values, axis=-1, keepdims=True)
    return values * lax.rsqrt(mean_square + EPSILON) * gain


def rotate(values, offsets):
    half_width = values.shape[-1] // 2
    frequency = 10000.0 ** (-jnp.arange(half_width, dtype=jnp.float32) / half_width)
    angles = offsets.astype(jnp.float32)[:, None] * frequency[None, :]
    cosine = jnp.cos(angles)[:, None, :]
    sine_part = jnp.sin(angles)[:, None, :]
    front_half = values[..., :half_width]
    back_half = values[..., half_width:]
    return jnp.concatenate(
        [front_half * cosine - back_half * sine_part, front_half * sine_part + back_half * cosine],
        axis=-1,
    )


def prompt_layout(lengths, token_count):
    prompt_ends = jnp.cumsum(lengths)
    prompt_starts = prompt_ends - lengths
    positions = jnp.arange(token_count, dtype=jnp.int32)
    segment = jnp.sum((positions[:, None] >= prompt_ends[None, :]).astype(jnp.int32), axis=1)
    member = segment[:, None] == jnp.arange(lengths.shape[0], dtype=jnp.int32)[None, :]
    offsets = positions - jnp.sum(jnp.where(member, prompt_starts[None, :], 0), axis=1)
    return (segment, offsets)


def project_rows(row_piece, weight):
    return jnp.dot(row_piece, weight, preferred_element_type=jnp.float32)


def gated_units(row_piece, weight):
    gate_up = jnp.dot(row_piece, weight, preferred_element_type=jnp.float32)
    half_width = weight.shape[1] // 2
    return (jax.nn.silu(gate_up[:, :half_width]) * gate_up[:, half_width:]).astype(jnp.bfloat16)


def project_out(source, weight):
    return lax.dot_general(
        source, weight, (((1,), (1,)), ((), ())), preferred_element_type=jnp.float32
    )


def gather_tp(values, tp_count):
    stacked = jnp.broadcast_to(values[None], (tp_count,) + values.shape)
    gathered = lax.all_to_all(stacked, "tp", 0, 0, tiled=True)
    return gathered.reshape((tp_count * values.shape[0],) + values.shape[1:])


def reduce_tp(products, tp_count):
    pieces = products.reshape((tp_count, products.shape[0] // tp_count) + products.shape[1:])
    received = lax.all_to_all(pieces, "tp", 0, 0, tiled=True)
    return jnp.sum(received.astype(jnp.float32), axis=0)


def project_owned(mixed_heads, out_weight, tp_count):
    own_rows = mixed_heads.shape[0] // tp_count
    pieces = mixed_heads.reshape(tp_count, own_rows, mixed_heads.shape[1])
    received = lax.all_to_all(pieces, "tp", 0, 0, tiled=True)
    group_weight = out_weight.reshape(out_weight.shape[0], tp_count, mixed_heads.shape[1])
    products = jnp.einsum(
        "gtc,rgc->gtr", received, group_weight, preferred_element_type=jnp.float32
    ).astype(jnp.bfloat16)
    return jnp.sum(products.astype(jnp.float32), axis=0)


def on_device(
    trainer_rows, shard_order, residual_in, norm_gains, prompt_lengths, variate_ids, variate_bias
):
    tp_count = lax.axis_size("tp")
    seq_count = lax.axis_size(SEQ_AXES)
    layer_count, block_rows, total_cols = trainer_rows.shape
    model_width = residual_in.shape[1]
    ff_width = (total_cols - 4 * model_width) // 3
    head_cols = model_width // tp_count
    unit_cols = ff_width // tp_count
    block_count = seq_count * tp_count
    part_widths = [model_width] * 4 + [ff_width] * 3

    rounded = trainer_rows.astype(jnp.bfloat16)
    grouped_parts = []
    column_start = 0
    for part_index, part_width in enumerate(part_widths):
        part = rounded[:, :, column_start : column_start + part_width]
        if part_index == 3:
            part = jnp.broadcast_to(part[:, :, None, :], (layer_count, block_rows, tp_count, part_width))
        else:
            part = part.reshape(layer_count, block_rows, tp_count, part_width // tp_count)
        grouped_parts.append(part)
        column_start = column_start + part_width
    grouped = jnp.concatenate(grouped_parts, axis=3)
    regrouped = lax.all_to_all(grouped, "tp", split_axis=2, concat_axis=1, tiled=True)
    chip_count = lax.axis_size(CHIP_AXES)
    core = lax.axis_index("core")
    core_swap = [(0, 1), (1, 0)]

    def join_cores(half):
        other = lax.ppermute(half, "core", core_swap)
        return jnp.concatenate([half, other], axis=0)

    def gather_seq(piece):
        return lax.all_gather(piece, SEQ_AXES, axis=0, tiled=True)

    def gather_chips(piece):
        stacked = jnp.broadcast_to(piece[None], (chip_count,) + piece.shape)
        half = lax.all_to_all(stacked, CHIP_AXES, 0, 0, tiled=True).reshape(
            chip_count * piece.shape[0], piece.shape[1]
        )
        return join_cores(half)

    block_index = jnp.arange(block_count, dtype=jnp.int32)
    half_blocks = block_count // 2
    core_of_block = jnp.where(block_index < half_blocks, core, 1 - core)
    within = block_index % half_blocks
    shard_of_block = ((within // tp_count) * 2 + core_of_block) * tp_count + within % tp_count

    def reorder(values, order):
        blocks = values.reshape(values.shape[:-1] + (block_count, block_rows))
        return jnp.take(blocks, order, axis=-2).reshape(values.shape)

    inverse_order = jnp.zeros_like(shard_order).at[shard_order].set(block_index)

    gains = [reorder(norm_gains[i], shard_order) for i in range(layer_count)]
    token_count = variate_ids.shape[0]
    segment, offsets = prompt_layout(prompt_lengths[0], token_count)
    same_prompt = segment[:, None] == segment[None, :]
    same_variate = variate_ids[:, None] == variate_ids[None, :]
    head_count = variate_bias.shape[1]
    local_heads = head_count // tp_count
    head_size = head_cols // local_heads
    bias_table = lax.dynamic_slice_in_dim(
        variate_bias, lax.axis_index("tp") * local_heads, local_heads, 1
    )
    residual = reorder(residual_in, shard_order)
    for layer_index in range(layer_count):
        layer_bias = bias_table[layer_index]
        pair_bias = jnp.where(
            same_variate[None], layer_bias[:, 1][:, None, None], layer_bias[:, 0][:, None, None]
        )
        normed = rms_scaled(residual, gains[layer_index][0]).astype(jnp.bfloat16)
        piece = regrouped[layer_index, :, 0, :]
        if layer_index == 0:
            qkv_weight = gather_chips(piece[:, : 3 * head_cols])
            normed = reorder(normed, shard_of_block)
            layer_weights = gather_seq(piece[:, 3 * head_cols :])
        else:
            layer_weights = gather_seq(piece)
            qkv_weight = layer_weights[:, : 3 * head_cols]
            layer_weights = layer_weights[:, 3 * head_cols :]
        out_weight = layer_weights[:, :model_width]
        gate_up_weight = layer_weights[:, model_width : model_width + 2 * unit_cols]
        down_weight = layer_weights[:, model_width + 2 * unit_cols :]
        projected = project_rows(gather_tp(normed, tp_count), weight=qkv_weight)
        queries = rotate(
            projected[:, :head_cols].reshape(token_count, local_heads, head_size), offsets
        ).astype(jnp.bfloat16)
        key_rows = rotate(
            projected[:, head_cols : 2 * head_cols].reshape(token_count, local_heads, head_size),
            offsets,
        ).astype(jnp.bfloat16)
        values = (
            projected[:, 2 * head_cols : 3 * head_cols]
            .reshape(token_count, local_heads, head_size)
            .astype(jnp.bfloat16)
        )
        scores = (
            jnp.einsum("qhd,khd->hqk", queries, key_rows, preferred_element_type=jnp.float32)
            * head_size ** (-0.5)
            + pair_bias
        )
        scores = jnp.where(same_prompt[None], scores, NEGATIVE)
        row_peak = jnp.max(scores, axis=2, keepdims=True)
        weights_exp = jnp.exp(scores - row_peak)
        row_sum = jnp.sum(weights_exp, axis=2)
        mixed_heads = (
            (
                jnp.einsum(
                    "hqk,khd->qhd",
                    weights_exp.astype(jnp.bfloat16),
                    values,
                    preferred_element_type=jnp.float32,
                )
                / row_sum.T[:, :, None]
            )
            .astype(jnp.bfloat16)
            .reshape(token_count, head_cols)
        )
        head_total = project_owned(mixed_heads, out_weight, tp_count)
        residual = residual + head_total
        normed_mlp = rms_scaled(residual, gains[layer_index][1]).astype(jnp.bfloat16)
        hidden = gated_units(gather_tp(normed_mlp, tp_count), weight=gate_up_weight)
        unit_total = reduce_tp(
            project_out(source=hidden, weight=down_weight).astype(jnp.bfloat16), tp_count
        )
        residual = residual + unit_total
    return reorder(residual, inverse_order)


def solution(mesh):
    seq_size = mesh.shape["seq"]
    chip_mesh = Mesh(
        mesh.devices.reshape((seq_size // 2, 2) + mesh.devices.shape[1:]),
        ("chip", "core", "tp"),
    )
    rows = SEQ_AXES + ("tp",)
    return jax.shard_map(
        on_device,
        mesh=chip_mesh,
        in_specs=(
            P(None, rows, None),
            P(),
            P(rows, None),
            P(),
            P(SEQ_AXES, None),
            P(SEQ_AXES),
            P(),
        ),
        out_specs=P(rows, None),
        check_vma=False,
    )
```

```python
import jax
import jax.numpy as jnp
from jax import lax
from jax.sharding import Mesh
from jax.sharding import PartitionSpec as P

NEGATIVE = -1e30
EPSILON = 1e-05
CHIP_AXES = "chip"
SEQ_AXES = ("chip", "core")


def rms_scaled(values, gain):
    mean_square = jnp.mean(values * values, axis=-1, keepdims=True)
    return values * lax.rsqrt(mean_square + EPSILON) * gain


def rotate(values, offsets):
    half_width = values.shape[-1] // 2
    frequency = 10000.0 ** (-jnp.arange(half_width, dtype=jnp.float32) / half_width)
    angles = offsets.astype(jnp.float32)[:, None] * frequency[None, :]
    cosine = jnp.cos(angles)[:, None, :]
    sine_part = jnp.sin(angles)[:, None, :]
    front_half = values[..., :half_width]
    back_half = values[..., half_width:]
    return jnp.concatenate(
        [front_half * cosine - back_half * sine_part, front_half * sine_part + back_half * cosine],
        axis=-1,
    )


def prompt_layout(lengths, token_count):
    prompt_ends = jnp.cumsum(lengths)
    prompt_starts = prompt_ends - lengths
    positions = jnp.arange(token_count, dtype=jnp.int32)
    segment = jnp.sum((positions[:, None] >= prompt_ends[None, :]).astype(jnp.int32), axis=1)
    member = segment[:, None] == jnp.arange(lengths.shape[0], dtype=jnp.int32)[None, :]
    offsets = positions - jnp.sum(jnp.where(member, prompt_starts[None, :], 0), axis=1)
    return (segment, offsets)


def project_rows(row_piece, weight):
    return jnp.dot(row_piece, weight, preferred_element_type=jnp.float32)


def gated_units(row_piece, weight):
    gate_up = jnp.dot(row_piece, weight, preferred_element_type=jnp.float32)
    half_width = weight.shape[1] // 2
    return (jax.nn.silu(gate_up[:, :half_width]) * gate_up[:, half_width:]).astype(jnp.bfloat16)


def project_out(source, weight):
    return lax.dot_general(
        source, weight, (((1,), (1,)), ((), ())), preferred_element_type=jnp.float32
    )


def gather_normed(residual, gain, tp_count):
    stacked = jnp.broadcast_to(residual[None], (tp_count,) + residual.shape)
    normed = rms_scaled(stacked, gain).astype(jnp.bfloat16)
    gathered = lax.all_to_all(normed, "tp", 0, 0, tiled=True)
    return gathered.reshape((tp_count * residual.shape[0],) + residual.shape[1:])


def gather_tp(values, tp_count):
    stacked = jnp.broadcast_to(values[None], (tp_count,) + values.shape)
    gathered = lax.all_to_all(stacked, "tp", 0, 0, tiled=True)
    return gathered.reshape((tp_count * values.shape[0],) + values.shape[1:])


def reduce_tp(products, tp_count):
    pieces = products.reshape((tp_count, products.shape[0] // tp_count) + products.shape[1:])
    received = lax.all_to_all(pieces, "tp", 0, 0, tiled=True)
    return jnp.sum(received.astype(jnp.float32), axis=0)


def project_owned(mixed_heads, out_weight, tp_count):
    own_rows = mixed_heads.shape[0] // tp_count
    pieces = mixed_heads.reshape(tp_count, own_rows, mixed_heads.shape[1])
    received = lax.all_to_all(pieces, "tp", 0, 0, tiled=True)
    group_weight = out_weight.reshape(out_weight.shape[0], tp_count, mixed_heads.shape[1])
    products = jnp.einsum(
        "gtc,rgc->gtr", received, group_weight, preferred_element_type=jnp.float32
    ).astype(jnp.bfloat16)
    return jnp.sum(products.astype(jnp.float32), axis=0)


def on_device(
    trainer_rows, shard_order, residual_in, norm_gains, prompt_lengths, variate_ids, variate_bias
):
    tp_count = lax.axis_size("tp")
    seq_count = lax.axis_size(SEQ_AXES)
    layer_count, block_rows, total_cols = trainer_rows.shape
    model_width = residual_in.shape[1]
    ff_width = (total_cols - 4 * model_width) // 3
    head_cols = model_width // tp_count
    unit_cols = ff_width // tp_count
    block_count = seq_count * tp_count
    part_widths = [model_width] * 4 + [ff_width] * 3

    rounded = trainer_rows.astype(jnp.bfloat16)
    grouped_parts = []
    column_start = 0
    for part_index, part_width in enumerate(part_widths):
        part = rounded[:, :, column_start : column_start + part_width]
        if part_index == 3:
            part = jnp.broadcast_to(part[:, :, None, :], (layer_count, block_rows, tp_count, part_width))
        else:
            part = part.reshape(layer_count, block_rows, tp_count, part_width // tp_count)
        grouped_parts.append(part)
        column_start = column_start + part_width
    grouped = jnp.concatenate(grouped_parts, axis=3)
    regrouped = lax.all_to_all(grouped, "tp", split_axis=2, concat_axis=1, tiled=True)
    chip_count = lax.axis_size(CHIP_AXES)
    core = lax.axis_index("core")
    core_swap = [(0, 1), (1, 0)]

    def join_cores(half):
        other = lax.ppermute(half, "core", core_swap)
        return jnp.concatenate([half, other], axis=0)

    def gather_seq(piece):
        return lax.all_gather(piece, SEQ_AXES, axis=0, tiled=True)

    def gather_chips(piece):
        stacked = jnp.broadcast_to(piece[None], (chip_count,) + piece.shape)
        half = lax.all_to_all(stacked, CHIP_AXES, 0, 0, tiled=True).reshape(
            chip_count * piece.shape[0], piece.shape[1]
        )
        return join_cores(half)

    block_index = jnp.arange(block_count, dtype=jnp.int32)
    half_blocks = block_count // 2
    core_of_block = jnp.where(block_index < half_blocks, core, 1 - core)
    within = block_index % half_blocks
    shard_of_block = ((within // tp_count) * 2 + core_of_block) * tp_count + within % tp_count

    def reorder(values, order):
        blocks = values.reshape(values.shape[:-1] + (block_count, block_rows))
        return jnp.take(blocks, order, axis=-2).reshape(values.shape)

    inverse_order = jnp.zeros_like(shard_order).at[shard_order].set(block_index)

    gains = [reorder(norm_gains[i], shard_order) for i in range(layer_count)]
    token_count = variate_ids.shape[0]
    segment, offsets = prompt_layout(prompt_lengths[0], token_count)
    same_prompt = segment[:, None] == segment[None, :]
    same_variate = variate_ids[:, None] == variate_ids[None, :]
    head_count = variate_bias.shape[1]
    local_heads = head_count // tp_count
    head_size = head_cols // local_heads
    bias_table = lax.dynamic_slice_in_dim(
        variate_bias, lax.axis_index("tp") * local_heads, local_heads, 1
    )
    residual = reorder(residual_in, shard_order)
    for layer_index in range(layer_count):
        layer_bias = bias_table[layer_index]
        pair_bias = jnp.where(
            same_variate[None], layer_bias[:, 1][:, None, None], layer_bias[:, 0][:, None, None]
        )
        normed = rms_scaled(residual, gains[layer_index][0]).astype(jnp.bfloat16)
        piece = regrouped[layer_index, :, 0, :]
        if layer_index == 0:
            qkv_weight = gather_chips(piece[:, : 3 * head_cols])
            normed = reorder(normed, shard_of_block)
            layer_weights = gather_seq(piece[:, 3 * head_cols :])
        else:
            layer_weights = gather_seq(piece)
            qkv_weight = layer_weights[:, : 3 * head_cols]
            layer_weights = layer_weights[:, 3 * head_cols :]
        out_weight = layer_weights[:, :model_width]
        gate_up_weight = layer_weights[:, model_width : model_width + 2 * unit_cols]
        down_weight = layer_weights[:, model_width + 2 * unit_cols :]
        projected = project_rows(gather_tp(normed, tp_count), weight=qkv_weight)
        queries = rotate(
            projected[:, :head_cols].reshape(token_count, local_heads, head_size), offsets
        ).astype(jnp.bfloat16)
        key_rows = rotate(
            projected[:, head_cols : 2 * head_cols].reshape(token_count, local_heads, head_size),
            offsets,
        ).astype(jnp.bfloat16)
        values = (
            projected[:, 2 * head_cols : 3 * head_cols]
            .reshape(token_count, local_heads, head_size)
            .astype(jnp.bfloat16)
        )
        scores = (
            jnp.einsum("qhd,khd->hqk", queries, key_rows, preferred_element_type=jnp.float32)
            * head_size ** (-0.5)
            + pair_bias
        )
        scores = jnp.where(same_prompt[None], scores, NEGATIVE)
        row_peak = jnp.max(scores, axis=2, keepdims=True)
        weights_exp = jnp.exp(scores - row_peak)
        attn_weights = (weights_exp / jnp.sum(weights_exp, axis=2, keepdims=True)).astype(
            jnp.bfloat16
        )
        mixed_heads = (
            jnp.einsum("hqk,khd->qhd", attn_weights, values, preferred_element_type=jnp.float32)
            .astype(jnp.bfloat16)
            .reshape(token_count, head_cols)
        )
        head_total = project_owned(mixed_heads, out_weight, tp_count)
        residual = residual + head_total
        hidden = gated_units(
            gather_normed(residual, gains[layer_index][1], tp_count), weight=gate_up_weight
        )
        unit_total = reduce_tp(
            project_out(source=hidden, weight=down_weight).astype(jnp.bfloat16), tp_count
        )
        residual = residual + unit_total
    return reorder(residual, inverse_order)


def solution(mesh):
    seq_size = mesh.shape["seq"]
    chip_mesh = Mesh(
        mesh.devices.reshape((seq_size // 2, 2) + mesh.devices.shape[1:]),
        ("chip", "core", "tp"),
    )
    rows = SEQ_AXES + ("tp",)
    return jax.shard_map(
        on_device,
        mesh=chip_mesh,
        in_specs=(
            P(None, rows, None),
            P(),
            P(rows, None),
            P(),
            P(SEQ_AXES, None),
            P(SEQ_AXES),
            P(),
        ),
        out_specs=P(rows, None),
        check_vma=False,
    )
```

```python
import jax
import jax.numpy as jnp
from jax import lax
from jax.sharding import Mesh
from jax.sharding import PartitionSpec as P

NEGATIVE = -1e30
EPSILON = 1e-05
CHIP_AXES = "chip"
SEQ_AXES = ("chip", "core")


def rms_scaled(values, gain):
    mean_square = jnp.mean(values * values, axis=-1, keepdims=True)
    return values * lax.rsqrt(mean_square + EPSILON) * gain


def rotate(values, offsets):
    half_width = values.shape[-1] // 2
    frequency = 10000.0 ** (-jnp.arange(half_width, dtype=jnp.float32) / half_width)
    angles = offsets.astype(jnp.float32)[:, None] * frequency[None, :]
    cosine = jnp.cos(angles)[:, None, :]
    sine_part = jnp.sin(angles)[:, None, :]
    front_half = values[..., :half_width]
    back_half = values[..., half_width:]
    return jnp.concatenate(
        [front_half * cosine - back_half * sine_part, front_half * sine_part + back_half * cosine],
        axis=-1,
    )


def prompt_layout(lengths, token_count):
    prompt_ends = jnp.cumsum(lengths)
    prompt_starts = prompt_ends - lengths
    positions = jnp.arange(token_count, dtype=jnp.int32)
    segment = jnp.sum((positions[:, None] >= prompt_ends[None, :]).astype(jnp.int32), axis=1)
    member = segment[:, None] == jnp.arange(lengths.shape[0], dtype=jnp.int32)[None, :]
    offsets = positions - jnp.sum(jnp.where(member, prompt_starts[None, :], 0), axis=1)
    return (segment, offsets)


def project_rows(row_piece, weight):
    return jnp.dot(row_piece, weight, preferred_element_type=jnp.float32)


def gated_units(row_piece, weight):
    gate_up = jnp.dot(row_piece, weight, preferred_element_type=jnp.float32)
    half_width = weight.shape[1] // 2
    return (jax.nn.silu(gate_up[:, :half_width]) * gate_up[:, half_width:]).astype(jnp.bfloat16)


def project_out(source, weight):
    return lax.dot_general(
        source, weight, (((1,), (1,)), ((), ())), preferred_element_type=jnp.float32
    )


def gather_normed(residual, gain, tp_count):
    stacked = jnp.broadcast_to(residual[None], (tp_count,) + residual.shape)
    normed = rms_scaled(stacked, gain).astype(jnp.bfloat16)
    gathered = lax.all_to_all(normed, "tp", 0, 0, tiled=True)
    return gathered.reshape((tp_count * residual.shape[0],) + residual.shape[1:])


def gather_tp(values, tp_count):
    stacked = jnp.broadcast_to(values[None], (tp_count,) + values.shape)
    gathered = lax.all_to_all(stacked, "tp", 0, 0, tiled=True)
    return gathered.reshape((tp_count * values.shape[0],) + values.shape[1:])


def reduce_tp(products, tp_count):
    pieces = products.reshape((tp_count, products.shape[0] // tp_count) + products.shape[1:])
    received = lax.all_to_all(pieces, "tp", 0, 0, tiled=True)
    return jnp.sum(received.astype(jnp.float32), axis=0)


def project_owned(mixed_heads, out_weight, tp_count):
    own_rows = mixed_heads.shape[0] // tp_count
    pieces = mixed_heads.reshape(tp_count, own_rows, mixed_heads.shape[1])
    received = lax.all_to_all(pieces, "tp", 0, 0, tiled=True)
    group_weight = out_weight.reshape(out_weight.shape[0], tp_count, mixed_heads.shape[1])
    products = jnp.einsum(
        "gtc,rgc->gtr", received, group_weight, preferred_element_type=jnp.float32
    ).astype(jnp.bfloat16)
    return jnp.sum(products.astype(jnp.float32), axis=0)


def on_device(
    trainer_rows, shard_order, residual_in, norm_gains, prompt_lengths, variate_ids, variate_bias
):
    tp_count = lax.axis_size("tp")
    seq_count = lax.axis_size(SEQ_AXES)
    layer_count, block_rows, total_cols = trainer_rows.shape
    model_width = residual_in.shape[1]
    ff_width = (total_cols - 4 * model_width) // 3
    head_cols = model_width // tp_count
    unit_cols = ff_width // tp_count
    block_count = seq_count * tp_count
    part_widths = [model_width] * 4 + [ff_width] * 3

    rounded = trainer_rows.astype(jnp.bfloat16)
    grouped_parts = []
    column_start = 0
    for part_index, part_width in enumerate(part_widths):
        part = rounded[:, :, column_start : column_start + part_width]
        if part_index == 3:
            part = jnp.broadcast_to(part[:, :, None, :], (layer_count, block_rows, tp_count, part_width))
        else:
            part = part.reshape(layer_count, block_rows, tp_count, part_width // tp_count)
        grouped_parts.append(part)
        column_start = column_start + part_width
    grouped = jnp.concatenate(grouped_parts, axis=3)
    regrouped = lax.all_to_all(grouped, "tp", split_axis=2, concat_axis=1, tiled=True)
    chip_count = lax.axis_size(CHIP_AXES)
    core = lax.axis_index("core")
    core_swap = [(0, 1), (1, 0)]

    def join_cores(half):
        other = lax.ppermute(half, "core", core_swap)
        return jnp.concatenate([half, other], axis=0)

    def gather_seq(piece):
        return lax.all_gather(piece, SEQ_AXES, axis=0, tiled=True)

    def gather_chips(piece):
        stacked = jnp.broadcast_to(piece[None], (chip_count,) + piece.shape)
        half = lax.all_to_all(stacked, CHIP_AXES, 0, 0, tiled=True).reshape(
            chip_count * piece.shape[0], piece.shape[1]
        )
        return join_cores(half)

    block_index = jnp.arange(block_count, dtype=jnp.int32)
    half_blocks = block_count // 2
    core_of_block = jnp.where(block_index < half_blocks, core, 1 - core)
    within = block_index % half_blocks
    shard_of_block = ((within // tp_count) * 2 + core_of_block) * tp_count + within % tp_count

    def reorder(values, order):
        blocks = values.reshape(values.shape[:-1] + (block_count, block_rows))
        return jnp.take(blocks, order, axis=-2).reshape(values.shape)

    inverse_order = jnp.zeros_like(shard_order).at[shard_order].set(block_index)

    gains = [reorder(norm_gains[i], shard_order) for i in range(layer_count)]
    token_count = variate_ids.shape[0]
    segment, offsets = prompt_layout(prompt_lengths[0], token_count)
    same_prompt = segment[:, None] == segment[None, :]
    same_variate = variate_ids[:, None] == variate_ids[None, :]
    head_count = variate_bias.shape[1]
    local_heads = head_count // tp_count
    head_size = head_cols // local_heads
    bias_table = lax.dynamic_slice_in_dim(
        variate_bias, lax.axis_index("tp") * local_heads, local_heads, 1
    )
    residual = reorder(residual_in, shard_order)
    for layer_index in range(layer_count):
        layer_bias = bias_table[layer_index]
        pair_bias = jnp.where(
            same_variate[None], layer_bias[:, 1][:, None, None], layer_bias[:, 0][:, None, None]
        )
        piece = regrouped[layer_index, :, 0, :]
        if layer_index == 0:
            qkv_weight = gather_chips(piece[:, : 3 * head_cols])
            qkv_tokens = gather_normed(
                reorder(residual, shard_of_block),
                reorder(gains[layer_index][0], shard_of_block),
                tp_count,
            )
            layer_weights = gather_seq(piece[:, 3 * head_cols :])
        else:
            qkv_tokens = gather_normed(residual, gains[layer_index][0], tp_count)
            layer_weights = gather_seq(piece)
            qkv_weight = layer_weights[:, : 3 * head_cols]
            layer_weights = layer_weights[:, 3 * head_cols :]
        out_weight = layer_weights[:, :model_width]
        gate_up_weight = layer_weights[:, model_width : model_width + 2 * unit_cols]
        down_weight = layer_weights[:, model_width + 2 * unit_cols :]
        projected = project_rows(qkv_tokens, weight=qkv_weight)
        queries = rotate(
            projected[:, :head_cols].reshape(token_count, local_heads, head_size), offsets
        ).astype(jnp.bfloat16)
        key_rows = rotate(
            projected[:, head_cols : 2 * head_cols].reshape(token_count, local_heads, head_size),
            offsets,
        ).astype(jnp.bfloat16)
        values = (
            projected[:, 2 * head_cols : 3 * head_cols]
            .reshape(token_count, local_heads, head_size)
            .astype(jnp.bfloat16)
        )
        scores = (
            jnp.einsum("qhd,khd->hqk", queries, key_rows, preferred_element_type=jnp.float32)
            * head_size ** (-0.5)
            + pair_bias
        )
        scores = jnp.where(same_prompt[None], scores, NEGATIVE)
        row_peak = jnp.max(scores, axis=2, keepdims=True)
        weights_exp = jnp.exp(scores - row_peak)
        attn_weights = (weights_exp / jnp.sum(weights_exp, axis=2, keepdims=True)).astype(
            jnp.bfloat16
        )
        mixed_heads = (
            jnp.einsum("hqk,khd->qhd", attn_weights, values, preferred_element_type=jnp.float32)
            .astype(jnp.bfloat16)
            .reshape(token_count, head_cols)
        )
        head_total = project_owned(mixed_heads, out_weight, tp_count)
        residual = residual + head_total
        hidden = gated_units(
            gather_normed(residual, gains[layer_index][1], tp_count), weight=gate_up_weight
        )
        unit_total = reduce_tp(
            project_out(source=hidden, weight=down_weight).astype(jnp.bfloat16), tp_count
        )
        residual = residual + unit_total
    return reorder(residual, inverse_order)


def solution(mesh):
    seq_size = mesh.shape["seq"]
    chip_mesh = Mesh(
        mesh.devices.reshape((seq_size // 2, 2) + mesh.devices.shape[1:]),
        ("chip", "core", "tp"),
    )
    rows = SEQ_AXES + ("tp",)
    return jax.shard_map(
        on_device,
        mesh=chip_mesh,
        in_specs=(
            P(None, rows, None),
            P(),
            P(rows, None),
            P(),
            P(SEQ_AXES, None),
            P(SEQ_AXES),
            P(),
        ),
        out_specs=P(rows, None),
        check_vma=False,
    )
```

```python
import jax
import jax.numpy as jnp
from jax import lax
from jax.sharding import Mesh
from jax.sharding import PartitionSpec as P

NEGATIVE = -1e30
EPSILON = 1e-05
CHIP_AXES = "chip"
SEQ_AXES = ("chip", "core")


def rms_scaled(values, gain):
    mean_square = jnp.mean(values * values, axis=-1, keepdims=True)
    return values * lax.rsqrt(mean_square + EPSILON) * gain


def rotate(values, offsets):
    half_width = values.shape[-1] // 2
    frequency = 10000.0 ** (-jnp.arange(half_width, dtype=jnp.float32) / half_width)
    angles = offsets.astype(jnp.float32)[:, None] * frequency[None, :]
    cosine = jnp.cos(angles)[:, None, :]
    sine_part = jnp.sin(angles)[:, None, :]
    front_half = values[..., :half_width]
    back_half = values[..., half_width:]
    return jnp.concatenate(
        [front_half * cosine - back_half * sine_part, front_half * sine_part + back_half * cosine],
        axis=-1,
    )


def prompt_layout(lengths, token_count):
    prompt_ends = jnp.cumsum(lengths)
    prompt_starts = prompt_ends - lengths
    positions = jnp.arange(token_count, dtype=jnp.int32)
    segment = jnp.sum((positions[:, None] >= prompt_ends[None, :]).astype(jnp.int32), axis=1)
    member = segment[:, None] == jnp.arange(lengths.shape[0], dtype=jnp.int32)[None, :]
    offsets = positions - jnp.sum(jnp.where(member, prompt_starts[None, :], 0), axis=1)
    return (segment, offsets)


def project_rows(row_piece, weight):
    return jnp.dot(row_piece, weight, preferred_element_type=jnp.float32)


def gated_units(row_piece, weight):
    gate_up = jnp.dot(row_piece, weight, preferred_element_type=jnp.float32)
    half_width = weight.shape[1] // 2
    return (jax.nn.silu(gate_up[:, :half_width]) * gate_up[:, half_width:]).astype(jnp.bfloat16)


def project_out(source, weight):
    return lax.dot_general(
        source, weight, (((1,), (1,)), ((), ())), preferred_element_type=jnp.float32
    )


def gather_normed(residual, gain, tp_count):
    stacked = jnp.broadcast_to(residual[None], (tp_count,) + residual.shape)
    normed = rms_scaled(stacked, gain).astype(jnp.bfloat16)
    gathered = lax.all_to_all(normed, "tp", 0, 0, tiled=True)
    return gathered.reshape((tp_count * residual.shape[0],) + residual.shape[1:])


def gather_tp(values, tp_count):
    stacked = jnp.broadcast_to(values[None], (tp_count,) + values.shape)
    gathered = lax.all_to_all(stacked, "tp", 0, 0, tiled=True)
    return gathered.reshape((tp_count * values.shape[0],) + values.shape[1:])


def reduce_tp(products, tp_count):
    pieces = products.reshape((tp_count, products.shape[0] // tp_count) + products.shape[1:])
    received = lax.all_to_all(pieces, "tp", 0, 0, tiled=True)
    return jnp.sum(received.astype(jnp.float32), axis=0)


def project_owned(mixed_heads, out_weight, tp_count):
    own_rows = mixed_heads.shape[0] // tp_count
    pieces = mixed_heads.reshape(tp_count, own_rows, mixed_heads.shape[1])
    received = lax.all_to_all(pieces, "tp", 0, 0, tiled=True)
    group_weight = out_weight.reshape(out_weight.shape[0], tp_count, mixed_heads.shape[1])
    products = jnp.einsum(
        "gtc,rgc->gtr", received, group_weight, preferred_element_type=jnp.float32
    ).astype(jnp.bfloat16)
    return jnp.sum(products.astype(jnp.float32), axis=0)


def on_device(
    trainer_rows, shard_order, residual_in, norm_gains, prompt_lengths, variate_ids, variate_bias
):
    tp_count = lax.axis_size("tp")
    seq_count = lax.axis_size(SEQ_AXES)
    layer_count, block_rows, total_cols = trainer_rows.shape
    model_width = residual_in.shape[1]
    ff_width = (total_cols - 4 * model_width) // 3
    head_cols = model_width // tp_count
    unit_cols = ff_width // tp_count
    block_count = seq_count * tp_count
    part_widths = [model_width] * 4 + [ff_width] * 3

    rounded = trainer_rows.astype(jnp.bfloat16)
    grouped_parts = []
    column_start = 0
    for part_index, part_width in enumerate(part_widths):
        part = rounded[:, :, column_start : column_start + part_width]
        if part_index == 3:
            part = jnp.broadcast_to(part[:, :, None, :], (layer_count, block_rows, tp_count, part_width))
        else:
            part = part.reshape(layer_count, block_rows, tp_count, part_width // tp_count)
        grouped_parts.append(part)
        column_start = column_start + part_width
    grouped = jnp.concatenate(grouped_parts, axis=3)
    regrouped = lax.all_to_all(grouped, "tp", split_axis=2, concat_axis=1, tiled=True)
    chip_count = lax.axis_size(CHIP_AXES)
    core = lax.axis_index("core")
    core_swap = [(0, 1), (1, 0)]

    def join_cores(half):
        other = lax.ppermute(half, "core", core_swap)
        return jnp.concatenate([half, other], axis=0)

    def gather_seq(piece):
        return lax.all_gather(piece, SEQ_AXES, axis=0, tiled=True)

    def gather_chips(piece):
        stacked = jnp.broadcast_to(piece[None], (chip_count,) + piece.shape)
        half = lax.all_to_all(stacked, CHIP_AXES, 0, 0, tiled=True).reshape(
            chip_count * piece.shape[0], piece.shape[1]
        )
        return join_cores(half)

    block_index = jnp.arange(block_count, dtype=jnp.int32)
    half_blocks = block_count // 2
    core_of_block = jnp.where(block_index < half_blocks, core, 1 - core)
    within = block_index % half_blocks
    shard_of_block = ((within // tp_count) * 2 + core_of_block) * tp_count + within % tp_count

    def reorder(values, order):
        blocks = values.reshape(values.shape[:-1] + (block_count, block_rows))
        return jnp.take(blocks, order, axis=-2).reshape(values.shape)

    inverse_order = jnp.zeros_like(shard_order).at[shard_order].set(block_index)

    gains = reorder(norm_gains, shard_order)
    token_count = variate_ids.shape[0]
    segment, offsets = prompt_layout(prompt_lengths[0], token_count)
    same_prompt = segment[:, None] == segment[None, :]
    same_variate = variate_ids[:, None] == variate_ids[None, :]
    head_count = variate_bias.shape[1]
    local_heads = head_count // tp_count
    head_size = head_cols // local_heads
    bias_table = lax.dynamic_slice_in_dim(
        variate_bias, lax.axis_index("tp") * local_heads, local_heads, 1
    )
    residual = reorder(residual_in, shard_order)
    for layer_index in range(layer_count):
        layer_bias = bias_table[layer_index]
        pair_bias = jnp.where(
            same_variate[None], layer_bias[:, 1][:, None, None], layer_bias[:, 0][:, None, None]
        )
        piece = regrouped[layer_index, :, 0, :]
        if layer_index == 0:
            qkv_weight = gather_chips(piece[:, : 3 * head_cols])
            qkv_tokens = gather_normed(
                reorder(residual, shard_of_block),
                reorder(gains[layer_index, 0], shard_of_block),
                tp_count,
            )
            layer_weights = gather_seq(piece[:, 3 * head_cols :])
        else:
            qkv_tokens = gather_normed(residual, gains[layer_index, 0], tp_count)
            layer_weights = gather_seq(piece)
            qkv_weight = layer_weights[:, : 3 * head_cols]
            layer_weights = layer_weights[:, 3 * head_cols :]
        out_weight = layer_weights[:, :model_width]
        gate_up_weight = layer_weights[:, model_width : model_width + 2 * unit_cols]
        down_weight = layer_weights[:, model_width + 2 * unit_cols :]
        projected = project_rows(qkv_tokens, weight=qkv_weight)
        queries = rotate(
            projected[:, :head_cols].reshape(token_count, local_heads, head_size), offsets
        ).astype(jnp.bfloat16)
        key_rows = rotate(
            projected[:, head_cols : 2 * head_cols].reshape(token_count, local_heads, head_size),
            offsets,
        ).astype(jnp.bfloat16)
        values = (
            projected[:, 2 * head_cols : 3 * head_cols]
            .reshape(token_count, local_heads, head_size)
            .astype(jnp.bfloat16)
        )
        scores = (
            jnp.einsum("qhd,khd->hqk", queries, key_rows, preferred_element_type=jnp.float32)
            * head_size ** (-0.5)
            + pair_bias
        )
        scores = jnp.where(same_prompt[None], scores, NEGATIVE)
        row_peak = jnp.max(scores, axis=2, keepdims=True)
        weights_exp = jnp.exp(scores - row_peak)
        attn_weights = (weights_exp / jnp.sum(weights_exp, axis=2, keepdims=True)).astype(
            jnp.bfloat16
        )
        mixed_heads = (
            jnp.einsum("hqk,khd->qhd", attn_weights, values, preferred_element_type=jnp.float32)
            .astype(jnp.bfloat16)
            .reshape(token_count, head_cols)
        )
        head_total = project_owned(mixed_heads, out_weight, tp_count)
        residual = residual + head_total
        hidden = gated_units(
            gather_normed(residual, gains[layer_index, 1], tp_count), weight=gate_up_weight
        )
        unit_total = reduce_tp(
            project_out(source=hidden, weight=down_weight).astype(jnp.bfloat16), tp_count
        )
        residual = residual + unit_total
    return reorder(residual, inverse_order)


def solution(mesh):
    seq_size = mesh.shape["seq"]
    chip_mesh = Mesh(
        mesh.devices.reshape((seq_size // 2, 2) + mesh.devices.shape[1:]),
        ("chip", "core", "tp"),
    )
    rows = SEQ_AXES + ("tp",)
    return jax.shard_map(
        on_device,
        mesh=chip_mesh,
        in_specs=(
            P(None, rows, None),
            P(),
            P(rows, None),
            P(),
            P(SEQ_AXES, None),
            P(SEQ_AXES),
            P(),
        ),
        out_specs=P(rows, None),
        check_vma=False,
    )
```

```python
import jax
import jax.numpy as jnp
from jax import lax
from jax.sharding import Mesh
from jax.sharding import PartitionSpec as P

NEGATIVE = -1e30
EPSILON = 1e-05
CHIP_AXES = "chip"
SEQ_AXES = ("chip", "core")


def rms_scaled(values, gain):
    mean_square = jnp.mean(values * values, axis=-1, keepdims=True)
    return values * lax.rsqrt(mean_square + EPSILON) * gain


def rotate(values, offsets):
    half_width = values.shape[-1] // 2
    frequency = 10000.0 ** (-jnp.arange(half_width, dtype=jnp.float32) / half_width)
    angles = offsets.astype(jnp.float32)[:, None] * frequency[None, :]
    cosine = jnp.cos(angles)[:, None, :]
    sine_part = jnp.sin(angles)[:, None, :]
    front_half = values[..., :half_width]
    back_half = values[..., half_width:]
    return jnp.concatenate(
        [front_half * cosine - back_half * sine_part, front_half * sine_part + back_half * cosine],
        axis=-1,
    )


def prompt_layout(lengths, token_count):
    prompt_ends = jnp.cumsum(lengths)
    prompt_starts = prompt_ends - lengths
    positions = jnp.arange(token_count, dtype=jnp.int32)
    segment = jnp.sum((positions[:, None] >= prompt_ends[None, :]).astype(jnp.int32), axis=1)
    member = segment[:, None] == jnp.arange(lengths.shape[0], dtype=jnp.int32)[None, :]
    offsets = positions - jnp.sum(jnp.where(member, prompt_starts[None, :], 0), axis=1)
    return (segment, offsets)


def project_rows(row_piece, weight):
    return jnp.dot(row_piece, weight, preferred_element_type=jnp.float32)


def gated_units(row_piece, weight):
    gate_up = jnp.dot(row_piece, weight, preferred_element_type=jnp.float32)
    half_width = weight.shape[1] // 2
    return (jax.nn.silu(gate_up[:, :half_width]) * gate_up[:, half_width:]).astype(jnp.bfloat16)


def project_out(source, weight):
    return lax.dot_general(
        source, weight, (((1,), (1,)), ((), ())), preferred_element_type=jnp.float32
    )


def gather_normed(residual, gain, tp_count):
    stacked = jnp.broadcast_to(residual[None], (tp_count,) + residual.shape)
    normed = rms_scaled(stacked, gain).astype(jnp.bfloat16)
    gathered = lax.all_to_all(normed, "tp", 0, 0, tiled=True)
    return gathered.reshape((tp_count * residual.shape[0],) + residual.shape[1:])


def gather_tp(values, tp_count):
    stacked = jnp.broadcast_to(values[None], (tp_count,) + values.shape)
    gathered = lax.all_to_all(stacked, "tp", 0, 0, tiled=True)
    return gathered.reshape((tp_count * values.shape[0],) + values.shape[1:])


def reduce_tp(products, tp_count):
    pieces = products.reshape((tp_count, products.shape[0] // tp_count) + products.shape[1:])
    received = lax.all_to_all(pieces, "tp", 0, 0, tiled=True)
    return jnp.sum(received.astype(jnp.float32), axis=0)


def project_owned(mixed_heads, out_weight, tp_count):
    own_rows = mixed_heads.shape[0] // tp_count
    pieces = mixed_heads.reshape(tp_count, own_rows, mixed_heads.shape[1])
    received = lax.all_to_all(pieces, "tp", 0, 0, tiled=True)
    group_weight = out_weight.reshape(out_weight.shape[0], tp_count, mixed_heads.shape[1])
    products = jnp.einsum(
        "gtc,rgc->gtr", received, group_weight, preferred_element_type=jnp.float32
    ).astype(jnp.bfloat16)
    return jnp.sum(products.astype(jnp.float32), axis=0)


def on_device(
    trainer_rows, shard_order, residual_in, norm_gains, prompt_lengths, variate_ids, variate_bias
):
    tp_count = lax.axis_size("tp")
    seq_count = lax.axis_size(SEQ_AXES)
    layer_count, block_rows, total_cols = trainer_rows.shape
    model_width = residual_in.shape[1]
    ff_width = (total_cols - 4 * model_width) // 3
    head_cols = model_width // tp_count
    unit_cols = ff_width // tp_count
    block_count = seq_count * tp_count
    part_widths = [model_width] * 4 + [ff_width] * 3

    rounded = trainer_rows.astype(jnp.bfloat16)
    grouped_parts = []
    column_start = 0
    for part_index, part_width in enumerate(part_widths):
        part = rounded[:, :, column_start : column_start + part_width]
        if part_index == 3:
            part = jnp.broadcast_to(part[:, :, None, :], (layer_count, block_rows, tp_count, part_width))
        else:
            part = part.reshape(layer_count, block_rows, tp_count, part_width // tp_count)
        grouped_parts.append(part)
        column_start = column_start + part_width
    grouped = jnp.concatenate(grouped_parts, axis=3)
    regrouped = lax.all_to_all(grouped, "tp", split_axis=2, concat_axis=1, tiled=True)
    chip_count = lax.axis_size(CHIP_AXES)
    core = lax.axis_index("core")
    core_swap = [(0, 1), (1, 0)]

    def join_cores(half):
        other = lax.ppermute(half, "core", core_swap)
        return jnp.concatenate([half, other], axis=0)

    def gather_seq(piece):
        return lax.all_gather(piece, SEQ_AXES, axis=0, tiled=True)

    def gather_chips(piece):
        stacked = jnp.broadcast_to(piece[None], (chip_count,) + piece.shape)
        half = lax.all_to_all(stacked, CHIP_AXES, 0, 0, tiled=True).reshape(
            chip_count * piece.shape[0], piece.shape[1]
        )
        return join_cores(half)

    block_index = jnp.arange(block_count, dtype=jnp.int32)
    half_blocks = block_count // 2
    core_of_block = jnp.where(block_index < half_blocks, core, 1 - core)
    within = block_index % half_blocks
    shard_of_block = ((within // tp_count) * 2 + core_of_block) * tp_count + within % tp_count

    def reorder(values, order):
        blocks = values.reshape(values.shape[:-1] + (block_count, block_rows))
        return jnp.take(blocks, order, axis=-2).reshape(values.shape)

    inverse_order = jnp.sum(
        jnp.where(shard_order[None, :] == block_index[:, None], block_index[None, :], 0), axis=1
    ).astype(shard_order.dtype)

    gains = reorder(norm_gains, shard_order)
    token_count = variate_ids.shape[0]
    segment, offsets = prompt_layout(prompt_lengths[0], token_count)
    same_prompt = segment[:, None] == segment[None, :]
    same_variate = variate_ids[:, None] == variate_ids[None, :]
    head_count = variate_bias.shape[1]
    local_heads = head_count // tp_count
    head_size = head_cols // local_heads
    bias_table = lax.dynamic_slice_in_dim(
        variate_bias, lax.axis_index("tp") * local_heads, local_heads, 1
    )
    residual = reorder(residual_in, shard_order)
    for layer_index in range(layer_count):
        layer_bias = bias_table[layer_index]
        pair_bias = jnp.where(
            same_variate[None], layer_bias[:, 1][:, None, None], layer_bias[:, 0][:, None, None]
        )
        piece = regrouped[layer_index, :, 0, :]
        if layer_index == 0:
            qkv_weight = gather_chips(piece[:, : 3 * head_cols])
            qkv_tokens = gather_normed(
                reorder(residual, shard_of_block),
                reorder(gains[layer_index, 0], shard_of_block),
                tp_count,
            )
            layer_weights = gather_seq(piece[:, 3 * head_cols :])
        else:
            qkv_tokens = gather_normed(residual, gains[layer_index, 0], tp_count)
            layer_weights = gather_seq(piece)
            qkv_weight = layer_weights[:, : 3 * head_cols]
            layer_weights = layer_weights[:, 3 * head_cols :]
        out_weight = layer_weights[:, :model_width]
        gate_up_weight = layer_weights[:, model_width : model_width + 2 * unit_cols]
        down_weight = layer_weights[:, model_width + 2 * unit_cols :]
        projected = project_rows(qkv_tokens, weight=qkv_weight)
        queries = rotate(
            projected[:, :head_cols].reshape(token_count, local_heads, head_size), offsets
        ).astype(jnp.bfloat16)
        key_rows = rotate(
            projected[:, head_cols : 2 * head_cols].reshape(token_count, local_heads, head_size),
            offsets,
        ).astype(jnp.bfloat16)
        values = (
            projected[:, 2 * head_cols : 3 * head_cols]
            .reshape(token_count, local_heads, head_size)
            .astype(jnp.bfloat16)
        )
        scores = (
            jnp.einsum("qhd,khd->hqk", queries, key_rows, preferred_element_type=jnp.float32)
            * head_size ** (-0.5)
            + pair_bias
        )
        scores = jnp.where(same_prompt[None], scores, NEGATIVE)
        row_peak = jnp.max(scores, axis=2, keepdims=True)
        weights_exp = jnp.exp(scores - row_peak)
        attn_weights = (weights_exp / jnp.sum(weights_exp, axis=2, keepdims=True)).astype(
            jnp.bfloat16
        )
        mixed_heads = (
            jnp.einsum("hqk,khd->qhd", attn_weights, values, preferred_element_type=jnp.float32)
            .astype(jnp.bfloat16)
            .reshape(token_count, head_cols)
        )
        head_total = project_owned(mixed_heads, out_weight, tp_count)
        residual = residual + head_total
        hidden = gated_units(
            gather_normed(residual, gains[layer_index, 1], tp_count), weight=gate_up_weight
        )
        unit_total = reduce_tp(
            project_out(source=hidden, weight=down_weight).astype(jnp.bfloat16), tp_count
        )
        residual = residual + unit_total
    return reorder(residual, inverse_order)


def solution(mesh):
    seq_size = mesh.shape["seq"]
    chip_mesh = Mesh(
        mesh.devices.reshape((seq_size // 2, 2) + mesh.devices.shape[1:]),
        ("chip", "core", "tp"),
    )
    rows = SEQ_AXES + ("tp",)
    return jax.shard_map(
        on_device,
        mesh=chip_mesh,
        in_specs=(
            P(None, rows, None),
            P(),
            P(rows, None),
            P(),
            P(SEQ_AXES, None),
            P(SEQ_AXES),
            P(),
        ),
        out_specs=P(rows, None),
        check_vma=False,
    )
```
